32 devices in a mesh: parts: 2 (over y), rows: 4 (over z), sub: 4 (over x, core), head: 1.
Axes of the slice: x: 2, y: 2, z: 4, core: 2. Of those that a mesh axis runs over, the one named last changes fastest.
Arguments:
- queries: bfloat16 [8192, 512], P(('parts', 'rows', 'sub'), 'head'), parts along dimension 0, may hold values from -6 to 6
- key_table: bfloat16 [8192, 512], P(('parts', 'rows', 'sub'), 'head'), parts along dimension 0, may hold values from -6 to 6
- value_table: bfloat16 [8192, 512], P(('parts', 'rows', 'sub'), 'head'), parts along dimension 0, may hold values from -4 to 4
- out_grad: bfloat16 [8192, 512], P(('parts', 'rows', 'sub'), 'head'), parts along dimension 0, may hold values from -6 to 6
- hilbert_order: int32 [32, 256], P(('parts', 'rows', 'sub')), parts along dimension 0, may hold values from 0 to 255, as said below
- key_valid: int32 [8192], P('parts'), parts along dimension 0, may hold values from 0 to 1, as said below
Outputs:
- attended: bfloat16 [8192, 512], P(('parts', 'rows', 'sub'), 'head'), parts along dimension 0
- query_grad: bfloat16 [8192, 512], P(('parts', 'rows', 'sub'), 'head'), parts along dimension 0
- key_grad: bfloat16 [8192, 512], P(('parts', 'rows', 'sub'), 'head'), parts along dimension 0
- value_grad: bfloat16 [8192, 512], P(('parts', 'rows', 'sub'), 'head'), parts along dimension 0
The draws below stay inside these ranges and needn't reach their ends.
There are 2 independent parts, one for each index of `parts`. The reference program is written for one: setup_inputs(seed, part) draws one part's arguments, and reference() takes and returns one part's arrays. A program takes and returns all parts, laid end to end along the dimension named above; each array names one. Nothing has to cross between parts.
Inputs may be any that keep to these rules, and one draw needn't show every extreme that they name: `hilbert_order`: each row lists every index from 0 to 255 once. `key_valid`: 1 where the position may serve as a key.
All inputs are finite; a program needn't handle non-finite values.
Results may differ from the reference program's by a relative error of at most 0.012.
Values may be sent and summed in bfloat16 or wider, within the bound.
No kernel may reach another device: no remote copies, remote signals or barrier semaphores. Data moves between devices by JAX's collectives and lax.ppermute only.
A program may use at most 64 MiB of HBM per device.

```python
import math
import jax
import jax.numpy as jnp
from jax import lax

D = 512
HEADS = 8
BLOCK = 128
ROWS_DEV = 256
ROWS = 4096


def shard_orders(seed_key):
    base = jax.random.fold_in(seed_key, 101)
    shard_keys = jax.random.split(base, ROWS // ROWS_DEV)
    return jax.vmap(lambda one_key: jax.random.permutation(one_key, ROWS_DEV))(shard_keys).astype(jnp.int32)


def drawn_rows(seed_key):
    base = jax.random.fold_in(seed_key, 202)
    picked = jax.random.randint(base, (ROWS,), 0, 40)
    position = jnp.arange(ROWS, dtype=jnp.int32)
    return (picked == 0) & (position % 2 == 0)


def smooth_wave(seed_key, amplitude):
    summed = jnp.zeros((ROWS, D), jnp.float32)
    location = (jnp.arange(ROWS, dtype=jnp.float32) / ROWS)[:, None]
    for wave_index in range(4):
        wave_keys = jax.random.split(jax.random.fold_in(seed_key, wave_index), 3)
        frequency = jax.random.uniform(wave_keys[0], (1, D), minval=0.5, maxval=6.0)
        phases = jax.random.uniform(wave_keys[1], (1, D), minval=0.0, maxval=2.0 * math.pi)
        heights = jax.random.uniform(wave_keys[2], (1, D), minval=-1.0, maxval=1.0)
        summed = summed + heights * jnp.sin(2.0 * math.pi * frequency * location + phases)
    return amplitude * summed / 2.0


def field_pair(seed_key):
    base = jax.random.fold_in(seed_key, 404)
    draw_keys = jax.random.split(base, 4)
    rough_query = jnp.clip(jax.random.normal(draw_keys[0], (ROWS, D)), -4.0, 4.0)
    rough_key = jnp.clip(jax.random.normal(draw_keys[1], (ROWS, D)), -4.0, 4.0)
    amplitude = 0.6
    query_field = 0.7 * rough_query + smooth_wave(draw_keys[2], amplitude)
    key_field = 0.7 * rough_key + smooth_wave(draw_keys[3], amplitude)
    return (query_field, key_field)


def draw_queries(key, part):
    return field_pair(key)[0].astype(jnp.bfloat16)


def draw_key_table(key, part):
    return field_pair(key)[1].astype(jnp.bfloat16)


def draw_value_table(key, part):
    base = jax.random.fold_in(key, 505)
    draw_keys = jax.random.split(base, 2)
    rough_part = jnp.clip(jax.random.normal(draw_keys[0], (ROWS, D)), -4.0, 4.0)
    amplitude = 0.8
    return (0.6 * rough_part + smooth_wave(draw_keys[1], amplitude)).astype(jnp.bfloat16)


def draw_hilbert_order(key, part):
    return shard_orders(key)


def draw_key_valid(key, part):
    coin_toss = jax.random.randint(jax.random.fold_in(key, 303), (ROWS,), 0, 8)
    chosen = drawn_rows(key)
    following = jnp.roll(chosen, 1)
    return ((coin_toss < 7) | chosen | following).astype(jnp.int32)


def steps_of(own_key, extent, cuts, least, high):
    def one(dim, parts):
        draws = jax.random.uniform(jax.random.fold_in(jax.random.fold_in(own_key, 6), dim), (parts,), jnp.float32, least / len(cuts), high / len(cuts))
        return jnp.repeat(jnp.exp(draws), extent[dim] // parts).reshape((-1,) + (1,) * (len(extent) - dim - 1))

    level = one(*cuts[0])
    for cut in cuts[1:]:
        level = level * one(*cut)
    return level


def scatter_about(stream_key, shape, width, limit, pieces=(), held_as=jnp.bfloat16):
    result = jax.random.normal(stream_key, shape, jnp.float32) * width
    if len(pieces) > 0:
        result = steps_of(stream_key, shape, pieces, -0.22, 0.18) * result
    return jnp.clip(result, min=-limit, max=limit).astype(held_as)


def setup_inputs(seed: int = 0, part: int = 0) -> dict:
    seeds = jax.random.split(jax.random.key(seed), 7)
    own_keys = jax.random.split(jax.random.fold_in(seeds[6], part), 7)
    return {
        "queries": draw_queries(jax.random.fold_in(jax.random.fold_in(seeds[6], part), 71), part),
        "key_table": draw_key_table(jax.random.fold_in(jax.random.fold_in(seeds[6], part), 71), part),
        "value_table": draw_value_table(jax.random.fold_in(jax.random.fold_in(seeds[6], part), 71), part),
        "out_grad": scatter_about(own_keys[3], (ROWS, D), 1.0, 6.0, ((0, 16),)),
        "hilbert_order": draw_hilbert_order(jax.random.fold_in(jax.random.fold_in(seeds[6], part), 71), part),
        "key_valid": draw_key_valid(jax.random.fold_in(jax.random.fold_in(seeds[6], part), 71), part),
    }


def pool_mean(rows_in, group_size):
    return lax.optimization_barrier(jnp.sum(rows_in.reshape(-1, group_size, rows_in.shape[-1]), axis=1)) / group_size

def add_rows(target, update, row_start):
    current = lax.dynamic_slice_in_dim(target, row_start, update.shape[0], 0)
    return lax.dynamic_update_slice_in_dim(target, current + update, row_start, 0)

def reference(queries, key_table, value_table, out_grad, hilbert_order, key_valid):
    block_rows = BLOCK
    head_dim = D // HEADS
    score_scale = 1.0 / math.sqrt(head_dim)
    shard_count = ROWS // ROWS_DEV
    block_count = ROWS // block_rows
    top_level = block_count.bit_length() - 1
    levels = list(range(2, top_level + 1))
    near_width = 3 * block_rows
    positions = (jnp.arange(shard_count, dtype=jnp.int32)[:, None] * ROWS_DEV + hilbert_order.astype(jnp.int32)).reshape(-1)
    query_rows = queries[positions]
    key_rows = key_table[positions]
    value_rows = value_table[positions]
    grad_rows = out_grad[positions]
    valid_rows = key_valid.astype(jnp.float32)
    masked_key = key_rows.astype(jnp.float32) * valid_rows[:, None]
    masked_value = value_rows.astype(jnp.float32) * valid_rows[:, None]
    pooled_key = [pool_mean(masked_key, 2 ** (level_num - 1)).astype(jnp.bfloat16) for level_num in levels]
    pooled_value = [pool_mean(masked_value, 2 ** (level_num - 1)).astype(jnp.bfloat16) for level_num in levels]
    key_pad = jnp.pad(key_rows, ((block_rows, block_rows), (0, 0)))
    value_pad = jnp.pad(value_rows, ((block_rows, block_rows), (0, 0)))
    valid_pad = jnp.pad(valid_rows, (block_rows, block_rows))

    def one_block(running, block_index):
        attended, query_grad, nearby_key_rows, nearby_value_rows, level_key, level_value = running
        row_start = block_index * block_rows
        probe_slice = lax.dynamic_slice_in_dim(query_rows, row_start, block_rows, 0).astype(jnp.float32).reshape(block_rows, HEADS, head_dim)
        derivative_slice = lax.dynamic_slice_in_dim(grad_rows, row_start, block_rows, 0).astype(jnp.float32).reshape(block_rows, HEADS, head_dim)
        key_list = [lax.dynamic_slice_in_dim(key_pad, row_start, near_width, 0)]
        value_list = [lax.dynamic_slice_in_dim(value_pad, row_start, near_width, 0)]
        sibling_starts = []
        for index_level, level_num in enumerate(levels):
            group_size = 2 ** (level_num - 1)
            sibling = jnp.bitwise_xor(block_index // group_size, 1) * block_rows
            sibling_starts.append(sibling)
            key_list.append(lax.dynamic_slice_in_dim(pooled_key[index_level], sibling, block_rows, 0))
            value_list.append(lax.dynamic_slice_in_dim(pooled_value[index_level], sibling, block_rows, 0))
        key_set = lax.optimization_barrier(jnp.concatenate(key_list, axis=0)).astype(jnp.float32).reshape(-1, HEADS, head_dim)
        value_set = lax.optimization_barrier(jnp.concatenate(value_list, axis=0)).astype(jnp.float32).reshape(-1, HEADS, head_dim)
        near_ok = lax.dynamic_slice_in_dim(valid_pad, row_start, near_width, 0) > 0.5
        column_ok = jnp.concatenate([near_ok, jnp.ones((len(levels) * block_rows,), dtype=bool)])
        scores = jnp.einsum('qhe,khe->hqk', probe_slice, key_set) * score_scale
        scores = jnp.where(column_ok[None, None, :], scores, -jnp.inf)
        largest = lax.optimization_barrier(jnp.max(scores, axis=-1, keepdims=True))
        exponent = jnp.exp(scores - largest)
        soft_weights = exponent / lax.optimization_barrier(jnp.sum(exponent, axis=-1, keepdims=True))
        rounded = lax.optimization_barrier(soft_weights.astype(jnp.bfloat16)).astype(jnp.float32)
        output = jnp.einsum('hqk,khe->qhe', rounded, value_set).reshape(block_rows, D).astype(jnp.bfloat16)
        value_dot = jnp.einsum('qhe,khe->hqk', derivative_slice, value_set)
        row_dot = lax.optimization_barrier(jnp.sum(soft_weights * value_dot, axis=-1, keepdims=True))
        score_grad = soft_weights * (value_dot - row_dot) * score_scale
        score_grad = lax.optimization_barrier(score_grad.astype(jnp.bfloat16)).astype(jnp.float32)
        query_term = jnp.einsum('hqk,khe->qhe', score_grad, key_set).reshape(block_rows, D).astype(jnp.bfloat16)
        key_term = jnp.einsum('hqk,qhe->khe', score_grad, probe_slice).reshape(-1, D)
        value_term = jnp.einsum('hqk,qhe->khe', rounded, derivative_slice).reshape(-1, D)
        attended = lax.dynamic_update_slice_in_dim(attended, output, row_start, 0)
        query_grad = lax.dynamic_update_slice_in_dim(query_grad, query_term, row_start, 0)
        nearby_key_rows = add_rows(nearby_key_rows, key_term[:near_width], row_start)
        nearby_value_rows = add_rows(nearby_value_rows, value_term[:near_width], row_start)
        new_key = []
        new_value = []
        for index_level in range(len(levels)):
            first_col = near_width + index_level * block_rows
            new_key.append(add_rows(level_key[index_level], key_term[first_col:first_col + block_rows], sibling_starts[index_level]))
            new_value.append(add_rows(level_value[index_level], value_term[first_col:first_col + block_rows], sibling_starts[index_level]))
        return ((attended, query_grad, nearby_key_rows, nearby_value_rows, new_key, new_value), None)
    initial = (jnp.zeros((ROWS, D), jnp.bfloat16), jnp.zeros((ROWS, D), jnp.bfloat16), jnp.zeros((ROWS + 2 * block_rows, D), jnp.float32), jnp.zeros((ROWS + 2 * block_rows, D), jnp.float32), [jnp.zeros((ROWS // 2 ** (level_num - 1), D), jnp.float32) for level_num in levels], [jnp.zeros((ROWS // 2 ** (level_num - 1), D), jnp.float32) for level_num in levels])
    finished, _ = lax.scan(one_block, initial, jnp.arange(block_count, dtype=jnp.int32))
    attended, query_grad, nearby_key_rows, nearby_value_rows, level_key, level_value = finished
    key_total = nearby_key_rows[block_rows:block_rows + ROWS]
    value_total = nearby_value_rows[block_rows:block_rows + ROWS]
    for index_level, level_num in enumerate(levels):
        group_size = 2 ** (level_num - 1)
        key_total = key_total + valid_rows[:, None] * jnp.repeat(level_key[index_level], group_size, axis=0) / group_size
        value_total = value_total + valid_rows[:, None] * jnp.repeat(level_value[index_level], group_size, axis=0) / group_size

    def restore(hilbert_rows):
        return jnp.zeros((ROWS, D), jnp.bfloat16).at[positions].set(hilbert_rows)
    return (restore(attended), restore(query_grad), restore(key_total.astype(jnp.bfloat16)), restore(value_total.astype(jnp.bfloat16)))
```

```python
import math

import jax
import jax.numpy as jnp
from jax import lax
from jax.experimental import pallas as pl
from jax.experimental.pallas import tpu as pltpu
from jax.sharding import PartitionSpec as P

D = 512
HEADS = 8
BLOCK = 128
AXES = ("rows", "sub")
LANES = 128


def attention_kernel(q_ref, g_ref, k_ref, v_ref, cv_ref, att_ref, qg_ref, kt_ref, vt_ref, *, head_dim, near_rows):
    rows = q_ref.shape[0]
    cols = k_ref.shape[0]
    scale = 1.0 / math.sqrt(head_dim)
    row = lax.broadcasted_iota(jnp.int32, (rows, cols), 0)
    col = lax.broadcasted_iota(jnp.int32, (rows, cols), 1)
    start = (row // BLOCK) * BLOCK
    in_window = (col >= start) & (col < start + 3 * BLOCK)
    ok = (col >= near_rows) | (in_window & (cv_ref[...] > 0))
    nt = (((1,), (1,)), ((), ()))
    tn = (((0,), (0,)), ((), ()))
    for h in range(LANES // head_dim):
        hs = slice(h * head_dim, (h + 1) * head_dim)
        q = q_ref[:, hs]
        g = g_ref[:, hs]
        k = k_ref[:, hs]
        v = v_ref[:, hs]
        s = lax.dot_general(q, k, nt, preferred_element_type=jnp.float32) * scale
        s = jnp.where(ok, s, -jnp.inf)
        m = jnp.max(s, axis=-1, keepdims=True)
        e = jnp.exp(s - m)
        w = e / jnp.sum(e, axis=-1, keepdims=True)
        wb = w.astype(jnp.bfloat16)
        att_ref[:, hs] = jnp.dot(wb, v, preferred_element_type=jnp.float32).astype(att_ref.dtype)
        vd = lax.dot_general(g, v, nt, preferred_element_type=jnp.float32)
        rd = jnp.sum(w * vd, axis=-1, keepdims=True)
        sg = (w * (vd - rd) * scale).astype(jnp.bfloat16)
        qg_ref[:, hs] = jnp.dot(sg, k, preferred_element_type=jnp.float32).astype(qg_ref.dtype)
        kt_ref[:, hs] = lax.dot_general(sg, q, tn, preferred_element_type=jnp.float32)
        vt_ref[:, hs] = lax.dot_general(wb, g, tn, preferred_element_type=jnp.float32)


def attention(q, g, k_all, v_all, col_valid, head_dim, near_rows):
    rows, features = q.shape
    cols = k_all.shape[0]
    row_spec = pl.BlockSpec((rows, LANES), lambda i: (0, i))
    col_spec = pl.BlockSpec((cols, LANES), lambda i: (0, i))
    kernel = lambda *refs: attention_kernel(*refs, head_dim=head_dim, near_rows=near_rows)
    return pl.pallas_call(
        kernel,
        grid=(features // LANES,),
        in_specs=[row_spec, row_spec, col_spec, col_spec, pl.BlockSpec((1, cols), lambda i: (0, 0))],
        out_specs=[row_spec, row_spec, col_spec, col_spec],
        out_shape=[
            jax.ShapeDtypeStruct((rows, features), jnp.bfloat16),
            jax.ShapeDtypeStruct((rows, features), jnp.bfloat16),
            jax.ShapeDtypeStruct((cols, features), jnp.float32),
            jax.ShapeDtypeStruct((cols, features), jnp.float32),
        ],
    )(q, g, k_all, v_all, col_valid)


def xor_permute(value, distance, count):
    return lax.ppermute(value, AXES, [(i, i ^ distance) for i in range(count)])


def per_device(queries, key_table, value_table, out_grad, hilbert_order, key_valid):
    rows_dev, features = queries.shape
    head_dim = D // HEADS
    shard_count = lax.axis_size(AXES)
    shard_bits = shard_count.bit_length() - 1
    my_index = lax.axis_index(AXES)
    permute = hilbert_order[0]
    query_rows = queries[permute]
    grad_rows = out_grad[permute]
    table_rows = jnp.stack([key_table[permute], value_table[permute]])
    padded_valid = jnp.pad(key_valid, (BLOCK, BLOCK))
    edge_valid = lax.dynamic_slice_in_dim(padded_valid, my_index * rows_dev, rows_dev + 2 * BLOCK)
    own_valid = edge_valid[BLOCK : BLOCK + rows_dev].astype(jnp.float32)[None, :, None]
    masked = table_rows.astype(jnp.float32) * own_valid

    up = [(i, i + 1) for i in range(shard_count - 1)]
    down = [(i + 1, i) for i in range(shard_count - 1)]
    before = lax.ppermute(table_rows[:, rows_dev - BLOCK :], AXES, up)
    after = lax.ppermute(table_rows[:, :BLOCK], AXES, down)

    distances = []
    far_chunks = []
    for bit in range(shard_bits):
        group = 2 ** (bit + 1)
        pooled = jnp.sum(masked.reshape(2, rows_dev // group, group, features), axis=2) / group
        pooled = pooled.astype(jnp.bfloat16)
        for low in range(2**bit):
            distance = (1 << bit) | low
            distances.append((bit, distance))
            far_chunks.append(xor_permute(pooled, distance, shard_count))

    full = jnp.concatenate([before, table_rows, after] + far_chunks, axis=1)
    near_rows = rows_dev + 2 * BLOCK
    cols = full.shape[1]
    col_valid = jnp.concatenate(
        [edge_valid, jnp.ones((cols - near_rows,), edge_valid.dtype)]
    ).reshape(1, cols)
    attended, query_grad, key_term, value_term = attention(
        query_rows, grad_rows, full[0], full[1], col_valid, head_dim, near_rows
    )
    terms = jnp.stack([key_term, value_term])

    from_next = lax.ppermute(terms[:, :BLOCK], AXES, down)
    from_prev = lax.ppermute(terms[:, near_rows - BLOCK : near_rows], AXES, up)
    row_grad = terms[:, BLOCK : BLOCK + rows_dev]
    row_grad = row_grad.at[:, :BLOCK].add(from_prev)
    row_grad = row_grad.at[:, rows_dev - BLOCK :].add(from_next)

    offset = near_rows
    level_sums = {}
    for (bit, distance), chunk in zip(distances, far_chunks):
        size = chunk.shape[1]
        returned = xor_permute(
            terms[:, offset : offset + size].astype(jnp.bfloat16), distance, shard_count
        ).astype(jnp.float32)
        offset += size
        level_sums[bit] = returned if bit not in level_sums else level_sums[bit] + returned
    for bit in range(shard_bits):
        group = 2 ** (bit + 1)
        row_grad = row_grad + own_valid * (jnp.repeat(level_sums[bit], group, axis=1) / group)

    def restore(hilbert_rows):
        return jnp.zeros((rows_dev, features), jnp.bfloat16).at[permute].set(hilbert_rows)

    return (
        restore(attended),
        restore(query_grad),
        restore(row_grad[0].astype(jnp.bfloat16)),
        restore(row_grad[1].astype(jnp.bfloat16)),
    )


def solution(mesh):
    in_specs = (
        P(("parts", "rows", "sub"), "head"),
        P(("parts", "rows", "sub"), "head"),
        P(("parts", "rows", "sub"), "head"),
        P(("parts", "rows", "sub"), "head"),
        P(("parts", "rows", "sub"), None),
        P("parts"),
    )
    out_specs = (
        P(("parts", "rows", "sub"), "head"),
        P(("parts", "rows", "sub"), "head"),
        P(("parts", "rows", "sub"), "head"),
        P(("parts", "rows", "sub"), "head"),
    )
    return jax.shard_map(
        per_device, mesh=mesh, in_specs=in_specs, out_specs=out_specs, check_vma=False
    )
```

```python
import math

import jax
import jax.numpy as jnp
from jax import lax
from jax.experimental import pallas as pl
from jax.experimental.pallas import tpu as pltpu
from jax.sharding import PartitionSpec as P

D = 512
HEADS = 8
BLOCK = 128
AXES = ("rows", "sub")
LANES = 128


def attention_kernel(q_ref, g_ref, k_ref, v_ref, cv_ref, att_ref, qg_ref, kt_ref, vt_ref, *, head_dim, near_rows):
    rows = q_ref.shape[0]
    cols = k_ref.shape[0]
    scale = 1.0 / math.sqrt(head_dim)
    row = lax.broadcasted_iota(jnp.int32, (rows, cols), 0)
    col = lax.broadcasted_iota(jnp.int32, (rows, cols), 1)
    start = (row // BLOCK) * BLOCK
    in_window = (col >= start) & (col < start + 3 * BLOCK)
    ok = (col >= near_rows) | (in_window & (cv_ref[...] > 0))
    nt = (((1,), (1,)), ((), ()))
    tn = (((0,), (0,)), ((), ()))
    for h in range(LANES // head_dim):
        hs = slice(h * head_dim, (h + 1) * head_dim)
        q = q_ref[:, hs]
        g = g_ref[:, hs]
        k = k_ref[:, hs]
        v = v_ref[:, hs]
        s = lax.dot_general(q, k, nt, preferred_element_type=jnp.float32) * scale
        s = jnp.where(ok, s, -jnp.inf)
        m = jnp.max(s, axis=-1, keepdims=True)
        e = jnp.exp(s - m)
        w = e / jnp.sum(e, axis=-1, keepdims=True)
        wb = w.astype(jnp.bfloat16)
        att_ref[:, hs] = jnp.dot(wb, v, preferred_element_type=jnp.float32).astype(att_ref.dtype)
        vd = lax.dot_general(g, v, nt, preferred_element_type=jnp.float32)
        rd = jnp.sum(w * vd, axis=-1, keepdims=True)
        sg = (w * (vd - rd) * scale).astype(jnp.bfloat16)
        qg_ref[:, hs] = jnp.dot(sg, k, preferred_element_type=jnp.float32).astype(qg_ref.dtype)
        kt_ref[:, hs] = lax.dot_general(sg, q, tn, preferred_element_type=jnp.float32)
        vt_ref[:, hs] = lax.dot_general(wb, g, tn, preferred_element_type=jnp.float32)


def attention(q, g, k_all, v_all, col_valid, head_dim, near_rows):
    rows, features = q.shape
    cols = k_all.shape[0]
    row_spec = pl.BlockSpec((rows, LANES), lambda i: (0, i))
    col_spec = pl.BlockSpec((cols, LANES), lambda i: (0, i))
    kernel = lambda *refs: attention_kernel(*refs, head_dim=head_dim, near_rows=near_rows)
    return pl.pallas_call(
        kernel,
        grid=(features // LANES,),
        in_specs=[row_spec, row_spec, col_spec, col_spec, pl.BlockSpec((1, cols), lambda i: (0, 0))],
        out_specs=[row_spec, row_spec, col_spec, col_spec],
        out_shape=[
            jax.ShapeDtypeStruct((rows, features), jnp.bfloat16),
            jax.ShapeDtypeStruct((rows, features), jnp.bfloat16),
            jax.ShapeDtypeStruct((cols, features), jnp.float32),
            jax.ShapeDtypeStruct((cols, features), jnp.float32),
        ],
    )(q, g, k_all, v_all, col_valid)


def xor_permute(value, distance, count):
    return lax.ppermute(value, AXES, [(i, i ^ distance) for i in range(count)])


def per_device(queries, key_table, value_table, out_grad, hilbert_order, key_valid):
    rows_dev, features = queries.shape
    head_dim = D // HEADS
    shard_count = lax.axis_size(AXES)
    shard_bits = shard_count.bit_length() - 1
    my_index = lax.axis_index(AXES)
    permute = hilbert_order[0]
    query_rows = queries[permute]
    grad_rows = out_grad[permute]
    table_rows = jnp.stack([key_table[permute], value_table[permute]])
    padded_valid = jnp.pad(key_valid, (BLOCK, BLOCK))
    edge_valid = lax.dynamic_slice_in_dim(padded_valid, my_index * rows_dev, rows_dev + 2 * BLOCK)
    own_valid = edge_valid[BLOCK : BLOCK + rows_dev].astype(jnp.float32)[None, :, None]
    masked = table_rows.astype(jnp.float32) * own_valid

    up = [(i, i + 1) for i in range(shard_count - 1)]
    down = [(i + 1, i) for i in range(shard_count - 1)]
    before = lax.ppermute(table_rows[:, rows_dev - BLOCK :], AXES, up)
    after = lax.ppermute(table_rows[:, :BLOCK], AXES, down)

    low_bits = shard_bits // 2
    low_count = 2**low_bits
    high_bits = list(range(low_bits, shard_bits))
    pooled = []
    for bit in range(shard_bits):
        group = 2 ** (bit + 1)
        summed = jnp.sum(masked.reshape(2, rows_dev // group, group, features), axis=2) / group
        pooled.append(summed.astype(jnp.bfloat16))
    sizes = [p.shape[1] for p in pooled]

    far_chunks = []
    gathered = {bit: [pooled[bit]] for bit in high_bits}
    for low in range(1, low_count):
        bit = low.bit_length() - 1
        payload = jnp.concatenate([pooled[bit]] + [pooled[b] for b in high_bits], axis=1)
        received = xor_permute(payload, low, shard_count)
        far_chunks.append(received[:, : sizes[bit]])
        offset = sizes[bit]
        for b in high_bits:
            gathered[b].append(received[:, offset : offset + sizes[b]])
            offset += sizes[b]
    high_distances = [high << low_bits for high in range(1, 2 ** (shard_bits - low_bits))]
    stacked = {b: jnp.concatenate(gathered[b], axis=1) for b in high_bits}
    for distance in high_distances:
        bit = distance.bit_length() - 1
        far_chunks.append(xor_permute(stacked[bit], distance, shard_count))

    full = jnp.concatenate([before, table_rows, after] + far_chunks, axis=1)
    near_rows = rows_dev + 2 * BLOCK
    cols = full.shape[1]
    col_valid = jnp.concatenate(
        [edge_valid, jnp.ones((cols - near_rows,), edge_valid.dtype)]
    ).reshape(1, cols)
    attended, query_grad, key_term, value_term = attention(
        query_rows, grad_rows, full[0], full[1], col_valid, head_dim, near_rows
    )
    terms = jnp.stack([key_term, value_term])

    from_next = lax.ppermute(terms[:, :BLOCK], AXES, down)
    from_prev = lax.ppermute(terms[:, near_rows - BLOCK : near_rows], AXES, up)
    row_grad = terms[:, BLOCK : BLOCK + rows_dev]
    row_grad = row_grad.at[:, :BLOCK].add(from_prev)
    row_grad = row_grad.at[:, rows_dev - BLOCK :].add(from_next)

    offset = near_rows
    direct_terms = []
    for low in range(1, low_count):
        size = sizes[low.bit_length() - 1]
        direct_terms.append(terms[:, offset : offset + size])
        offset += size
    stacked_sums = {}
    for distance in high_distances:
        bit = distance.bit_length() - 1
        size = low_count * sizes[bit]
        returned = xor_permute(
            terms[:, offset : offset + size].astype(jnp.bfloat16), distance, shard_count
        ).astype(jnp.float32)
        offset += size
        stacked_sums[bit] = returned if bit not in stacked_sums else stacked_sums[bit] + returned
    level_sums = {b: stacked_sums[b][:, : sizes[b]] for b in high_bits}
    for low in range(1, low_count):
        bit = low.bit_length() - 1
        parts = [direct_terms[low - 1]] + [
            stacked_sums[b][:, low * sizes[b] : (low + 1) * sizes[b]] for b in high_bits
        ]
        received = xor_permute(jnp.concatenate(parts, axis=1), low, shard_count)
        level_sums[bit] = (
            received[:, : sizes[bit]] if bit not in level_sums else level_sums[bit] + received[:, : sizes[bit]]
        )
        offset = sizes[bit]
        for b in high_bits:
            level_sums[b] = level_sums[b] + received[:, offset : offset + sizes[b]]
            offset += sizes[b]
    for bit in range(shard_bits):
        group = 2 ** (bit + 1)
        row_grad = row_grad + own_valid * (jnp.repeat(level_sums[bit], group, axis=1) / group)

    def restore(hilbert_rows):
        return jnp.zeros((rows_dev, features), jnp.bfloat16).at[permute].set(hilbert_rows)

    return (
        restore(attended),
        restore(query_grad),
        restore(row_grad[0].astype(jnp.bfloat16)),
        restore(row_grad[1].astype(jnp.bfloat16)),
    )


def solution(mesh):
    in_specs = (
        P(("parts", "rows", "sub"), "head"),
        P(("parts", "rows", "sub"), "head"),
        P(("parts", "rows", "sub"), "head"),
        P(("parts", "rows", "sub"), "head"),
        P(("parts", "rows", "sub"), None),
        P("parts"),
    )
    out_specs = (
        P(("parts", "rows", "sub"), "head"),
        P(("parts", "rows", "sub"), "head"),
        P(("parts", "rows", "sub"), "head"),
        P(("parts", "rows", "sub"), "head"),
    )
    return jax.shard_map(
        per_device, mesh=mesh, in_specs=in_specs, out_specs=out_specs, check_vma=False
    )
```

```python
import math

import jax
import jax.numpy as jnp
from jax import lax
from jax.experimental import pallas as pl
from jax.experimental.pallas import tpu as pltpu
from jax.sharding import PartitionSpec as P

D = 512
HEADS = 8
BLOCK = 128
AXES = ("rows", "sub")
LANES = 128


def attention_kernel(q_ref, g_ref, k_ref, v_ref, cv_ref, att_ref, qg_ref, kt_ref, vt_ref, *, head_dim, near_rows):
    rows = q_ref.shape[0]
    cols = k_ref.shape[0]
    scale = 1.0 / math.sqrt(head_dim)
    row = lax.broadcasted_iota(jnp.int32, (rows, cols), 0)
    col = lax.broadcasted_iota(jnp.int32, (rows, cols), 1)
    start = (row // BLOCK) * BLOCK
    in_window = (col >= start) & (col < start + 3 * BLOCK)
    ok = (col >= near_rows) | (in_window & (cv_ref[...] > 0))
    nt = (((1,), (1,)), ((), ()))
    tn = (((0,), (0,)), ((), ()))
    for h in range(LANES // head_dim):
        hs = slice(h * head_dim, (h + 1) * head_dim)
        q = q_ref[:, hs]
        g = g_ref[:, hs]
        k = k_ref[:, hs]
        v = v_ref[:, hs]
        s = lax.dot_general(q, k, nt, preferred_element_type=jnp.float32) * scale
        s = jnp.where(ok, s, -jnp.inf)
        m = jnp.max(s, axis=-1, keepdims=True)
        e = jnp.exp(s - m)
        w = e / jnp.sum(e, axis=-1, keepdims=True)
        wb = w.astype(jnp.bfloat16)
        att_ref[:, hs] = jnp.dot(wb, v, preferred_element_type=jnp.float32).astype(att_ref.dtype)
        vd = lax.dot_general(g, v, nt, preferred_element_type=jnp.float32)
        rd = jnp.sum(w * vd, axis=-1, keepdims=True)
        sg = (w * (vd - rd) * scale).astype(jnp.bfloat16)
        qg_ref[:, hs] = jnp.dot(sg, k, preferred_element_type=jnp.float32).astype(qg_ref.dtype)
        kt_ref[:, hs] = lax.dot_general(sg, q, tn, preferred_element_type=jnp.float32)
        vt_ref[:, hs] = lax.dot_general(wb, g, tn, preferred_element_type=jnp.float32)


def attention(q, g, k_all, v_all, col_valid, head_dim, near_rows):
    rows, features = q.shape
    cols = k_all.shape[0]
    row_spec = pl.BlockSpec((rows, LANES), lambda i: (0, i))
    col_spec = pl.BlockSpec((cols, LANES), lambda i: (0, i))
    kernel = lambda *refs: attention_kernel(*refs, head_dim=head_dim, near_rows=near_rows)
    return pl.pallas_call(
        kernel,
        grid=(features // LANES,),
        in_specs=[row_spec, row_spec, col_spec, col_spec, pl.BlockSpec((1, cols), lambda i: (0, 0))],
        out_specs=[row_spec, row_spec, col_spec, col_spec],
        out_shape=[
            jax.ShapeDtypeStruct((rows, features), jnp.bfloat16),
            jax.ShapeDtypeStruct((rows, features), jnp.bfloat16),
            jax.ShapeDtypeStruct((cols, features), jnp.float32),
            jax.ShapeDtypeStruct((cols, features), jnp.float32),
        ],
    )(q, g, k_all, v_all, col_valid)


def xor_permute(value, distance, count):
    return lax.ppermute(value, AXES, [(i, i ^ distance) for i in range(count)])


def per_device(queries, key_table, value_table, out_grad, hilbert_order, key_valid):
    rows_dev, features = queries.shape
    head_dim = D // HEADS
    shard_count = lax.axis_size(AXES)
    shard_bits = shard_count.bit_length() - 1
    my_index = lax.axis_index(AXES)
    permute = hilbert_order[0]
    one_hot = (permute[:, None] == lax.broadcasted_iota(jnp.int32, (rows_dev, rows_dev), 1)).astype(
        jnp.bfloat16
    )

    def take(storage_rows):
        return jnp.dot(one_hot, storage_rows, preferred_element_type=jnp.float32).astype(jnp.bfloat16)

    query_rows = take(queries)
    grad_rows = take(out_grad)
    table_rows = jnp.stack([take(key_table), take(value_table)])
    padded_valid = jnp.pad(key_valid, (BLOCK, BLOCK))
    edge_valid = lax.dynamic_slice_in_dim(padded_valid, my_index * rows_dev, rows_dev + 2 * BLOCK)
    own_valid = edge_valid[BLOCK : BLOCK + rows_dev].astype(jnp.float32)[None, :, None]
    masked = table_rows.astype(jnp.float32) * own_valid

    up = [(i, i + 1) for i in range(shard_count - 1)]
    down = [(i + 1, i) for i in range(shard_count - 1)]
    before = lax.ppermute(table_rows[:, rows_dev - BLOCK :], AXES, up)
    after = lax.ppermute(table_rows[:, :BLOCK], AXES, down)

    low_bits = shard_bits // 2
    low_count = 2**low_bits
    high_bits = list(range(low_bits, shard_bits))
    pooled = []
    for bit in range(shard_bits):
        group = 2 ** (bit + 1)
        summed = jnp.sum(masked.reshape(2, rows_dev // group, group, features), axis=2) / group
        pooled.append(summed.astype(jnp.bfloat16))
    sizes = [p.shape[1] for p in pooled]

    far_chunks = []
    gathered = {bit: [pooled[bit]] for bit in high_bits}
    for low in range(1, low_count):
        bit = low.bit_length() - 1
        payload = jnp.concatenate([pooled[bit]] + [pooled[b] for b in high_bits], axis=1)
        received = xor_permute(payload, low, shard_count)
        far_chunks.append(received[:, : sizes[bit]])
        offset = sizes[bit]
        for b in high_bits:
            gathered[b].append(received[:, offset : offset + sizes[b]])
            offset += sizes[b]
    high_distances = [high << low_bits for high in range(1, 2 ** (shard_bits - low_bits))]
    stacked = {b: jnp.concatenate(gathered[b], axis=1) for b in high_bits}
    for distance in high_distances:
        bit = distance.bit_length() - 1
        far_chunks.append(xor_permute(stacked[bit], distance, shard_count))

    full = jnp.concatenate([before, table_rows, after] + far_chunks, axis=1)
    near_rows = rows_dev + 2 * BLOCK
    cols = full.shape[1]
    col_valid = jnp.concatenate(
        [edge_valid, jnp.ones((cols - near_rows,), edge_valid.dtype)]
    ).reshape(1, cols)
    attended, query_grad, key_term, value_term = attention(
        query_rows, grad_rows, full[0], full[1], col_valid, head_dim, near_rows
    )
    terms = jnp.stack([key_term, value_term])

    from_next = lax.ppermute(terms[:, :BLOCK], AXES, down)
    from_prev = lax.ppermute(terms[:, near_rows - BLOCK : near_rows], AXES, up)
    row_grad = terms[:, BLOCK : BLOCK + rows_dev]
    row_grad = row_grad.at[:, :BLOCK].add(from_prev)
    row_grad = row_grad.at[:, rows_dev - BLOCK :].add(from_next)

    offset = near_rows
    direct_terms = []
    for low in range(1, low_count):
        size = sizes[low.bit_length() - 1]
        direct_terms.append(terms[:, offset : offset + size])
        offset += size
    stacked_sums = {}
    for distance in high_distances:
        bit = distance.bit_length() - 1
        size = low_count * sizes[bit]
        returned = xor_permute(
            terms[:, offset : offset + size].astype(jnp.bfloat16), distance, shard_count
        ).astype(jnp.float32)
        offset += size
        stacked_sums[bit] = returned if bit not in stacked_sums else stacked_sums[bit] + returned
    level_sums = {b: stacked_sums[b][:, : sizes[b]] for b in high_bits}
    for low in range(1, low_count):
        bit = low.bit_length() - 1
        parts = [direct_terms[low - 1]] + [
            stacked_sums[b][:, low * sizes[b] : (low + 1) * sizes[b]] for b in high_bits
        ]
        received = xor_permute(jnp.concatenate(parts, axis=1), low, shard_count)
        level_sums[bit] = (
            received[:, : sizes[bit]] if bit not in level_sums else level_sums[bit] + received[:, : sizes[bit]]
        )
        offset = sizes[bit]
        for b in high_bits:
            level_sums[b] = level_sums[b] + received[:, offset : offset + sizes[b]]
            offset += sizes[b]
    for bit in range(shard_bits):
        group = 2 ** (bit + 1)
        row_grad = row_grad + own_valid * (jnp.repeat(level_sums[bit], group, axis=1) / group)

    def restore(hilbert_rows):
        restored = lax.dot_general(
            one_hot, hilbert_rows, (((0,), (0,)), ((), ())), preferred_element_type=jnp.float32
        )
        return restored.astype(jnp.bfloat16)

    return (
        restore(attended),
        restore(query_grad),
        restore(row_grad[0].astype(jnp.bfloat16)),
        restore(row_grad[1].astype(jnp.bfloat16)),
    )


def solution(mesh):
    in_specs = (
        P(("parts", "rows", "sub"), "head"),
        P(("parts", "rows", "sub"), "head"),
        P(("parts", "rows", "sub"), "head"),
        P(("parts", "rows", "sub"), "head"),
        P(("parts", "rows", "sub"), None),
        P("parts"),
    )
    out_specs = (
        P(("parts", "rows", "sub"), "head"),
        P(("parts", "rows", "sub"), "head"),
        P(("parts", "rows", "sub"), "head"),
        P(("parts", "rows", "sub"), "head"),
    )
    return jax.shard_map(
        per_device, mesh=mesh, in_specs=in_specs, out_specs=out_specs, check_vma=False
    )
```

```python
import math

import jax
import jax.numpy as jnp
from jax import lax
from jax.experimental import pallas as pl
from jax.experimental.pallas import tpu as pltpu
from jax.sharding import PartitionSpec as P

D = 512
HEADS = 8
BLOCK = 128
AXES = ("rows", "sub")
LANES = 128


def attention_kernel(
    order_col_ref, order_row_ref, q_ref, g_ref, kv_ref, cv_ref, att_ref, qg_ref, terms_ref, att_tmp, qg_tmp,
    *, head_dim, near_rows
):
    rows = q_ref.shape[0]
    cols = kv_ref.shape[1]
    scale = 1.0 / math.sqrt(head_dim)
    gather = (
        order_col_ref[...] == lax.broadcasted_iota(jnp.int32, (rows, rows), 1)
    ).astype(jnp.bfloat16)
    scatter = (
        order_row_ref[...] == lax.broadcasted_iota(jnp.int32, (rows, rows), 0)
    ).astype(jnp.bfloat16)
    q_all = jnp.dot(gather, q_ref[...], preferred_element_type=jnp.float32).astype(jnp.bfloat16)
    g_all = jnp.dot(gather, g_ref[...], preferred_element_type=jnp.float32).astype(jnp.bfloat16)
    row = lax.broadcasted_iota(jnp.int32, (rows, cols), 0)
    col = lax.broadcasted_iota(jnp.int32, (rows, cols), 1)
    start = (row // BLOCK) * BLOCK
    in_window = (col >= start) & (col < start + 3 * BLOCK)
    ok = (col >= near_rows) | (in_window & (cv_ref[...] > 0))
    nt = (((1,), (1,)), ((), ()))
    tn = (((0,), (0,)), ((), ()))
    for h in range(LANES // head_dim):
        hs = slice(h * head_dim, (h + 1) * head_dim)
        q = q_all[:, hs]
        g = g_all[:, hs]
        k = kv_ref[0, :, hs]
        v = kv_ref[1, :, hs]
        s = lax.dot_general(q, k, nt, preferred_element_type=jnp.float32) * scale
        s = jnp.where(ok, s, -jnp.inf)
        m = jnp.max(s, axis=-1, keepdims=True)
        e = jnp.exp(s - m)
        w = e / jnp.sum(e, axis=-1, keepdims=True)
        wb = w.astype(jnp.bfloat16)
        att_tmp[:, hs] = jnp.dot(wb, v, preferred_element_type=jnp.float32).astype(jnp.bfloat16)
        vd = lax.dot_general(g, v, nt, preferred_element_type=jnp.float32)
        rd = jnp.sum(w * vd, axis=-1, keepdims=True)
        sg = (w * (vd - rd) * scale).astype(jnp.bfloat16)
        qg_tmp[:, hs] = jnp.dot(sg, k, preferred_element_type=jnp.float32).astype(jnp.bfloat16)
        terms_ref[0, :, hs] = lax.dot_general(sg, q, tn, preferred_element_type=jnp.float32)
        terms_ref[1, :, hs] = lax.dot_general(wb, g, tn, preferred_element_type=jnp.float32)
    att_ref[...] = jnp.dot(scatter, att_tmp[...], preferred_element_type=jnp.float32).astype(att_ref.dtype)
    qg_ref[...] = jnp.dot(scatter, qg_tmp[...], preferred_element_type=jnp.float32).astype(qg_ref.dtype)


def attention(order, queries, out_grad, kv_all, col_valid, head_dim, near_rows):
    rows, features = queries.shape
    cols = kv_all.shape[1]
    row_spec = pl.BlockSpec((rows, LANES), lambda i: (0, i))
    kv_spec = pl.BlockSpec((2, cols, LANES), lambda i: (0, 0, i))
    kernel = lambda *refs: attention_kernel(*refs, head_dim=head_dim, near_rows=near_rows)
    return pl.pallas_call(
        kernel,
        grid=(features // LANES,),
        in_specs=[
            pl.BlockSpec((rows, 1), lambda i: (0, 0)),
            pl.BlockSpec((1, rows), lambda i: (0, 0)),
            row_spec,
            row_spec,
            kv_spec,
            pl.BlockSpec((1, cols), lambda i: (0, 0)),
        ],
        out_specs=[row_spec, row_spec, kv_spec],
        out_shape=[
            jax.ShapeDtypeStruct((rows, features), jnp.bfloat16),
            jax.ShapeDtypeStruct((rows, features), jnp.bfloat16),
            jax.ShapeDtypeStruct((2, cols, features), jnp.float32),
        ],
        scratch_shapes=[pltpu.VMEM((rows, LANES), jnp.bfloat16), pltpu.VMEM((rows, LANES), jnp.bfloat16)],
    )(order.reshape(rows, 1), order.reshape(1, rows), queries, out_grad, kv_all, col_valid)


def finalize_kernel(order_row_ref, valid_ref, terms_ref, prev_ref, next_ref, *rest):
    level_refs = rest[:-2]
    key_ref, value_ref = rest[-2:]
    rows = key_ref.shape[0]
    scatter = (
        order_row_ref[...] == lax.broadcasted_iota(jnp.int32, (rows, rows), 0)
    ).astype(jnp.bfloat16)
    for c, out_ref in enumerate((key_ref, value_ref)):
        total = terms_ref[c, BLOCK : BLOCK + rows, :] + jnp.concatenate([prev_ref[c], next_ref[c]], axis=0)
        spread = None
        for level_ref in level_refs:
            pooled_rows = level_ref.shape[1]
            group = rows // pooled_rows
            expand = jnp.where(
                lax.broadcasted_iota(jnp.int32, (rows, pooled_rows), 0) // group
                == lax.broadcasted_iota(jnp.int32, (rows, pooled_rows), 1),
                1.0 / group,
                0.0,
            ).astype(jnp.float32)
            part = jnp.dot(
                expand, level_ref[c], preferred_element_type=jnp.float32, precision=lax.Precision.HIGHEST
            )
            spread = part if spread is None else spread + part
        total = total + valid_ref[...] * spread
        out_ref[...] = jnp.dot(
            scatter, total.astype(jnp.bfloat16), preferred_element_type=jnp.float32
        ).astype(out_ref.dtype)


def finalize(order, valid, terms, from_prev, from_next, levels):
    rows = order.shape[0]
    features = terms.shape[2]
    cols = terms.shape[1]
    edge_spec = pl.BlockSpec((2, BLOCK, LANES), lambda i: (0, 0, i))
    level_specs = [pl.BlockSpec((2, lv.shape[1], LANES), lambda i: (0, 0, i)) for lv in levels]
    out_spec = pl.BlockSpec((rows, LANES), lambda i: (0, i))
    return pl.pallas_call(
        finalize_kernel,
        grid=(features // LANES,),
        in_specs=[
            pl.BlockSpec((1, rows), lambda i: (0, 0)),
            pl.BlockSpec((rows, 1), lambda i: (0, 0)),
            pl.BlockSpec((2, cols, LANES), lambda i: (0, 0, i)),
            edge_spec,
            edge_spec,
        ]
        + level_specs,
        out_specs=[out_spec, out_spec],
        out_shape=[
            jax.ShapeDtypeStruct((rows, features), jnp.bfloat16),
            jax.ShapeDtypeStruct((rows, features), jnp.bfloat16),
        ],
    )(order.reshape(1, rows), valid.reshape(rows, 1), terms, from_prev, from_next, *levels)


def xor_permute(value, distance, count):
    return lax.ppermute(value, AXES, [(i, i ^ distance) for i in range(count)])


def per_device(queries, key_table, value_table, out_grad, hilbert_order, key_valid):
    rows_dev, features = queries.shape
    head_dim = D // HEADS
    shard_count = lax.axis_size(AXES)
    shard_bits = shard_count.bit_length() - 1
    my_index = lax.axis_index(AXES)
    permute = hilbert_order[0]
    one_hot = (permute[:, None] == lax.broadcasted_iota(jnp.int32, (rows_dev, rows_dev), 1)).astype(
        jnp.bfloat16
    )

    def take(storage_rows):
        return jnp.dot(one_hot, storage_rows, preferred_element_type=jnp.float32).astype(jnp.bfloat16)

    table_rows = jnp.stack([take(key_table), take(value_table)])
    padded_valid = jnp.pad(key_valid, (BLOCK, BLOCK))
    edge_valid = lax.dynamic_slice_in_dim(padded_valid, my_index * rows_dev, rows_dev + 2 * BLOCK)
    own_valid_rows = edge_valid[BLOCK : BLOCK + rows_dev].astype(jnp.float32)
    own_valid = own_valid_rows[None, :, None]
    masked = table_rows.astype(jnp.float32) * own_valid

    up = [(i, i + 1) for i in range(shard_count - 1)]
    down = [(i + 1, i) for i in range(shard_count - 1)]
    before = lax.ppermute(table_rows[:, rows_dev - BLOCK :], AXES, up)
    after = lax.ppermute(table_rows[:, :BLOCK], AXES, down)

    low_bits = shard_bits // 2
    low_count = 2**low_bits
    high_bits = list(range(low_bits, shard_bits))
    pooled = []
    for bit in range(shard_bits):
        group = 2 ** (bit + 1)
        summed = jnp.sum(masked.reshape(2, rows_dev // group, group, features), axis=2) / group
        pooled.append(summed.astype(jnp.bfloat16))
    sizes = [p.shape[1] for p in pooled]

    far_chunks = []
    gathered = {bit: [pooled[bit]] for bit in high_bits}
    for low in range(1, low_count):
        bit = low.bit_length() - 1
        payload = jnp.concatenate([pooled[bit]] + [pooled[b] for b in high_bits], axis=1)
        received = xor_permute(payload, low, shard_count)
        far_chunks.append(received[:, : sizes[bit]])
        offset = sizes[bit]
        for b in high_bits:
            gathered[b].append(received[:, offset : offset + sizes[b]])
            offset += sizes[b]
    high_distances = [high << low_bits for high in range(1, 2 ** (shard_bits - low_bits))]
    stacked = {b: jnp.concatenate(gathered[b], axis=1) for b in high_bits}
    for distance in high_distances:
        bit = distance.bit_length() - 1
        far_chunks.append(xor_permute(stacked[bit], distance, shard_count))

    full = jnp.concatenate([before, table_rows, after] + far_chunks, axis=1)
    near_rows = rows_dev + 2 * BLOCK
    cols = full.shape[1]
    col_valid = jnp.concatenate(
        [edge_valid, jnp.ones((cols - near_rows,), edge_valid.dtype)]
    ).reshape(1, cols)
    attended, query_grad, terms = attention(
        permute, queries, out_grad, full, col_valid, head_dim, near_rows
    )

    from_next = lax.ppermute(terms[:, :BLOCK], AXES, down)
    from_prev = lax.ppermute(terms[:, near_rows - BLOCK : near_rows], AXES, up)

    offset = near_rows
    direct_terms = []
    for low in range(1, low_count):
        size = sizes[low.bit_length() - 1]
        direct_terms.append(terms[:, offset : offset + size])
        offset += size
    stacked_sums = {}
    for distance in high_distances:
        bit = distance.bit_length() - 1
        size = low_count * sizes[bit]
        returned = xor_permute(
            terms[:, offset : offset + size].astype(jnp.bfloat16), distance, shard_count
        ).astype(jnp.float32)
        offset += size
        stacked_sums[bit] = returned if bit not in stacked_sums else stacked_sums[bit] + returned
    level_sums = {b: stacked_sums[b][:, : sizes[b]] for b in high_bits}
    for low in range(1, low_count):
        bit = low.bit_length() - 1
        parts = [direct_terms[low - 1]] + [
            stacked_sums[b][:, low * sizes[b] : (low + 1) * sizes[b]] for b in high_bits
        ]
        received = xor_permute(jnp.concatenate(parts, axis=1), low, shard_count)
        level_sums[bit] = (
            received[:, : sizes[bit]] if bit not in level_sums else level_sums[bit] + received[:, : sizes[bit]]
        )
        offset = sizes[bit]
        for b in high_bits:
            level_sums[b] = level_sums[b] + received[:, offset : offset + sizes[b]]
            offset += sizes[b]
    key_grad, value_grad = finalize(
        permute, own_valid_rows, terms, from_prev, from_next, [level_sums[b] for b in range(shard_bits)]
    )
    return (attended, query_grad, key_grad, value_grad)


def solution(mesh):
    in_specs = (
        P(("parts", "rows", "sub"), "head"),
        P(("parts", "rows", "sub"), "head"),
        P(("parts", "rows", "sub"), "head"),
        P(("parts", "rows", "sub"), "head"),
        P(("parts", "rows", "sub"), None),
        P("parts"),
    )
    out_specs = (
        P(("parts", "rows", "sub"), "head"),
        P(("parts", "rows", "sub"), "head"),
        P(("parts", "rows", "sub"), "head"),
        P(("parts", "rows", "sub"), "head"),
    )
    return jax.shard_map(
        per_device, mesh=mesh, in_specs=in_specs, out_specs=out_specs, check_vma=False
    )
```

```python
import math

import jax
import jax.numpy as jnp
from jax import lax
from jax.experimental import pallas as pl
from jax.experimental.pallas import tpu as pltpu
from jax.sharding import PartitionSpec as P

D = 512
HEADS = 8
BLOCK = 128
AXES = ("rows", "sub")
LANES = 128


def attention_kernel(
    order_col_ref, order_row_ref, q_ref, g_ref, kv_ref, cv_ref, att_ref, qg_ref, near_ref, far_ref, att_tmp, qg_tmp,
    *, head_dim, near_rows
):
    rows = q_ref.shape[0]
    cols = kv_ref.shape[1]
    scale = 1.0 / math.sqrt(head_dim)
    gather = (
        order_col_ref[...] == lax.broadcasted_iota(jnp.int32, (rows, rows), 1)
    ).astype(jnp.bfloat16)
    scatter = (
        order_row_ref[...] == lax.broadcasted_iota(jnp.int32, (rows, rows), 0)
    ).astype(jnp.bfloat16)
    q_all = jnp.dot(gather, q_ref[...], preferred_element_type=jnp.float32).astype(jnp.bfloat16)
    g_all = jnp.dot(gather, g_ref[...], preferred_element_type=jnp.float32).astype(jnp.bfloat16)
    row = lax.broadcasted_iota(jnp.int32, (rows, cols), 0)
    col = lax.broadcasted_iota(jnp.int32, (rows, cols), 1)
    start = (row // BLOCK) * BLOCK
    in_window = (col >= start) & (col < start + 3 * BLOCK)
    ok = (col >= near_rows) | (in_window & (cv_ref[...] > 0))
    nt = (((1,), (1,)), ((), ()))
    tn = (((0,), (0,)), ((), ()))
    for h in range(LANES // head_dim):
        hs = slice(h * head_dim, (h + 1) * head_dim)
        q = q_all[:, hs]
        g = g_all[:, hs]
        k = kv_ref[0, :, hs]
        v = kv_ref[1, :, hs]
        s = lax.dot_general(q, k, nt, preferred_element_type=jnp.float32) * scale
        s = jnp.where(ok, s, -jnp.inf)
        m = jnp.max(s, axis=-1, keepdims=True)
        e = jnp.exp(s - m)
        w = e / jnp.sum(e, axis=-1, keepdims=True)
        wb = w.astype(jnp.bfloat16)
        att_tmp[:, hs] = jnp.dot(wb, v, preferred_element_type=jnp.float32).astype(jnp.bfloat16)
        vd = lax.dot_general(g, v, nt, preferred_element_type=jnp.float32)
        rd = jnp.sum(w * vd, axis=-1, keepdims=True)
        sg = (w * (vd - rd) * scale).astype(jnp.bfloat16)
        qg_tmp[:, hs] = jnp.dot(sg, k, preferred_element_type=jnp.float32).astype(jnp.bfloat16)
        for c, term in enumerate((lax.dot_general(sg, q, tn, preferred_element_type=jnp.float32),
                                  lax.dot_general(wb, g, tn, preferred_element_type=jnp.float32))):
            near_ref[c, :, hs] = term[:near_rows]
            far_ref[c, :, hs] = term[near_rows:].astype(far_ref.dtype)
    att_ref[...] = jnp.dot(scatter, att_tmp[...], preferred_element_type=jnp.float32).astype(att_ref.dtype)
    qg_ref[...] = jnp.dot(scatter, qg_tmp[...], preferred_element_type=jnp.float32).astype(qg_ref.dtype)


def attention(order, queries, out_grad, kv_all, col_valid, head_dim, near_rows):
    rows, features = queries.shape
    cols = kv_all.shape[1]
    row_spec = pl.BlockSpec((rows, LANES), lambda i: (0, i))
    kv_spec = pl.BlockSpec((2, cols, LANES), lambda i: (0, 0, i))
    kernel = lambda *refs: attention_kernel(*refs, head_dim=head_dim, near_rows=near_rows)
    return pl.pallas_call(
        kernel,
        grid=(features // LANES,),
        in_specs=[
            pl.BlockSpec((rows, 1), lambda i: (0, 0)),
            pl.BlockSpec((1, rows), lambda i: (0, 0)),
            row_spec,
            row_spec,
            kv_spec,
            pl.BlockSpec((1, cols), lambda i: (0, 0)),
        ],
        out_specs=[
            row_spec,
            row_spec,
            pl.BlockSpec((2, near_rows, LANES), lambda i: (0, 0, i)),
            pl.BlockSpec((2, cols - near_rows, LANES), lambda i: (0, 0, i)),
        ],
        out_shape=[
            jax.ShapeDtypeStruct((rows, features), jnp.bfloat16),
            jax.ShapeDtypeStruct((rows, features), jnp.bfloat16),
            jax.ShapeDtypeStruct((2, near_rows, features), jnp.float32),
            jax.ShapeDtypeStruct((2, cols - near_rows, features), jnp.bfloat16),
        ],
        scratch_shapes=[pltpu.VMEM((rows, LANES), jnp.bfloat16), pltpu.VMEM((rows, LANES), jnp.bfloat16)],
    )(order.reshape(rows, 1), order.reshape(1, rows), queries, out_grad, kv_all, col_valid)


def xor_permute(value, distance, count):
    return lax.ppermute(value, AXES, [(i, i ^ distance) for i in range(count)])


def per_device(queries, key_table, value_table, out_grad, hilbert_order, key_valid):
    rows_dev, features = queries.shape
    head_dim = D // HEADS
    shard_count = lax.axis_size(AXES)
    shard_bits = shard_count.bit_length() - 1
    my_index = lax.axis_index(AXES)
    permute = hilbert_order[0]
    one_hot = (permute[:, None] == lax.broadcasted_iota(jnp.int32, (rows_dev, rows_dev), 1)).astype(
        jnp.bfloat16
    )

    def take(storage_rows):
        return jnp.dot(one_hot, storage_rows, preferred_element_type=jnp.float32).astype(jnp.bfloat16)

    table_rows = jnp.stack([take(key_table), take(value_table)])
    padded_valid = jnp.pad(key_valid, (BLOCK, BLOCK))
    edge_valid = lax.dynamic_slice_in_dim(padded_valid, my_index * rows_dev, rows_dev + 2 * BLOCK)
    own_valid_rows = edge_valid[BLOCK : BLOCK + rows_dev].astype(jnp.float32)
    own_valid = own_valid_rows[None, :, None]
    masked = table_rows.astype(jnp.float32) * own_valid

    up = [(i, i + 1) for i in range(shard_count - 1)]
    down = [(i + 1, i) for i in range(shard_count - 1)]
    before = lax.ppermute(table_rows[:, rows_dev - BLOCK :], AXES, up)
    after = lax.ppermute(table_rows[:, :BLOCK], AXES, down)

    low_bits = shard_bits // 2
    low_count = 2**low_bits
    high_bits = list(range(low_bits, shard_bits))
    pooled = []
    for bit in range(shard_bits):
        group = 2 ** (bit + 1)
        summed = jnp.sum(masked.reshape(2, rows_dev // group, group, features), axis=2) / group
        pooled.append(summed.astype(jnp.bfloat16))
    sizes = [p.shape[1] for p in pooled]

    far_chunks = []
    gathered = {bit: [pooled[bit]] for bit in high_bits}
    for low in range(1, low_count):
        bit = low.bit_length() - 1
        payload = jnp.concatenate([pooled[bit]] + [pooled[b] for b in high_bits], axis=1)
        received = xor_permute(payload, low, shard_count)
        far_chunks.append(received[:, : sizes[bit]])
        offset = sizes[bit]
        for b in high_bits:
            gathered[b].append(received[:, offset : offset + sizes[b]])
            offset += sizes[b]
    high_distances = [high << low_bits for high in range(1, 2 ** (shard_bits - low_bits))]
    stacked = {b: jnp.concatenate(gathered[b], axis=1) for b in high_bits}
    for distance in high_distances:
        bit = distance.bit_length() - 1
        far_chunks.append(xor_permute(stacked[bit], distance, shard_count))

    full = jnp.concatenate([before, table_rows, after] + far_chunks, axis=1)
    near_rows = rows_dev + 2 * BLOCK
    cols = full.shape[1]
    col_valid = jnp.concatenate(
        [edge_valid, jnp.ones((cols - near_rows,), edge_valid.dtype)]
    ).reshape(1, cols)
    attended, query_grad, terms, far_terms = attention(
        permute, queries, out_grad, full, col_valid, head_dim, near_rows
    )

    from_next = lax.ppermute(terms[:, :BLOCK], AXES, down)
    from_prev = lax.ppermute(terms[:, near_rows - BLOCK : near_rows], AXES, up)

    offset = 0
    direct_terms = []
    for low in range(1, low_count):
        size = sizes[low.bit_length() - 1]
        direct_terms.append(far_terms[:, offset : offset + size].astype(jnp.float32))
        offset += size
    stacked_sums = {}
    for distance in high_distances:
        bit = distance.bit_length() - 1
        size = low_count * sizes[bit]
        returned = xor_permute(
            far_terms[:, offset : offset + size], distance, shard_count
        ).astype(jnp.float32)
        offset += size
        stacked_sums[bit] = returned if bit not in stacked_sums else stacked_sums[bit] + returned
    level_sums = {b: stacked_sums[b][:, : sizes[b]] for b in high_bits}
    for low in range(1, low_count):
        bit = low.bit_length() - 1
        parts = [direct_terms[low - 1]] + [
            stacked_sums[b][:, low * sizes[b] : (low + 1) * sizes[b]] for b in high_bits
        ]
        received = xor_permute(jnp.concatenate(parts, axis=1), low, shard_count)
        level_sums[bit] = (
            received[:, : sizes[bit]] if bit not in level_sums else level_sums[bit] + received[:, : sizes[bit]]
        )
        offset = sizes[bit]
        for b in high_bits:
            level_sums[b] = level_sums[b] + received[:, offset : offset + sizes[b]]
            offset += sizes[b]
    spread = level_sums[shard_bits - 1] / 2**shard_bits
    for bit in reversed(range(shard_bits - 1)):
        spread = jnp.repeat(spread, 2, axis=1) + level_sums[bit] / 2 ** (bit + 1)
    spread = jnp.repeat(spread, 2, axis=1)
    edges = jnp.concatenate([from_prev, from_next], axis=1)
    row_grad = terms[:, BLOCK : BLOCK + rows_dev] + edges + own_valid * spread

    def restore(hilbert_rows):
        restored = lax.dot_general(
            one_hot, hilbert_rows, (((0,), (0,)), ((), ())), preferred_element_type=jnp.float32
        )
        return restored.astype(jnp.bfloat16)

    return (attended, query_grad, restore(row_grad[0].astype(jnp.bfloat16)), restore(row_grad[1].astype(jnp.bfloat16)))


def solution(mesh):
    in_specs = (
        P(("parts", "rows", "sub"), "head"),
        P(("parts", "rows", "sub"), "head"),
        P(("parts", "rows", "sub"), "head"),
        P(("parts", "rows", "sub"), "head"),
        P(("parts", "rows", "sub"), None),
        P("parts"),
    )
    out_specs = (
        P(("parts", "rows", "sub"), "head"),
        P(("parts", "rows", "sub"), "head"),
        P(("parts", "rows", "sub"), "head"),
        P(("parts", "rows", "sub"), "head"),
    )
    return jax.shard_map(
        per_device, mesh=mesh, in_specs=in_specs, out_specs=out_specs, check_vma=False
    )
```

```python
import math

import jax
import jax.numpy as jnp
from jax import lax
from jax.experimental import pallas as pl
from jax.experimental.pallas import tpu as pltpu
from jax.sharding import PartitionSpec as P

D = 512
HEADS = 8
BLOCK = 128
AXES = ("rows", "sub")
LANES = 128


def attention_kernel(
    order_col_ref, order_row_ref, q_ref, g_ref, kv_ref, cv_ref, att_ref, qg_ref, near_ref, far_ref, att_tmp, qg_tmp,
    *, head_dim, near_rows
):
    rows = q_ref.shape[0]
    cols = kv_ref.shape[1]
    scale = 1.0 / math.sqrt(head_dim)
    gather = (
        order_col_ref[...] == lax.broadcasted_iota(jnp.int32, (rows, rows), 1)
    ).astype(jnp.bfloat16)
    scatter = (
        order_row_ref[...] == lax.broadcasted_iota(jnp.int32, (rows, rows), 0)
    ).astype(jnp.bfloat16)
    q_all = jnp.dot(gather, q_ref[...], preferred_element_type=jnp.float32).astype(jnp.bfloat16)
    g_all = jnp.dot(gather, g_ref[...], preferred_element_type=jnp.float32).astype(jnp.bfloat16)
    row = lax.broadcasted_iota(jnp.int32, (rows, cols), 0)
    col = lax.broadcasted_iota(jnp.int32, (rows, cols), 1)
    start = (row // BLOCK) * BLOCK
    in_window = (col >= start) & (col < start + 3 * BLOCK)
    ok = (col >= near_rows) | (in_window & (cv_ref[...] > 0))
    nt = (((1,), (1,)), ((), ()))
    tn = (((0,), (0,)), ((), ()))
    for h in range(LANES // head_dim):
        hs = slice(h * head_dim, (h + 1) * head_dim)
        q = q_all[:, hs]
        g = g_all[:, hs]
        k = kv_ref[0, :, hs]
        v = kv_ref[1, :, hs]
        s = lax.dot_general(q, k, nt, preferred_element_type=jnp.float32) * scale
        s = jnp.where(ok, s, -jnp.inf)
        m = jnp.max(s, axis=-1, keepdims=True)
        e = jnp.exp(s - m)
        w = e / jnp.sum(e, axis=-1, keepdims=True)
        wb = w.astype(jnp.bfloat16)
        att_tmp[:, hs] = jnp.dot(wb, v, preferred_element_type=jnp.float32).astype(jnp.bfloat16)
        vd = lax.dot_general(g, v, nt, preferred_element_type=jnp.float32)
        rd = jnp.sum(w * vd, axis=-1, keepdims=True)
        sg = (w * (vd - rd) * scale).astype(jnp.bfloat16)
        qg_tmp[:, hs] = jnp.dot(sg, k, preferred_element_type=jnp.float32).astype(jnp.bfloat16)
        for c, term in enumerate((lax.dot_general(sg, q, tn, preferred_element_type=jnp.float32),
                                  lax.dot_general(wb, g, tn, preferred_element_type=jnp.float32))):
            near_ref[c, :, hs] = term[:near_rows]
            far_ref[c, :, hs] = term[near_rows:].astype(far_ref.dtype)
    att_ref[...] = jnp.dot(scatter, att_tmp[...], preferred_element_type=jnp.float32).astype(att_ref.dtype)
    qg_ref[...] = jnp.dot(scatter, qg_tmp[...], preferred_element_type=jnp.float32).astype(qg_ref.dtype)


def attention(order, queries, out_grad, kv_all, col_valid, head_dim, near_rows):
    rows, features = queries.shape
    cols = kv_all.shape[1]
    row_spec = pl.BlockSpec((rows, LANES), lambda i: (0, i))
    kv_spec = pl.BlockSpec((2, cols, LANES), lambda i: (0, 0, i))
    kernel = lambda *refs: attention_kernel(*refs, head_dim=head_dim, near_rows=near_rows)
    return pl.pallas_call(
        kernel,
        grid=(features // LANES,),
        in_specs=[
            pl.BlockSpec((rows, 1), lambda i: (0, 0)),
            pl.BlockSpec((1, rows), lambda i: (0, 0)),
            row_spec,
            row_spec,
            kv_spec,
            pl.BlockSpec((1, cols), lambda i: (0, 0)),
        ],
        out_specs=[
            row_spec,
            row_spec,
            pl.BlockSpec((2, near_rows, LANES), lambda i: (0, 0, i)),
            pl.BlockSpec((2, cols - near_rows, LANES), lambda i: (0, 0, i)),
        ],
        out_shape=[
            jax.ShapeDtypeStruct((rows, features), jnp.bfloat16),
            jax.ShapeDtypeStruct((rows, features), jnp.bfloat16),
            jax.ShapeDtypeStruct((2, near_rows, features), jnp.float32),
            jax.ShapeDtypeStruct((2, cols - near_rows, features), jnp.bfloat16),
        ],
        scratch_shapes=[pltpu.VMEM((rows, LANES), jnp.bfloat16), pltpu.VMEM((rows, LANES), jnp.bfloat16)],
    )(order.reshape(rows, 1), order.reshape(1, rows), queries, out_grad, kv_all, col_valid)


def xor_permute(value, distance, count):
    return lax.ppermute(value, AXES, [(i, i ^ distance) for i in range(count)])


def per_device(queries, key_table, value_table, out_grad, hilbert_order, key_valid):
    rows_dev, features = queries.shape
    head_dim = D // HEADS
    shard_count = lax.axis_size(AXES)
    shard_bits = shard_count.bit_length() - 1
    my_index = lax.axis_index(AXES)
    permute = hilbert_order[0]
    one_hot = (permute[:, None] == lax.broadcasted_iota(jnp.int32, (rows_dev, rows_dev), 1)).astype(
        jnp.bfloat16
    )

    def take(storage_rows):
        return jnp.dot(one_hot, storage_rows, preferred_element_type=jnp.float32).astype(jnp.bfloat16)

    table_rows = jnp.stack([take(key_table), take(value_table)])
    padded_valid = jnp.pad(key_valid, (BLOCK, BLOCK))
    edge_valid = lax.dynamic_slice_in_dim(padded_valid, my_index * rows_dev, rows_dev + 2 * BLOCK)
    own_valid_rows = edge_valid[BLOCK : BLOCK + rows_dev].astype(jnp.float32)
    own_valid = own_valid_rows[None, :, None]
    masked = table_rows.astype(jnp.float32) * own_valid

    up = [(i, i + 1) for i in range(shard_count - 1)]
    down = [(i + 1, i) for i in range(shard_count - 1)]
    before = lax.ppermute(table_rows[:, rows_dev - BLOCK :], AXES, up)
    after = lax.ppermute(table_rows[:, :BLOCK], AXES, down)

    low_bits = shard_bits // 2
    low_count = 2**low_bits
    high_bits = list(range(low_bits, shard_bits))
    pooled = []
    for bit in range(shard_bits):
        group = 2 ** (bit + 1)
        summed = jnp.sum(masked.reshape(2, rows_dev // group, group, features), axis=2) / group
        pooled.append(summed.astype(jnp.bfloat16))
    sizes = [p.shape[1] for p in pooled]

    far_chunks = []
    gathered = {bit: [pooled[bit]] for bit in high_bits}
    for low in range(1, low_count):
        bit = low.bit_length() - 1
        payload = jnp.concatenate([pooled[bit]] + [pooled[b] for b in high_bits], axis=1)
        received = xor_permute(payload, low, shard_count)
        far_chunks.append(received[:, : sizes[bit]])
        offset = sizes[bit]
        for b in high_bits:
            gathered[b].append(received[:, offset : offset + sizes[b]])
            offset += sizes[b]
    high_distances = [high << low_bits for high in range(1, 2 ** (shard_bits - low_bits))]
    stacked = {b: jnp.concatenate(gathered[b], axis=1) for b in high_bits}
    for distance in high_distances:
        bit = distance.bit_length() - 1
        far_chunks.append(xor_permute(stacked[bit], distance, shard_count))

    full = jnp.concatenate([before, table_rows, after] + far_chunks, axis=1)
    near_rows = rows_dev + 2 * BLOCK
    cols = full.shape[1]
    col_valid = jnp.concatenate(
        [edge_valid, jnp.ones((cols - near_rows,), edge_valid.dtype)]
    ).reshape(1, cols)
    attended, query_grad, terms, far_terms = attention(
        permute, queries, out_grad, full, col_valid, head_dim, near_rows
    )

    from_next = lax.ppermute(terms[:, :BLOCK].astype(jnp.bfloat16), AXES, down).astype(jnp.float32)
    from_prev = lax.ppermute(
        terms[:, near_rows - BLOCK : near_rows].astype(jnp.bfloat16), AXES, up
    ).astype(jnp.float32)

    offset = 0
    direct_terms = []
    for low in range(1, low_count):
        size = sizes[low.bit_length() - 1]
        direct_terms.append(far_terms[:, offset : offset + size])
        offset += size
    stacked_sums = {}
    for distance in high_distances:
        bit = distance.bit_length() - 1
        size = low_count * sizes[bit]
        returned = xor_permute(
            far_terms[:, offset : offset + size], distance, shard_count
        ).astype(jnp.float32)
        offset += size
        stacked_sums[bit] = returned if bit not in stacked_sums else stacked_sums[bit] + returned
    level_sums = {b: stacked_sums[b][:, : sizes[b]] for b in high_bits}
    for low in range(1, low_count):
        bit = low.bit_length() - 1
        parts = [direct_terms[low - 1]] + [
            stacked_sums[b][:, low * sizes[b] : (low + 1) * sizes[b]] for b in high_bits
        ]
        received = xor_permute(
            jnp.concatenate(parts, axis=1).astype(jnp.bfloat16), low, shard_count
        ).astype(jnp.float32)
        level_sums[bit] = (
            received[:, : sizes[bit]] if bit not in level_sums else level_sums[bit] + received[:, : sizes[bit]]
        )
        offset = sizes[bit]
        for b in high_bits:
            level_sums[b] = level_sums[b] + received[:, offset : offset + sizes[b]]
            offset += sizes[b]
    spread = level_sums[shard_bits - 1] / 2**shard_bits
    for bit in reversed(range(shard_bits - 1)):
        spread = jnp.repeat(spread, 2, axis=1) + level_sums[bit] / 2 ** (bit + 1)
    spread = jnp.repeat(spread, 2, axis=1)
    edges = jnp.concatenate([from_prev, from_next], axis=1)
    row_grad = terms[:, BLOCK : BLOCK + rows_dev] + edges + own_valid * spread

    def restore(hilbert_rows):
        restored = lax.dot_general(
            one_hot, hilbert_rows, (((0,), (0,)), ((), ())), preferred_element_type=jnp.float32
        )
        return restored.astype(jnp.bfloat16)

    return (attended, query_grad, restore(row_grad[0].astype(jnp.bfloat16)), restore(row_grad[1].astype(jnp.bfloat16)))


def solution(mesh):
    in_specs = (
        P(("parts", "rows", "sub"), "head"),
        P(("parts", "rows", "sub"), "head"),
        P(("parts", "rows", "sub"), "head"),
        P(("parts", "rows", "sub"), "head"),
        P(("parts", "rows", "sub"), None),
        P("parts"),
    )
    out_specs = (
        P(("parts", "rows", "sub"), "head"),
        P(("parts", "rows", "sub"), "head"),
        P(("parts", "rows", "sub"), "head"),
        P(("parts", "rows", "sub"), "head"),
    )
    return jax.shard_map(
        per_device, mesh=mesh, in_specs=in_specs, out_specs=out_specs, check_vma=False
    )
```

```python
import math

import numpy as np

import jax
import jax.numpy as jnp
from jax import lax
from jax.experimental import pallas as pl
from jax.experimental.pallas import tpu as pltpu
from jax.sharding import PartitionSpec as P

D = 512
HEADS = 8
BLOCK = 128
AXES = ("rows", "sub")
LANES = 128


def attention_kernel(
    order_col_ref, order_row_ref, q_ref, g_ref, kv_ref, cv_ref, att_ref, qg_ref, near_ref, far_ref, att_tmp, qg_tmp,
    *, head_dim, near_rows
):
    rows = q_ref.shape[0]
    cols = kv_ref.shape[1]
    scale = 1.0 / math.sqrt(head_dim)
    gather = (
        order_col_ref[...] == lax.broadcasted_iota(jnp.int32, (rows, rows), 1)
    ).astype(jnp.bfloat16)
    scatter = (
        order_row_ref[...] == lax.broadcasted_iota(jnp.int32, (rows, rows), 0)
    ).astype(jnp.bfloat16)
    q_all = jnp.dot(gather, q_ref[...], preferred_element_type=jnp.float32).astype(jnp.bfloat16)
    g_all = jnp.dot(gather, g_ref[...], preferred_element_type=jnp.float32).astype(jnp.bfloat16)
    row = lax.broadcasted_iota(jnp.int32, (rows, cols), 0)
    col = lax.broadcasted_iota(jnp.int32, (rows, cols), 1)
    start = (row // BLOCK) * BLOCK
    in_window = (col >= start) & (col < start + 3 * BLOCK)
    ok = (col >= near_rows) | (in_window & (cv_ref[...] > 0))
    nt = (((1,), (1,)), ((), ()))
    tn = (((0,), (0,)), ((), ()))
    for h in range(LANES // head_dim):
        hs = slice(h * head_dim, (h + 1) * head_dim)
        q = q_all[:, hs]
        g = g_all[:, hs]
        k = kv_ref[0, :, hs]
        v = kv_ref[1, :, hs]
        s = lax.dot_general(q, k, nt, preferred_element_type=jnp.float32) * scale
        s = jnp.where(ok, s, -jnp.inf)
        m = jnp.max(s, axis=-1, keepdims=True)
        e = jnp.exp(s - m)
        w = e / jnp.sum(e, axis=-1, keepdims=True)
        wb = w.astype(jnp.bfloat16)
        att_tmp[:, hs] = jnp.dot(wb, v, preferred_element_type=jnp.float32).astype(jnp.bfloat16)
        vd = lax.dot_general(g, v, nt, preferred_element_type=jnp.float32)
        rd = jnp.sum(w * vd, axis=-1, keepdims=True)
        sg = (w * (vd - rd) * scale).astype(jnp.bfloat16)
        qg_tmp[:, hs] = jnp.dot(sg, k, preferred_element_type=jnp.float32).astype(jnp.bfloat16)
        for c, term in enumerate((lax.dot_general(sg, q, tn, preferred_element_type=jnp.float32),
                                  lax.dot_general(wb, g, tn, preferred_element_type=jnp.float32))):
            near_ref[c, :, hs] = term[:near_rows]
            far_ref[c, :, hs] = term[near_rows:].astype(far_ref.dtype)
    att_ref[...] = jnp.dot(scatter, att_tmp[...], preferred_element_type=jnp.float32).astype(att_ref.dtype)
    qg_ref[...] = jnp.dot(scatter, qg_tmp[...], preferred_element_type=jnp.float32).astype(qg_ref.dtype)


def attention(order, queries, out_grad, kv_all, col_valid, head_dim, near_rows):
    rows, features = queries.shape
    cols = kv_all.shape[1]
    row_spec = pl.BlockSpec((rows, LANES), lambda i: (0, i))
    kv_spec = pl.BlockSpec((2, cols, LANES), lambda i: (0, 0, i))
    kernel = lambda *refs: attention_kernel(*refs, head_dim=head_dim, near_rows=near_rows)
    return pl.pallas_call(
        kernel,
        grid=(features // LANES,),
        in_specs=[
            pl.BlockSpec((rows, 1), lambda i: (0, 0)),
            pl.BlockSpec((1, rows), lambda i: (0, 0)),
            row_spec,
            row_spec,
            kv_spec,
            pl.BlockSpec((1, cols), lambda i: (0, 0)),
        ],
        out_specs=[
            row_spec,
            row_spec,
            pl.BlockSpec((2, near_rows, LANES), lambda i: (0, 0, i)),
            pl.BlockSpec((2, cols - near_rows, LANES), lambda i: (0, 0, i)),
        ],
        out_shape=[
            jax.ShapeDtypeStruct((rows, features), jnp.bfloat16),
            jax.ShapeDtypeStruct((rows, features), jnp.bfloat16),
            jax.ShapeDtypeStruct((2, near_rows, features), jnp.float32),
            jax.ShapeDtypeStruct((2, cols - near_rows, features), jnp.bfloat16),
        ],
        scratch_shapes=[pltpu.VMEM((rows, LANES), jnp.bfloat16), pltpu.VMEM((rows, LANES), jnp.bfloat16)],
    )(order.reshape(rows, 1), order.reshape(1, rows), queries, out_grad, kv_all, col_valid)


def xor_permute(value, distance, count):
    return lax.ppermute(value, AXES, [(i, i ^ distance) for i in range(count)])


def per_device(queries, key_table, value_table, out_grad, hilbert_order, key_valid):
    rows_dev, features = queries.shape
    head_dim = D // HEADS
    shard_count = lax.axis_size(AXES)
    shard_bits = shard_count.bit_length() - 1
    my_index = lax.axis_index(AXES)
    permute = hilbert_order[0]
    one_hot = (permute[:, None] == lax.broadcasted_iota(jnp.int32, (rows_dev, rows_dev), 1)).astype(
        jnp.bfloat16
    )

    def take(storage_rows):
        return jnp.dot(one_hot, storage_rows, preferred_element_type=jnp.float32).astype(jnp.bfloat16)

    table_rows = jnp.stack([take(key_table), take(value_table)])
    padded_valid = jnp.pad(key_valid, (BLOCK, BLOCK))
    edge_valid = lax.dynamic_slice_in_dim(padded_valid, my_index * rows_dev, rows_dev + 2 * BLOCK)
    own_valid_rows = edge_valid[BLOCK : BLOCK + rows_dev].astype(jnp.float32)
    own_valid = own_valid_rows[None, :, None]
    masked = table_rows.astype(jnp.float32) * own_valid

    up = [(i, i + 1) for i in range(shard_count - 1)]
    down = [(i + 1, i) for i in range(shard_count - 1)]
    before = lax.ppermute(table_rows[:, rows_dev - BLOCK :], AXES, up)
    after = lax.ppermute(table_rows[:, :BLOCK], AXES, down)

    low_bits = shard_bits // 2
    low_count = 2**low_bits
    high_bits = list(range(low_bits, shard_bits))
    pooled = []
    for bit in range(shard_bits):
        group = 2 ** (bit + 1)
        summed = jnp.sum(masked.reshape(2, rows_dev // group, group, features), axis=2) / group
        pooled.append(summed.astype(jnp.bfloat16))
    sizes = [p.shape[1] for p in pooled]

    far_chunks = []
    gathered = {bit: [pooled[bit]] for bit in high_bits}
    for low in range(1, low_count):
        bit = low.bit_length() - 1
        payload = jnp.concatenate([pooled[bit]] + [pooled[b] for b in high_bits], axis=1)
        received = xor_permute(payload, low, shard_count)
        far_chunks.append(received[:, : sizes[bit]])
        offset = sizes[bit]
        for b in high_bits:
            gathered[b].append(received[:, offset : offset + sizes[b]])
            offset += sizes[b]
    high_distances = [high << low_bits for high in range(1, 2 ** (shard_bits - low_bits))]
    stacked = {b: jnp.concatenate(gathered[b], axis=1) for b in high_bits}
    for distance in high_distances:
        bit = distance.bit_length() - 1
        far_chunks.append(xor_permute(stacked[bit], distance, shard_count))

    full = jnp.concatenate([before, table_rows, after] + far_chunks, axis=1)
    near_rows = rows_dev + 2 * BLOCK
    cols = full.shape[1]
    col_valid = jnp.concatenate(
        [edge_valid, jnp.ones((cols - near_rows,), edge_valid.dtype)]
    ).reshape(1, cols)
    attended, query_grad, terms, far_terms = attention(
        permute, queries, out_grad, full, col_valid, head_dim, near_rows
    )

    from_next = lax.ppermute(terms[:, :BLOCK].astype(jnp.bfloat16), AXES, down).astype(jnp.float32)
    from_prev = lax.ppermute(
        terms[:, near_rows - BLOCK : near_rows].astype(jnp.bfloat16), AXES, up
    ).astype(jnp.float32)

    offset = 0
    direct_terms = []
    for low in range(1, low_count):
        size = sizes[low.bit_length() - 1]
        direct_terms.append(far_terms[:, offset : offset + size])
        offset += size
    stacked_sums = {}
    pieces = []
    segments = []
    for distance in high_distances:
        bit = distance.bit_length() - 1
        size = low_count * sizes[bit]
        returned = xor_permute(far_terms[:, offset : offset + size], distance, shard_count)
        offset += size
        pieces.append(returned[:, : sizes[bit]])
        segments.append(bit)
        returned = returned.astype(jnp.float32)
        stacked_sums[bit] = returned if bit not in stacked_sums else stacked_sums[bit] + returned
    for low in range(1, low_count):
        bit = low.bit_length() - 1
        parts = [direct_terms[low - 1]] + [
            stacked_sums[b][:, low * sizes[b] : (low + 1) * sizes[b]].astype(jnp.bfloat16) for b in high_bits
        ]
        pieces.append(xor_permute(jnp.concatenate(parts, axis=1), low, shard_count))
        segments.extend([bit] + high_bits)
    expand = np.zeros((rows_dev, sum(sizes[b] for b in segments)), np.float32)
    column = 0
    for bit in segments:
        group = 2 ** (bit + 1)
        for j in range(sizes[bit]):
            expand[j * group : (j + 1) * group, column + j] = 1.0 / group
        column += sizes[bit]
    expand = jnp.asarray(expand, dtype=jnp.bfloat16)
    spread = jnp.stack(
        [
            jnp.dot(expand, jnp.concatenate([piece[c] for piece in pieces], axis=0), preferred_element_type=jnp.float32)
            for c in range(2)
        ]
    )
    edges = jnp.concatenate([from_prev, from_next], axis=1)
    row_grad = terms[:, BLOCK : BLOCK + rows_dev] + edges + own_valid * spread

    def restore(hilbert_rows):
        restored = lax.dot_general(
            one_hot, hilbert_rows, (((0,), (0,)), ((), ())), preferred_element_type=jnp.float32
        )
        return restored.astype(jnp.bfloat16)

    return (attended, query_grad, restore(row_grad[0].astype(jnp.bfloat16)), restore(row_grad[1].astype(jnp.bfloat16)))


def solution(mesh):
    in_specs = (
        P(("parts", "rows", "sub"), "head"),
        P(("parts", "rows", "sub"), "head"),
        P(("parts", "rows", "sub"), "head"),
        P(("parts", "rows", "sub"), "head"),
        P(("parts", "rows", "sub"), None),
        P("parts"),
    )
    out_specs = (
        P(("parts", "rows", "sub"), "head"),
        P(("parts", "rows", "sub"), "head"),
        P(("parts", "rows", "sub"), "head"),
        P(("parts", "rows", "sub"), "head"),
    )
    return jax.shard_map(
        per_device, mesh=mesh, in_specs=in_specs, out_specs=out_specs, check_vma=False
    )
```

```python
import math

import numpy as np

import jax
import jax.numpy as jnp
from jax import lax
from jax.experimental import pallas as pl
from jax.experimental.pallas import tpu as pltpu
from jax.sharding import PartitionSpec as P

D = 512
HEADS = 8
BLOCK = 128
AXES = ("rows", "sub")
LANES = 128


def attention_kernel(
    order_col_ref, order_row_ref, q_ref, g_ref, kv_ref, cv_ref, att_ref, qg_ref, near_ref, far_ref,
    att_tmp, qg_tmp, far_acc, *, head_dim, near_rows
):
    rows = q_ref.shape[0]
    scale = 1.0 / math.sqrt(head_dim)
    gather = (
        order_col_ref[...] == lax.broadcasted_iota(jnp.int32, (rows, rows), 1)
    ).astype(jnp.bfloat16)
    scatter = (
        order_row_ref[...] == lax.broadcasted_iota(jnp.int32, (rows, rows), 0)
    ).astype(jnp.bfloat16)
    q_all = jnp.dot(gather, q_ref[...], preferred_element_type=jnp.float32).astype(jnp.bfloat16)
    g_all = jnp.dot(gather, g_ref[...], preferred_element_type=jnp.float32).astype(jnp.bfloat16)
    near_ref[...] = jnp.zeros(near_ref.shape, near_ref.dtype)
    far_acc[...] = jnp.zeros(far_acc.shape, far_acc.dtype)
    nt = (((1,), (1,)), ((), ()))
    tn = (((0,), (0,)), ((), ()))
    width = 3 * BLOCK

    def mm(a, b, dims=None):
        if dims is None:
            return jnp.dot(a, b, preferred_element_type=jnp.float32)
        return lax.dot_general(a, b, dims, preferred_element_type=jnp.float32)

    for block in range(rows // BLOCK):
        r0 = block * BLOCK
        near_ok = cv_ref[:, r0 : r0 + width] > 0
        for h in range(LANES // head_dim):
            hs = slice(h * head_dim, (h + 1) * head_dim)
            q = q_all[r0 : r0 + BLOCK, hs]
            g = g_all[r0 : r0 + BLOCK, hs]
            kn = kv_ref[0, r0 : r0 + width, hs]
            vn = kv_ref[1, r0 : r0 + width, hs]
            kf = kv_ref[0, near_rows:, hs]
            vf = kv_ref[1, near_rows:, hs]
            sn = jnp.where(near_ok, mm(q, kn, nt) * scale, -jnp.inf)
            sf = mm(q, kf, nt) * scale
            m = jnp.maximum(jnp.max(sn, axis=-1, keepdims=True), jnp.max(sf, axis=-1, keepdims=True))
            en = jnp.exp(sn - m)
            ef = jnp.exp(sf - m)
            den = jnp.sum(en, axis=-1, keepdims=True) + jnp.sum(ef, axis=-1, keepdims=True)
            wn = en / den
            wf = ef / den
            wbn = wn.astype(jnp.bfloat16)
            wbf = wf.astype(jnp.bfloat16)
            att_tmp[r0 : r0 + BLOCK, hs] = (mm(wbn, vn) + mm(wbf, vf)).astype(jnp.bfloat16)
            vdn = mm(g, vn, nt)
            vdf = mm(g, vf, nt)
            rd = jnp.sum(wn * vdn, axis=-1, keepdims=True) + jnp.sum(wf * vdf, axis=-1, keepdims=True)
            sgn = (wn * (vdn - rd) * scale).astype(jnp.bfloat16)
            sgf = (wf * (vdf - rd) * scale).astype(jnp.bfloat16)
            qg_tmp[r0 : r0 + BLOCK, hs] = (mm(sgn, kn) + mm(sgf, kf)).astype(jnp.bfloat16)
            near_ref[0, r0 : r0 + width, hs] += mm(sgn, q, tn)
            near_ref[1, r0 : r0 + width, hs] += mm(wbn, g, tn)
            far_acc[0, :, hs] += mm(sgf, q, tn)
            far_acc[1, :, hs] += mm(wbf, g, tn)
    far_ref[...] = far_acc[...].astype(far_ref.dtype)
    att_ref[...] = jnp.dot(scatter, att_tmp[...], preferred_element_type=jnp.float32).astype(att_ref.dtype)
    qg_ref[...] = jnp.dot(scatter, qg_tmp[...], preferred_element_type=jnp.float32).astype(qg_ref.dtype)


def attention(order, queries, out_grad, kv_all, col_valid, head_dim, near_rows):
    rows, features = queries.shape
    cols = kv_all.shape[1]
    row_spec = pl.BlockSpec((rows, LANES), lambda i: (0, i))
    kv_spec = pl.BlockSpec((2, cols, LANES), lambda i: (0, 0, i))
    kernel = lambda *refs: attention_kernel(*refs, head_dim=head_dim, near_rows=near_rows)
    return pl.pallas_call(
        kernel,
        grid=(features // LANES,),
        in_specs=[
            pl.BlockSpec((rows, 1), lambda i: (0, 0)),
            pl.BlockSpec((1, rows), lambda i: (0, 0)),
            row_spec,
            row_spec,
            kv_spec,
            pl.BlockSpec((1, cols), lambda i: (0, 0)),
        ],
        out_specs=[
            row_spec,
            row_spec,
            pl.BlockSpec((2, near_rows, LANES), lambda i: (0, 0, i)),
            pl.BlockSpec((2, cols - near_rows, LANES), lambda i: (0, 0, i)),
        ],
        out_shape=[
            jax.ShapeDtypeStruct((rows, features), jnp.bfloat16),
            jax.ShapeDtypeStruct((rows, features), jnp.bfloat16),
            jax.ShapeDtypeStruct((2, near_rows, features), jnp.float32),
            jax.ShapeDtypeStruct((2, cols - near_rows, features), jnp.bfloat16),
        ],
        scratch_shapes=[
            pltpu.VMEM((rows, LANES), jnp.bfloat16),
            pltpu.VMEM((rows, LANES), jnp.bfloat16),
            pltpu.VMEM((2, cols - near_rows, LANES), jnp.float32),
        ],
    )(order.reshape(rows, 1), order.reshape(1, rows), queries, out_grad, kv_all, col_valid)


def xor_permute(value, distance, count):
    return lax.ppermute(value, AXES, [(i, i ^ distance) for i in range(count)])


def per_device(queries, key_table, value_table, out_grad, hilbert_order, key_valid):
    rows_dev, features = queries.shape
    head_dim = D // HEADS
    shard_count = lax.axis_size(AXES)
    shard_bits = shard_count.bit_length() - 1
    my_index = lax.axis_index(AXES)
    permute = hilbert_order[0]
    one_hot = (permute[:, None] == lax.broadcasted_iota(jnp.int32, (rows_dev, rows_dev), 1)).astype(
        jnp.bfloat16
    )

    def take(storage_rows):
        return jnp.dot(one_hot, storage_rows, preferred_element_type=jnp.float32).astype(jnp.bfloat16)

    table_rows = jnp.stack([take(key_table), take(value_table)])
    padded_valid = jnp.pad(key_valid, (BLOCK, BLOCK))
    edge_valid = lax.dynamic_slice_in_dim(padded_valid, my_index * rows_dev, rows_dev + 2 * BLOCK)
    own_valid_rows = edge_valid[BLOCK : BLOCK + rows_dev].astype(jnp.float32)
    own_valid = own_valid_rows[None, :, None]
    masked = table_rows.astype(jnp.float32) * own_valid

    up = [(i, i + 1) for i in range(shard_count - 1)]
    down = [(i + 1, i) for i in range(shard_count - 1)]
    before = lax.ppermute(table_rows[:, rows_dev - BLOCK :], AXES, up)
    after = lax.ppermute(table_rows[:, :BLOCK], AXES, down)

    low_bits = shard_bits // 2
    low_count = 2**low_bits
    high_bits = list(range(low_bits, shard_bits))
    pooled = []
    for bit in range(shard_bits):
        group = 2 ** (bit + 1)
        summed = jnp.sum(masked.reshape(2, rows_dev // group, group, features), axis=2) / group
        pooled.append(summed.astype(jnp.bfloat16))
    sizes = [p.shape[1] for p in pooled]

    far_chunks = []
    gathered = {bit: [pooled[bit]] for bit in high_bits}
    for low in range(1, low_count):
        bit = low.bit_length() - 1
        payload = jnp.concatenate([pooled[bit]] + [pooled[b] for b in high_bits], axis=1)
        received = xor_permute(payload, low, shard_count)
        far_chunks.append(received[:, : sizes[bit]])
        offset = sizes[bit]
        for b in high_bits:
            gathered[b].append(received[:, offset : offset + sizes[b]])
            offset += sizes[b]
    high_distances = [high << low_bits for high in range(1, 2 ** (shard_bits - low_bits))]
    stacked = {b: jnp.concatenate(gathered[b], axis=1) for b in high_bits}
    for distance in high_distances:
        bit = distance.bit_length() - 1
        far_chunks.append(xor_permute(stacked[bit], distance, shard_count))

    full = jnp.concatenate([before, table_rows, after] + far_chunks, axis=1)
    near_rows = rows_dev + 2 * BLOCK
    cols = full.shape[1]
    col_valid = jnp.concatenate(
        [edge_valid, jnp.ones((cols - near_rows,), edge_valid.dtype)]
    ).reshape(1, cols)
    attended, query_grad, terms, far_terms = attention(
        permute, queries, out_grad, full, col_valid, head_dim, near_rows
    )

    from_next = lax.ppermute(terms[:, :BLOCK].astype(jnp.bfloat16), AXES, down).astype(jnp.float32)
    from_prev = lax.ppermute(
        terms[:, near_rows - BLOCK : near_rows].astype(jnp.bfloat16), AXES, up
    ).astype(jnp.float32)

    offset = 0
    direct_terms = []
    for low in range(1, low_count):
        size = sizes[low.bit_length() - 1]
        direct_terms.append(far_terms[:, offset : offset + size])
        offset += size
    stacked_sums = {}
    pieces = []
    segments = []
    for distance in high_distances:
        bit = distance.bit_length() - 1
        size = low_count * sizes[bit]
        returned = xor_permute(far_terms[:, offset : offset + size], distance, shard_count)
        offset += size
        pieces.append(returned[:, : sizes[bit]])
        segments.append(bit)
        returned = returned.astype(jnp.float32)
        stacked_sums[bit] = returned if bit not in stacked_sums else stacked_sums[bit] + returned
    for low in range(1, low_count):
        bit = low.bit_length() - 1
        parts = [direct_terms[low - 1]] + [
            stacked_sums[b][:, low * sizes[b] : (low + 1) * sizes[b]].astype(jnp.bfloat16) for b in high_bits
        ]
        pieces.append(xor_permute(jnp.concatenate(parts, axis=1), low, shard_count))
        segments.extend([bit] + high_bits)
    expand = np.zeros((rows_dev, sum(sizes[b] for b in segments)), np.float32)
    column = 0
    for bit in segments:
        group = 2 ** (bit + 1)
        for j in range(sizes[bit]):
            expand[j * group : (j + 1) * group, column + j] = 1.0 / group
        column += sizes[bit]
    expand = jnp.asarray(expand, dtype=jnp.bfloat16)
    spread = jnp.stack(
        [
            jnp.dot(expand, jnp.concatenate([piece[c] for piece in pieces], axis=0), preferred_element_type=jnp.float32)
            for c in range(2)
        ]
    )
    edges = jnp.concatenate([from_prev, from_next], axis=1)
    row_grad = terms[:, BLOCK : BLOCK + rows_dev] + edges + own_valid * spread

    def restore(hilbert_rows):
        restored = lax.dot_general(
            one_hot, hilbert_rows, (((0,), (0,)), ((), ())), preferred_element_type=jnp.float32
        )
        return restored.astype(jnp.bfloat16)

    return (attended, query_grad, restore(row_grad[0].astype(jnp.bfloat16)), restore(row_grad[1].astype(jnp.bfloat16)))


def solution(mesh):
    in_specs = (
        P(("parts", "rows", "sub"), "head"),
        P(("parts", "rows", "sub"), "head"),
        P(("parts", "rows", "sub"), "head"),
        P(("parts", "rows", "sub"), "head"),
        P(("parts", "rows", "sub"), None),
        P("parts"),
    )
    out_specs = (
        P(("parts", "rows", "sub"), "head"),
        P(("parts", "rows", "sub"), "head"),
        P(("parts", "rows", "sub"), "head"),
        P(("parts", "rows", "sub"), "head"),
    )
    return jax.shard_map(
        per_device, mesh=mesh, in_specs=in_specs, out_specs=out_specs, check_vma=False
    )
```

```python
import math

import numpy as np

import jax
import jax.numpy as jnp
from jax import lax
from jax.experimental import pallas as pl
from jax.experimental.pallas import tpu as pltpu
from jax.sharding import PartitionSpec as P

D = 512
HEADS = 8
BLOCK = 128
AXES = ("rows", "sub")
LANES = 128


def attention_kernel(
    order_col_ref, order_row_ref, q_ref, g_ref, kv_ref, cv_ref, att_ref, qg_ref, near_ref, far_ref,
    *, head_dim, near_rows
):
    rows = q_ref.shape[0]
    cols = kv_ref.shape[1]
    scale = 1.0 / math.sqrt(head_dim)
    gather = (
        order_col_ref[...] == lax.broadcasted_iota(jnp.int32, (rows, rows), 1)
    ).astype(jnp.bfloat16)
    scatter = (
        order_row_ref[...] == lax.broadcasted_iota(jnp.int32, (rows, rows), 0)
    ).astype(jnp.bfloat16)
    q_all = jnp.dot(gather, q_ref[...], preferred_element_type=jnp.float32).astype(jnp.bfloat16)
    g_all = jnp.dot(gather, g_ref[...], preferred_element_type=jnp.float32).astype(jnp.bfloat16)
    row = lax.broadcasted_iota(jnp.int32, (rows, cols), 0)
    col = lax.broadcasted_iota(jnp.int32, (rows, cols), 1)
    start = (row // BLOCK) * BLOCK
    in_window = (col >= start) & (col < start + 3 * BLOCK)
    ok = (col >= near_rows) | (in_window & (cv_ref[...] > 0))
    nt = (((1,), (1,)), ((), ()))
    tn = (((0,), (0,)), ((), ()))
    lane = lax.broadcasted_iota(jnp.int32, (1, LANES), 1)
    k = kv_ref[0]
    v = kv_ref[1]
    att = qg = key_term = value_term = None
    for h in range(LANES // head_dim):
        sel = (lane >= h * head_dim) & (lane < (h + 1) * head_dim)
        q = jnp.where(sel, q_all, jnp.zeros_like(q_all))
        g = jnp.where(sel, g_all, jnp.zeros_like(g_all))
        s = lax.dot_general(q, k, nt, preferred_element_type=jnp.float32) * scale
        s = jnp.where(ok, s, -jnp.inf)
        m = jnp.max(s, axis=-1, keepdims=True)
        e = jnp.exp(s - m)
        w = e / jnp.sum(e, axis=-1, keepdims=True)
        wb = w.astype(jnp.bfloat16)
        vd = lax.dot_general(g, v, nt, preferred_element_type=jnp.float32)
        rd = jnp.sum(w * vd, axis=-1, keepdims=True)
        sg = (w * (vd - rd) * scale).astype(jnp.bfloat16)
        outs = (
            jnp.dot(wb, v, preferred_element_type=jnp.float32),
            jnp.dot(sg, k, preferred_element_type=jnp.float32),
            lax.dot_general(sg, q_all, tn, preferred_element_type=jnp.float32),
            lax.dot_general(wb, g_all, tn, preferred_element_type=jnp.float32),
        )
        if att is None:
            att, qg, key_term, value_term = outs
        else:
            att, qg, key_term, value_term = (
                jnp.where(sel, new, old) for new, old in zip(outs, (att, qg, key_term, value_term))
            )
    for c, term in enumerate((key_term, value_term)):
        near_ref[c] = term[:near_rows]
        far_ref[c] = term[near_rows:].astype(far_ref.dtype)
    att_ref[...] = jnp.dot(
        scatter, att.astype(jnp.bfloat16), preferred_element_type=jnp.float32
    ).astype(att_ref.dtype)
    qg_ref[...] = jnp.dot(
        scatter, qg.astype(jnp.bfloat16), preferred_element_type=jnp.float32
    ).astype(qg_ref.dtype)


def attention(order, queries, out_grad, kv_all, col_valid, head_dim, near_rows):
    rows, features = queries.shape
    cols = kv_all.shape[1]
    row_spec = pl.BlockSpec((rows, LANES), lambda i: (0, i))
    kv_spec = pl.BlockSpec((2, cols, LANES), lambda i: (0, 0, i))
    kernel = lambda *refs: attention_kernel(*refs, head_dim=head_dim, near_rows=near_rows)
    return pl.pallas_call(
        kernel,
        grid=(features // LANES,),
        in_specs=[
            pl.BlockSpec((rows, 1), lambda i: (0, 0)),
            pl.BlockSpec((1, rows), lambda i: (0, 0)),
            row_spec,
            row_spec,
            kv_spec,
            pl.BlockSpec((1, cols), lambda i: (0, 0)),
        ],
        out_specs=[
            row_spec,
            row_spec,
            pl.BlockSpec((2, near_rows, LANES), lambda i: (0, 0, i)),
            pl.BlockSpec((2, cols - near_rows, LANES), lambda i: (0, 0, i)),
        ],
        out_shape=[
            jax.ShapeDtypeStruct((rows, features), jnp.bfloat16),
            jax.ShapeDtypeStruct((rows, features), jnp.bfloat16),
            jax.ShapeDtypeStruct((2, near_rows, features), jnp.float32),
            jax.ShapeDtypeStruct((2, cols - near_rows, features), jnp.bfloat16),
        ],
    )(order.reshape(rows, 1), order.reshape(1, rows), queries, out_grad, kv_all, col_valid)


def xor_permute(value, distance, count):
    return lax.ppermute(value, AXES, [(i, i ^ distance) for i in range(count)])


def per_device(queries, key_table, value_table, out_grad, hilbert_order, key_valid):
    rows_dev, features = queries.shape
    head_dim = D // HEADS
    shard_count = lax.axis_size(AXES)
    shard_bits = shard_count.bit_length() - 1
    my_index = lax.axis_index(AXES)
    permute = hilbert_order[0]
    one_hot = (permute[:, None] == lax.broadcasted_iota(jnp.int32, (rows_dev, rows_dev), 1)).astype(
        jnp.bfloat16
    )

    def take(storage_rows):
        return jnp.dot(one_hot, storage_rows, preferred_element_type=jnp.float32).astype(jnp.bfloat16)

    table_rows = jnp.stack([take(key_table), take(value_table)])
    padded_valid = jnp.pad(key_valid, (BLOCK, BLOCK))
    edge_valid = lax.dynamic_slice_in_dim(padded_valid, my_index * rows_dev, rows_dev + 2 * BLOCK)
    own_valid_rows = edge_valid[BLOCK : BLOCK + rows_dev].astype(jnp.float32)
    own_valid = own_valid_rows[None, :, None]
    masked = table_rows.astype(jnp.float32) * own_valid

    up = [(i, i + 1) for i in range(shard_count - 1)]
    down = [(i + 1, i) for i in range(shard_count - 1)]
    before = lax.ppermute(table_rows[:, rows_dev - BLOCK :], AXES, up)
    after = lax.ppermute(table_rows[:, :BLOCK], AXES, down)

    low_bits = shard_bits // 2
    low_count = 2**low_bits
    high_bits = list(range(low_bits, shard_bits))
    pooled = []
    for bit in range(shard_bits):
        group = 2 ** (bit + 1)
        summed = jnp.sum(masked.reshape(2, rows_dev // group, group, features), axis=2) / group
        pooled.append(summed.astype(jnp.bfloat16))
    sizes = [p.shape[1] for p in pooled]

    far_chunks = []
    gathered = {bit: [pooled[bit]] for bit in high_bits}
    for low in range(1, low_count):
        bit = low.bit_length() - 1
        payload = jnp.concatenate([pooled[bit]] + [pooled[b] for b in high_bits], axis=1)
        received = xor_permute(payload, low, shard_count)
        far_chunks.append(received[:, : sizes[bit]])
        offset = sizes[bit]
        for b in high_bits:
            gathered[b].append(received[:, offset : offset + sizes[b]])
            offset += sizes[b]
    high_distances = [high << low_bits for high in range(1, 2 ** (shard_bits - low_bits))]
    stacked = {b: jnp.concatenate(gathered[b], axis=1) for b in high_bits}
    for distance in high_distances:
        bit = distance.bit_length() - 1
        far_chunks.append(xor_permute(stacked[bit], distance, shard_count))

    full = jnp.concatenate([before, table_rows, after] + far_chunks, axis=1)
    near_rows = rows_dev + 2 * BLOCK
    cols = full.shape[1]
    col_valid = jnp.concatenate(
        [edge_valid, jnp.ones((cols - near_rows,), edge_valid.dtype)]
    ).reshape(1, cols)
    attended, query_grad, terms, far_terms = attention(
        permute, queries, out_grad, full, col_valid, head_dim, near_rows
    )

    from_next = lax.ppermute(terms[:, :BLOCK].astype(jnp.bfloat16), AXES, down).astype(jnp.float32)
    from_prev = lax.ppermute(
        terms[:, near_rows - BLOCK : near_rows].astype(jnp.bfloat16), AXES, up
    ).astype(jnp.float32)

    offset = 0
    direct_terms = []
    for low in range(1, low_count):
        size = sizes[low.bit_length() - 1]
        direct_terms.append(far_terms[:, offset : offset + size])
        offset += size
    stacked_sums = {}
    pieces = []
    segments = []
    for distance in high_distances:
        bit = distance.bit_length() - 1
        size = low_count * sizes[bit]
        returned = xor_permute(far_terms[:, offset : offset + size], distance, shard_count)
        offset += size
        pieces.append(returned[:, : sizes[bit]])
        segments.append(bit)
        returned = returned.astype(jnp.float32)
        stacked_sums[bit] = returned if bit not in stacked_sums else stacked_sums[bit] + returned
    for low in range(1, low_count):
        bit = low.bit_length() - 1
        parts = [direct_terms[low - 1]] + [
            stacked_sums[b][:, low * sizes[b] : (low + 1) * sizes[b]].astype(jnp.bfloat16) for b in high_bits
        ]
        pieces.append(xor_permute(jnp.concatenate(parts, axis=1), low, shard_count))
        segments.extend([bit] + high_bits)
    expand = np.zeros((rows_dev, sum(sizes[b] for b in segments)), np.float32)
    column = 0
    for bit in segments:
        group = 2 ** (bit + 1)
        for j in range(sizes[bit]):
            expand[j * group : (j + 1) * group, column + j] = 1.0 / group
        column += sizes[bit]
    expand = jnp.asarray(expand, dtype=jnp.bfloat16)
    spread = jnp.stack(
        [
            jnp.dot(expand, jnp.concatenate([piece[c] for piece in pieces], axis=0), preferred_element_type=jnp.float32)
            for c in range(2)
        ]
    )
    edges = jnp.concatenate([from_prev, from_next], axis=1)
    row_grad = terms[:, BLOCK : BLOCK + rows_dev] + edges + own_valid * spread

    def restore(hilbert_rows):
        restored = lax.dot_general(
            one_hot, hilbert_rows, (((0,), (0,)), ((), ())), preferred_element_type=jnp.float32
        )
        return restored.astype(jnp.bfloat16)

    return (attended, query_grad, restore(row_grad[0].astype(jnp.bfloat16)), restore(row_grad[1].astype(jnp.bfloat16)))


def solution(mesh):
    in_specs = (
        P(("parts", "rows", "sub"), "head"),
        P(("parts", "rows", "sub"), "head"),
        P(("parts", "rows", "sub"), "head"),
        P(("parts", "rows", "sub"), "head"),
        P(("parts", "rows", "sub"), None),
        P("parts"),
    )
    out_specs = (
        P(("parts", "rows", "sub"), "head"),
        P(("parts", "rows", "sub"), "head"),
        P(("parts", "rows", "sub"), "head"),
        P(("parts", "rows", "sub"), "head"),
    )
    return jax.shard_map(
        per_device, mesh=mesh, in_specs=in_specs, out_specs=out_specs, check_vma=False
    )
```

```python
import math

import numpy as np

import jax
import jax.numpy as jnp
from jax import lax
from jax.experimental import pallas as pl
from jax.experimental.pallas import tpu as pltpu
from jax.sharding import PartitionSpec as P

D = 512
HEADS = 8
BLOCK = 128
AXES = ("rows", "sub")
LANES = 128


def attention_kernel(
    order_col_ref, order_row_ref, q_ref, g_ref, kv_ref, cv_ref, att_ref, qg_ref, near_ref, far_ref, bias_ref,
    *, head_dim, near_rows
):
    rows = q_ref.shape[0]
    cols = kv_ref.shape[1]
    scale = 1.0 / math.sqrt(head_dim)
    gather = (
        order_col_ref[...] == lax.broadcasted_iota(jnp.int32, (rows, rows), 1)
    ).astype(jnp.bfloat16)
    scatter = (
        order_row_ref[...] == lax.broadcasted_iota(jnp.int32, (rows, rows), 0)
    ).astype(jnp.bfloat16)
    q_all = jnp.dot(gather, q_ref[...], preferred_element_type=jnp.float32).astype(jnp.bfloat16)
    g_all = jnp.dot(gather, g_ref[...], preferred_element_type=jnp.float32).astype(jnp.bfloat16)

    @pl.when(pl.program_id(0) == 0)
    def _():
        row = lax.broadcasted_iota(jnp.int32, (rows, cols), 0)
        col = lax.broadcasted_iota(jnp.int32, (rows, cols), 1)
        start = (row // BLOCK) * BLOCK
        in_window = (col >= start) & (col < start + 3 * BLOCK)
        ok = (col >= near_rows) | (in_window & (cv_ref[...] > 0))
        bias_ref[...] = jnp.where(ok, 0.0, -jnp.inf).astype(jnp.float32)

    nt = (((1,), (1,)), ((), ()))
    tn = (((0,), (0,)), ((), ()))
    lane = lax.broadcasted_iota(jnp.int32, (1, LANES), 1)
    k = kv_ref[0]
    v = kv_ref[1]
    att = qg = key_term = value_term = None
    for h in range(LANES // head_dim):
        sel = (lane >= h * head_dim) & (lane < (h + 1) * head_dim)
        q = jnp.where(sel, q_all, jnp.zeros_like(q_all))
        g = jnp.where(sel, g_all, jnp.zeros_like(g_all))
        s = lax.dot_general(q, k, nt, preferred_element_type=jnp.float32) * scale + bias_ref[...]
        m = jnp.max(s, axis=-1, keepdims=True)
        e = jnp.exp(s - m)
        w = e / jnp.sum(e, axis=-1, keepdims=True)
        wb = w.astype(jnp.bfloat16)
        vd = lax.dot_general(g, v, nt, preferred_element_type=jnp.float32)
        rd = jnp.sum(w * vd, axis=-1, keepdims=True)
        sg = (w * (vd - rd) * scale).astype(jnp.bfloat16)
        outs = (
            jnp.dot(wb, v, preferred_element_type=jnp.float32),
            jnp.dot(sg, k, preferred_element_type=jnp.float32),
            lax.dot_general(sg, q_all, tn, preferred_element_type=jnp.float32),
            lax.dot_general(wb, g_all, tn, preferred_element_type=jnp.float32),
        )
        if att is None:
            att, qg, key_term, value_term = outs
        else:
            att, qg, key_term, value_term = (
                jnp.where(sel, new, old) for new, old in zip(outs, (att, qg, key_term, value_term))
            )
    for c, term in enumerate((key_term, value_term)):
        near_ref[c] = term[:near_rows]
        far_ref[c] = term[near_rows:].astype(far_ref.dtype)
    att_ref[...] = jnp.dot(
        scatter, att.astype(jnp.bfloat16), preferred_element_type=jnp.float32
    ).astype(att_ref.dtype)
    qg_ref[...] = jnp.dot(
        scatter, qg.astype(jnp.bfloat16), preferred_element_type=jnp.float32
    ).astype(qg_ref.dtype)


def attention(order, queries, out_grad, kv_all, col_valid, head_dim, near_rows):
    rows, features = queries.shape
    cols = kv_all.shape[1]
    row_spec = pl.BlockSpec((rows, LANES), lambda i: (0, i))
    kv_spec = pl.BlockSpec((2, cols, LANES), lambda i: (0, 0, i))
    kernel = lambda *refs: attention_kernel(*refs, head_dim=head_dim, near_rows=near_rows)
    return pl.pallas_call(
        kernel,
        grid=(features // LANES,),
        in_specs=[
            pl.BlockSpec((rows, 1), lambda i: (0, 0)),
            pl.BlockSpec((1, rows), lambda i: (0, 0)),
            row_spec,
            row_spec,
            kv_spec,
            pl.BlockSpec((1, cols), lambda i: (0, 0)),
        ],
        out_specs=[
            row_spec,
            row_spec,
            pl.BlockSpec((2, near_rows, LANES), lambda i: (0, 0, i)),
            pl.BlockSpec((2, cols - near_rows, LANES), lambda i: (0, 0, i)),
        ],
        out_shape=[
            jax.ShapeDtypeStruct((rows, features), jnp.bfloat16),
            jax.ShapeDtypeStruct((rows, features), jnp.bfloat16),
            jax.ShapeDtypeStruct((2, near_rows, features), jnp.float32),
            jax.ShapeDtypeStruct((2, cols - near_rows, features), jnp.bfloat16),
        ],
        scratch_shapes=[pltpu.VMEM((rows, cols), jnp.float32)],
    )(order.reshape(rows, 1), order.reshape(1, rows), queries, out_grad, kv_all, col_valid)


def xor_permute(value, distance, count):
    return lax.ppermute(value, AXES, [(i, i ^ distance) for i in range(count)])


def per_device(queries, key_table, value_table, out_grad, hilbert_order, key_valid):
    rows_dev, features = queries.shape
    head_dim = D // HEADS
    shard_count = lax.axis_size(AXES)
    shard_bits = shard_count.bit_length() - 1
    my_index = lax.axis_index(AXES)
    permute = hilbert_order[0]
    one_hot = (permute[:, None] == lax.broadcasted_iota(jnp.int32, (rows_dev, rows_dev), 1)).astype(
        jnp.bfloat16
    )

    def take(storage_rows):
        return jnp.dot(one_hot, storage_rows, preferred_element_type=jnp.float32).astype(jnp.bfloat16)

    table_rows = jnp.stack([take(key_table), take(value_table)])
    padded_valid = jnp.pad(key_valid, (BLOCK, BLOCK))
    edge_valid = lax.dynamic_slice_in_dim(padded_valid, my_index * rows_dev, rows_dev + 2 * BLOCK)
    own_valid_rows = edge_valid[BLOCK : BLOCK + rows_dev].astype(jnp.float32)
    own_valid = own_valid_rows[None, :, None]

    up = [(i, i + 1) for i in range(shard_count - 1)]
    down = [(i + 1, i) for i in range(shard_count - 1)]
    before = lax.ppermute(table_rows[:, rows_dev - BLOCK :], AXES, up)
    after = lax.ppermute(table_rows[:, :BLOCK], AXES, down)

    low_bits = shard_bits // 2
    low_count = 2**low_bits
    high_bits = list(range(low_bits, shard_bits))
    sizes = [rows_dev // 2 ** (bit + 1) for bit in range(shard_bits)]

    def pool(bits):
        matrix = np.zeros((sum(sizes[b] for b in bits), rows_dev), np.float32)
        offset = 0
        for b in bits:
            group = 2 ** (b + 1)
            for j in range(sizes[b]):
                matrix[offset + j, j * group : (j + 1) * group] = 1.0 / group
            offset += sizes[b]
        weights = (jnp.asarray(matrix) * own_valid_rows[None, :]).astype(jnp.bfloat16)
        return jnp.stack(
            [
                jnp.dot(weights, table_rows[c], preferred_element_type=jnp.float32).astype(jnp.bfloat16)
                for c in range(2)
            ]
        )

    far_chunks = []
    own_high = pool(high_bits)
    gathered = {}
    offset = 0
    for b in high_bits:
        gathered[b] = [own_high[:, offset : offset + sizes[b]]]
        offset += sizes[b]
    for low in range(1, low_count):
        bit = low.bit_length() - 1
        received = xor_permute(pool([bit] + high_bits), low, shard_count)
        far_chunks.append(received[:, : sizes[bit]])
        offset = sizes[bit]
        for b in high_bits:
            gathered[b].append(received[:, offset : offset + sizes[b]])
            offset += sizes[b]
    high_distances = [high << low_bits for high in range(1, 2 ** (shard_bits - low_bits))]
    stacked = {b: jnp.concatenate(gathered[b], axis=1) for b in high_bits}
    for distance in high_distances:
        bit = distance.bit_length() - 1
        far_chunks.append(xor_permute(stacked[bit], distance, shard_count))

    full = jnp.concatenate([before, table_rows, after] + far_chunks, axis=1)
    near_rows = rows_dev + 2 * BLOCK
    cols = full.shape[1]
    col_valid = jnp.concatenate(
        [edge_valid, jnp.ones((cols - near_rows,), edge_valid.dtype)]
    ).reshape(1, cols)
    attended, query_grad, terms, far_terms = attention(
        permute, queries, out_grad, full, col_valid, head_dim, near_rows
    )

    from_next = lax.ppermute(terms[:, :BLOCK].astype(jnp.bfloat16), AXES, down).astype(jnp.float32)
    from_prev = lax.ppermute(
        terms[:, near_rows - BLOCK : near_rows].astype(jnp.bfloat16), AXES, up
    ).astype(jnp.float32)

    offset = 0
    direct_terms = []
    for low in range(1, low_count):
        size = sizes[low.bit_length() - 1]
        direct_terms.append(far_terms[:, offset : offset + size])
        offset += size
    stacked_sums = {}
    pieces = []
    segments = []
    for distance in high_distances:
        bit = distance.bit_length() - 1
        size = low_count * sizes[bit]
        returned = xor_permute(far_terms[:, offset : offset + size], distance, shard_count)
        offset += size
        pieces.append(returned[:, : sizes[bit]])
        segments.append(bit)
        returned = returned.astype(jnp.float32)
        stacked_sums[bit] = returned if bit not in stacked_sums else stacked_sums[bit] + returned
    for low in range(1, low_count):
        bit = low.bit_length() - 1
        parts = [direct_terms[low - 1]] + [
            stacked_sums[b][:, low * sizes[b] : (low + 1) * sizes[b]].astype(jnp.bfloat16) for b in high_bits
        ]
        pieces.append(xor_permute(jnp.concatenate(parts, axis=1), low, shard_count))
        segments.extend([bit] + high_bits)
    expand = np.zeros((rows_dev, sum(sizes[b] for b in segments)), np.float32)
    column = 0
    for bit in segments:
        group = 2 ** (bit + 1)
        for j in range(sizes[bit]):
            expand[j * group : (j + 1) * group, column + j] = 1.0 / group
        column += sizes[bit]
    expand = jnp.asarray(expand, dtype=jnp.bfloat16)
    spread = jnp.stack(
        [
            jnp.dot(expand, jnp.concatenate([piece[c] for piece in pieces], axis=0), preferred_element_type=jnp.float32)
            for c in range(2)
        ]
    )
    edges = jnp.concatenate([from_prev, from_next], axis=1)
    row_grad = terms[:, BLOCK : BLOCK + rows_dev] + edges + own_valid * spread

    def restore(hilbert_rows):
        restored = lax.dot_general(
            one_hot, hilbert_rows, (((0,), (0,)), ((), ())), preferred_element_type=jnp.float32
        )
        return restored.astype(jnp.bfloat16)

    return (attended, query_grad, restore(row_grad[0].astype(jnp.bfloat16)), restore(row_grad[1].astype(jnp.bfloat16)))


def solution(mesh):
    in_specs = (
        P(("parts", "rows", "sub"), "head"),
        P(("parts", "rows", "sub"), "head"),
        P(("parts", "rows", "sub"), "head"),
        P(("parts", "rows", "sub"), "head"),
        P(("parts", "rows", "sub"), None),
        P("parts"),
    )
    out_specs = (
        P(("parts", "rows", "sub"), "head"),
        P(("parts", "rows", "sub"), "head"),
        P(("parts", "rows", "sub"), "head"),
        P(("parts", "rows", "sub"), "head"),
    )
    return jax.shard_map(
        per_device, mesh=mesh, in_specs=in_specs, out_specs=out_specs, check_vma=False
    )
```

```python
import math

import numpy as np

import jax
import jax.numpy as jnp
from jax import lax
from jax.experimental import pallas as pl
from jax.experimental.pallas import tpu as pltpu
from jax.sharding import PartitionSpec as P

D = 512
HEADS = 8
BLOCK = 128
AXES = ("rows", "sub")
LANES = 128
CHUNK = 16


def attention_kernel(
    order_col_ref, order_row_ref, q_ref, g_ref, kv_ref, cv_ref, att_ref, qg_ref, near_ref, far_ref, bias_ref,
    s_ref, vd_ref, wb_ref, sg_ref, *, head_dim, near_rows
):
    rows = q_ref.shape[0]
    cols = kv_ref.shape[1]
    scale = 1.0 / math.sqrt(head_dim)
    gather = (
        order_col_ref[...] == lax.broadcasted_iota(jnp.int32, (rows, rows), 1)
    ).astype(jnp.bfloat16)
    scatter = (
        order_row_ref[...] == lax.broadcasted_iota(jnp.int32, (rows, rows), 0)
    ).astype(jnp.bfloat16)
    q_all = jnp.dot(gather, q_ref[...], preferred_element_type=jnp.float32).astype(jnp.bfloat16)
    g_all = jnp.dot(gather, g_ref[...], preferred_element_type=jnp.float32).astype(jnp.bfloat16)

    @pl.when(pl.program_id(0) == 0)
    def _():
        row = lax.broadcasted_iota(jnp.int32, (rows, cols), 0)
        col = lax.broadcasted_iota(jnp.int32, (rows, cols), 1)
        start = (row // BLOCK) * BLOCK
        in_window = (col >= start) & (col < start + 3 * BLOCK)
        ok = (col >= near_rows) | (in_window & (cv_ref[...] > 0))
        bias_ref[...] = jnp.where(ok, 0.0, -jnp.inf).astype(jnp.float32)

    nt = (((1,), (1,)), ((), ()))
    tn = (((0,), (0,)), ((), ()))
    lane = lax.broadcasted_iota(jnp.int32, (1, LANES), 1)
    k = kv_ref[0]
    v = kv_ref[1]
    att = qg = key_term = value_term = None
    for h in range(LANES // head_dim):
        sel = (lane >= h * head_dim) & (lane < (h + 1) * head_dim)
        q = jnp.where(sel, q_all, jnp.zeros_like(q_all))
        g = jnp.where(sel, g_all, jnp.zeros_like(g_all))
        s_ref[...] = lax.dot_general(q, k, nt, preferred_element_type=jnp.float32)
        vd_ref[...] = lax.dot_general(g, v, nt, preferred_element_type=jnp.float32)

        def chunk(step, carry):
            r = pl.multiple_of(step * CHUNK, CHUNK)
            s = s_ref[pl.ds(r, CHUNK), :] * scale + bias_ref[pl.ds(r, CHUNK), :]
            m = jnp.max(s, axis=-1, keepdims=True)
            e = jnp.exp(s - m)
            w = e / jnp.sum(e, axis=-1, keepdims=True)
            wb_ref[pl.ds(r, CHUNK), :] = w.astype(jnp.bfloat16)
            vd = vd_ref[pl.ds(r, CHUNK), :]
            rd = jnp.sum(w * vd, axis=-1, keepdims=True)
            sg_ref[pl.ds(r, CHUNK), :] = (w * (vd - rd) * scale).astype(jnp.bfloat16)
            return carry

        lax.fori_loop(0, rows // CHUNK, chunk, 0)
        wb = wb_ref[...]
        sg = sg_ref[...]
        outs = (
            jnp.dot(wb, v, preferred_element_type=jnp.float32),
            jnp.dot(sg, k, preferred_element_type=jnp.float32),
            lax.dot_general(sg, q_all, tn, preferred_element_type=jnp.float32),
            lax.dot_general(wb, g_all, tn, preferred_element_type=jnp.float32),
        )
        if att is None:
            att, qg, key_term, value_term = outs
        else:
            att, qg, key_term, value_term = (
                jnp.where(sel, new, old) for new, old in zip(outs, (att, qg, key_term, value_term))
            )
    for c, term in enumerate((key_term, value_term)):
        near_ref[c] = term[:near_rows]
        far_ref[c] = term[near_rows:].astype(far_ref.dtype)
    att_ref[...] = jnp.dot(
        scatter, att.astype(jnp.bfloat16), preferred_element_type=jnp.float32
    ).astype(att_ref.dtype)
    qg_ref[...] = jnp.dot(
        scatter, qg.astype(jnp.bfloat16), preferred_element_type=jnp.float32
    ).astype(qg_ref.dtype)


def attention(order, queries, out_grad, kv_all, col_valid, head_dim, near_rows):
    rows, features = queries.shape
    cols = kv_all.shape[1]
    row_spec = pl.BlockSpec((rows, LANES), lambda i: (0, i))
    kv_spec = pl.BlockSpec((2, cols, LANES), lambda i: (0, 0, i))
    kernel = lambda *refs: attention_kernel(*refs, head_dim=head_dim, near_rows=near_rows)
    return pl.pallas_call(
        kernel,
        grid=(features // LANES,),
        in_specs=[
            pl.BlockSpec((rows, 1), lambda i: (0, 0)),
            pl.BlockSpec((1, rows), lambda i: (0, 0)),
            row_spec,
            row_spec,
            kv_spec,
            pl.BlockSpec((1, cols), lambda i: (0, 0)),
        ],
        out_specs=[
            row_spec,
            row_spec,
            pl.BlockSpec((2, near_rows, LANES), lambda i: (0, 0, i)),
            pl.BlockSpec((2, cols - near_rows, LANES), lambda i: (0, 0, i)),
        ],
        out_shape=[
            jax.ShapeDtypeStruct((rows, features), jnp.bfloat16),
            jax.ShapeDtypeStruct((rows, features), jnp.bfloat16),
            jax.ShapeDtypeStruct((2, near_rows, features), jnp.float32),
            jax.ShapeDtypeStruct((2, cols - near_rows, features), jnp.bfloat16),
        ],
        scratch_shapes=[
            pltpu.VMEM((rows, cols), jnp.float32),
            pltpu.VMEM((rows, cols), jnp.float32),
            pltpu.VMEM((rows, cols), jnp.float32),
            pltpu.VMEM((rows, cols), jnp.bfloat16),
            pltpu.VMEM((rows, cols), jnp.bfloat16),
        ],
    )(order.reshape(rows, 1), order.reshape(1, rows), queries, out_grad, kv_all, col_valid)


def xor_permute(value, distance, count):
    return lax.ppermute(value, AXES, [(i, i ^ distance) for i in range(count)])


def per_device(queries, key_table, value_table, out_grad, hilbert_order, key_valid):
    rows_dev, features = queries.shape
    head_dim = D // HEADS
    shard_count = lax.axis_size(AXES)
    shard_bits = shard_count.bit_length() - 1
    my_index = lax.axis_index(AXES)
    permute = hilbert_order[0]
    one_hot = (permute[:, None] == lax.broadcasted_iota(jnp.int32, (rows_dev, rows_dev), 1)).astype(
        jnp.bfloat16
    )

    def take(storage_rows):
        return jnp.dot(one_hot, storage_rows, preferred_element_type=jnp.float32).astype(jnp.bfloat16)

    table_rows = jnp.stack([take(key_table), take(value_table)])
    padded_valid = jnp.pad(key_valid, (BLOCK, BLOCK))
    edge_valid = lax.dynamic_slice_in_dim(padded_valid, my_index * rows_dev, rows_dev + 2 * BLOCK)
    own_valid_rows = edge_valid[BLOCK : BLOCK + rows_dev].astype(jnp.float32)
    own_valid = own_valid_rows[None, :, None]

    up = [(i, i + 1) for i in range(shard_count - 1)]
    down = [(i + 1, i) for i in range(shard_count - 1)]
    before = lax.ppermute(table_rows[:, rows_dev - BLOCK :], AXES, up)
    after = lax.ppermute(table_rows[:, :BLOCK], AXES, down)

    low_bits = shard_bits // 2
    low_count = 2**low_bits
    high_bits = list(range(low_bits, shard_bits))
    sizes = [rows_dev // 2 ** (bit + 1) for bit in range(shard_bits)]

    def pool(bits):
        matrix = np.zeros((sum(sizes[b] for b in bits), rows_dev), np.float32)
        offset = 0
        for b in bits:
            group = 2 ** (b + 1)
            for j in range(sizes[b]):
                matrix[offset + j, j * group : (j + 1) * group] = 1.0 / group
            offset += sizes[b]
        weights = (jnp.asarray(matrix) * own_valid_rows[None, :]).astype(jnp.bfloat16)
        return jnp.stack(
            [
                jnp.dot(weights, table_rows[c], preferred_element_type=jnp.float32).astype(jnp.bfloat16)
                for c in range(2)
            ]
        )

    far_chunks = []
    own_high = pool(high_bits)
    gathered = {}
    offset = 0
    for b in high_bits:
        gathered[b] = [own_high[:, offset : offset + sizes[b]]]
        offset += sizes[b]
    for low in range(1, low_count):
        bit = low.bit_length() - 1
        received = xor_permute(pool([bit] + high_bits), low, shard_count)
        far_chunks.append(received[:, : sizes[bit]])
        offset = sizes[bit]
        for b in high_bits:
            gathered[b].append(received[:, offset : offset + sizes[b]])
            offset += sizes[b]
    high_distances = [high << low_bits for high in range(1, 2 ** (shard_bits - low_bits))]
    stacked = {b: jnp.concatenate(gathered[b], axis=1) for b in high_bits}
    for distance in high_distances:
        bit = distance.bit_length() - 1
        far_chunks.append(xor_permute(stacked[bit], distance, shard_count))

    full = jnp.concatenate([before, table_rows, after] + far_chunks, axis=1)
    near_rows = rows_dev + 2 * BLOCK
    cols = full.shape[1]
    col_valid = jnp.concatenate(
        [edge_valid, jnp.ones((cols - near_rows,), edge_valid.dtype)]
    ).reshape(1, cols)
    attended, query_grad, terms, far_terms = attention(
        permute, queries, out_grad, full, col_valid, head_dim, near_rows
    )

    from_next = lax.ppermute(terms[:, :BLOCK].astype(jnp.bfloat16), AXES, down).astype(jnp.float32)
    from_prev = lax.ppermute(
        terms[:, near_rows - BLOCK : near_rows].astype(jnp.bfloat16), AXES, up
    ).astype(jnp.float32)

    offset = 0
    direct_terms = []
    for low in range(1, low_count):
        size = sizes[low.bit_length() - 1]
        direct_terms.append(far_terms[:, offset : offset + size])
        offset += size
    stacked_sums = {}
    pieces = []
    segments = []
    for distance in high_distances:
        bit = distance.bit_length() - 1
        size = low_count * sizes[bit]
        returned = xor_permute(far_terms[:, offset : offset + size], distance, shard_count)
        offset += size
        pieces.append(returned[:, : sizes[bit]])
        segments.append(bit)
        returned = returned.astype(jnp.float32)
        stacked_sums[bit] = returned if bit not in stacked_sums else stacked_sums[bit] + returned
    for low in range(1, low_count):
        bit = low.bit_length() - 1
        parts = [direct_terms[low - 1]] + [
            stacked_sums[b][:, low * sizes[b] : (low + 1) * sizes[b]].astype(jnp.bfloat16) for b in high_bits
        ]
        pieces.append(xor_permute(jnp.concatenate(parts, axis=1), low, shard_count))
        segments.extend([bit] + high_bits)
    expand = np.zeros((rows_dev, sum(sizes[b] for b in segments)), np.float32)
    column = 0
    for bit in segments:
        group = 2 ** (bit + 1)
        for j in range(sizes[bit]):
            expand[j * group : (j + 1) * group, column + j] = 1.0 / group
        column += sizes[bit]
    expand = jnp.asarray(expand, dtype=jnp.bfloat16)
    spread = jnp.stack(
        [
            jnp.dot(expand, jnp.concatenate([piece[c] for piece in pieces], axis=0), preferred_element_type=jnp.float32)
            for c in range(2)
        ]
    )
    edges = jnp.concatenate([from_prev, from_next], axis=1)
    row_grad = terms[:, BLOCK : BLOCK + rows_dev] + edges + own_valid * spread

    def restore(hilbert_rows):
        restored = lax.dot_general(
            one_hot, hilbert_rows, (((0,), (0,)), ((), ())), preferred_element_type=jnp.float32
        )
        return restored.astype(jnp.bfloat16)

    return (attended, query_grad, restore(row_grad[0].astype(jnp.bfloat16)), restore(row_grad[1].astype(jnp.bfloat16)))


def solution(mesh):
    in_specs = (
        P(("parts", "rows", "sub"), "head"),
        P(("parts", "rows", "sub"), "head"),
        P(("parts", "rows", "sub"), "head"),
        P(("parts", "rows", "sub"), "head"),
        P(("parts", "rows", "sub"), None),
        P("parts"),
    )
    out_specs = (
        P(("parts", "rows", "sub"), "head"),
        P(("parts", "rows", "sub"), "head"),
        P(("parts", "rows", "sub"), "head"),
        P(("parts", "rows", "sub"), "head"),
    )
    return jax.shard_map(
        per_device, mesh=mesh, in_specs=in_specs, out_specs=out_specs, check_vma=False
    )
```

```python
import math

import numpy as np

import jax
import jax.numpy as jnp
from jax import lax
from jax.experimental import pallas as pl
from jax.experimental.pallas import tpu as pltpu
from jax.sharding import PartitionSpec as P

D = 512
HEADS = 8
BLOCK = 128
AXES = ("rows", "sub")
LANES = 128


def attention_kernel(
    order_col_ref, order_row_ref, q_ref, g_ref, kv_ref, cv_ref, att_ref, qg_ref, near_ref, far_ref, bias_ref,
    *, head_dim, near_rows
):
    rows = q_ref.shape[0]
    cols = kv_ref.shape[1]
    scale = 1.0 / math.sqrt(head_dim)
    gather = (
        order_col_ref[...] == lax.broadcasted_iota(jnp.int32, (rows, rows), 1)
    ).astype(jnp.bfloat16)
    scatter = (
        order_row_ref[...] == lax.broadcasted_iota(jnp.int32, (rows, rows), 0)
    ).astype(jnp.bfloat16)
    q_all = jnp.dot(gather, q_ref[...], preferred_element_type=jnp.float32).astype(jnp.bfloat16)
    g_all = jnp.dot(gather, g_ref[...], preferred_element_type=jnp.float32).astype(jnp.bfloat16)

    @pl.when(pl.program_id(0) == 0)
    def _():
        row = lax.broadcasted_iota(jnp.int32, (rows, cols), 0)
        col = lax.broadcasted_iota(jnp.int32, (rows, cols), 1)
        start = (row // BLOCK) * BLOCK
        in_window = (col >= start) & (col < start + 3 * BLOCK)
        ok = (col >= near_rows) | (in_window & (cv_ref[...] > 0))
        bias_ref[...] = jnp.where(ok, 0.0, -jnp.inf).astype(jnp.float32)

    nt = (((1,), (1,)), ((), ()))
    tn = (((0,), (0,)), ((), ()))
    lane = lax.broadcasted_iota(jnp.int32, (1, LANES), 1)
    k = kv_ref[0]
    v = kv_ref[1]
    att = qg = key_term = value_term = None
    for h in range(LANES // head_dim):
        sel = (lane >= h * head_dim) & (lane < (h + 1) * head_dim)
        q = jnp.where(sel, q_all, jnp.zeros_like(q_all))
        g = jnp.where(sel, g_all, jnp.zeros_like(g_all))
        s = lax.dot_general(q, k, nt, preferred_element_type=jnp.float32) * scale + bias_ref[...]
        m = jnp.max(s, axis=-1, keepdims=True)
        e = jnp.exp(s - m)
        w = e / jnp.sum(e, axis=-1, keepdims=True)
        wb = w.astype(jnp.bfloat16)
        vd = lax.dot_general(g, v, nt, preferred_element_type=jnp.float32)
        rd = jnp.sum(w * vd, axis=-1, keepdims=True)
        sg = (w * (vd - rd) * scale).astype(jnp.bfloat16)
        outs = (
            jnp.dot(wb, v, preferred_element_type=jnp.float32),
            jnp.dot(sg, k, preferred_element_type=jnp.float32),
            lax.dot_general(sg, q_all, tn, preferred_element_type=jnp.float32),
            lax.dot_general(wb, g_all, tn, preferred_element_type=jnp.float32),
        )
        if att is None:
            att, qg, key_term, value_term = outs
        else:
            att, qg, key_term, value_term = (
                jnp.where(sel, new, old) for new, old in zip(outs, (att, qg, key_term, value_term))
            )
    for c, term in enumerate((key_term, value_term)):
        near_ref[c] = term[:near_rows]
        far_ref[c] = term[near_rows:].astype(far_ref.dtype)
    att_ref[...] = jnp.dot(
        scatter, att.astype(jnp.bfloat16), preferred_element_type=jnp.float32
    ).astype(att_ref.dtype)
    qg_ref[...] = jnp.dot(
        scatter, qg.astype(jnp.bfloat16), preferred_element_type=jnp.float32
    ).astype(qg_ref.dtype)


def attention(order, queries, out_grad, kv_all, col_valid, head_dim, near_rows):
    rows, features = queries.shape
    cols = kv_all.shape[1]
    row_spec = pl.BlockSpec((rows, LANES), lambda i: (0, i))
    kv_spec = pl.BlockSpec((2, cols, LANES), lambda i: (0, 0, i))
    kernel = lambda *refs: attention_kernel(*refs, head_dim=head_dim, near_rows=near_rows)
    return pl.pallas_call(
        kernel,
        grid=(features // LANES,),
        in_specs=[
            pl.BlockSpec((rows, 1), lambda i: (0, 0)),
            pl.BlockSpec((1, rows), lambda i: (0, 0)),
            row_spec,
            row_spec,
            kv_spec,
            pl.BlockSpec((1, cols), lambda i: (0, 0)),
        ],
        out_specs=[
            row_spec,
            row_spec,
            pl.BlockSpec((2, near_rows, LANES), lambda i: (0, 0, i)),
            pl.BlockSpec((2, cols - near_rows, LANES), lambda i: (0, 0, i)),
        ],
        out_shape=[
            jax.ShapeDtypeStruct((rows, features), jnp.bfloat16),
            jax.ShapeDtypeStruct((rows, features), jnp.bfloat16),
            jax.ShapeDtypeStruct((2, near_rows, features), jnp.float32),
            jax.ShapeDtypeStruct((2, cols - near_rows, features), jnp.bfloat16),
        ],
        scratch_shapes=[pltpu.VMEM((rows, cols), jnp.float32)],
    )(order.reshape(rows, 1), order.reshape(1, rows), queries, out_grad, kv_all, col_valid)


def xor_permute(value, distance, count):
    return lax.ppermute(value, AXES, [(i, i ^ distance) for i in range(count)])


def per_device(queries, key_table, value_table, out_grad, hilbert_order, key_valid):
    rows_dev, features = queries.shape
    head_dim = D // HEADS
    shard_count = lax.axis_size(AXES)
    shard_bits = shard_count.bit_length() - 1
    my_index = lax.axis_index(AXES)
    permute = hilbert_order[0]
    one_hot = (permute[:, None] == lax.broadcasted_iota(jnp.int32, (rows_dev, rows_dev), 1)).astype(
        jnp.bfloat16
    )

    def take(storage_rows):
        return jnp.dot(one_hot, storage_rows, preferred_element_type=jnp.float32).astype(jnp.bfloat16)

    table_rows = jnp.stack([take(key_table), take(value_table)])
    padded_valid = jnp.pad(key_valid, (BLOCK, BLOCK))
    edge_valid = lax.dynamic_slice_in_dim(padded_valid, my_index * rows_dev, rows_dev + 2 * BLOCK)
    own_valid_rows = edge_valid[BLOCK : BLOCK + rows_dev].astype(jnp.float32)
    own_valid = own_valid_rows[None, :, None]

    up = [(i, i + 1) for i in range(shard_count - 1)]
    down = [(i + 1, i) for i in range(shard_count - 1)]
    before = lax.ppermute(table_rows[:, rows_dev - BLOCK :], AXES, up)
    after = lax.ppermute(table_rows[:, :BLOCK], AXES, down)

    low_bits = shard_bits // 2
    low_count = 2**low_bits
    high_bits = list(range(low_bits, shard_bits))
    sizes = [rows_dev // 2 ** (bit + 1) for bit in range(shard_bits)]

    def pool(bits):
        matrix = np.zeros((sum(sizes[b] for b in bits), rows_dev), np.float32)
        offset = 0
        for b in bits:
            group = 2 ** (b + 1)
            for j in range(sizes[b]):
                matrix[offset + j, j * group : (j + 1) * group] = 1.0 / group
            offset += sizes[b]
        weights = (jnp.asarray(matrix) * own_valid_rows[None, :]).astype(jnp.bfloat16)
        return jnp.stack(
            [
                jnp.dot(weights, table_rows[c], preferred_element_type=jnp.float32).astype(jnp.bfloat16)
                for c in range(2)
            ]
        )

    far_chunks = []
    own_high = pool(high_bits)
    gathered = {}
    offset = 0
    for b in high_bits:
        gathered[b] = [own_high[:, offset : offset + sizes[b]]]
        offset += sizes[b]
    for low in range(1, low_count):
        bit = low.bit_length() - 1
        received = xor_permute(pool([bit] + high_bits), low, shard_count)
        far_chunks.append(received[:, : sizes[bit]])
        offset = sizes[bit]
        for b in high_bits:
            gathered[b].append(received[:, offset : offset + sizes[b]])
            offset += sizes[b]
    high_distances = [high << low_bits for high in range(1, 2 ** (shard_bits - low_bits))]
    stacked = {b: jnp.concatenate(gathered[b][0::2], axis=1) for b in high_bits}
    second = []
    for distance in high_distances:
        bit = distance.bit_length() - 1
        second.append(xor_permute(stacked[bit], distance, shard_count))
    third = xor_permute(jnp.concatenate(second, axis=1), 1, shard_count)
    far_chunks = far_chunks + second + [third]

    full = jnp.concatenate([before, table_rows, after] + far_chunks, axis=1)
    near_rows = rows_dev + 2 * BLOCK
    cols = full.shape[1]
    col_valid = jnp.concatenate(
        [edge_valid, jnp.ones((cols - near_rows,), edge_valid.dtype)]
    ).reshape(1, cols)
    attended, query_grad, terms, far_terms = attention(
        permute, queries, out_grad, full, col_valid, head_dim, near_rows
    )

    from_next = lax.ppermute(terms[:, :BLOCK].astype(jnp.bfloat16), AXES, down).astype(jnp.float32)
    from_prev = lax.ppermute(
        terms[:, near_rows - BLOCK : near_rows].astype(jnp.bfloat16), AXES, up
    ).astype(jnp.float32)

    offset = 0
    direct_terms = []
    for low in range(1, low_count):
        size = sizes[low.bit_length() - 1]
        direct_terms.append(far_terms[:, offset : offset + size])
        offset += size
    half = low_count // 2
    second_rows = [half * sizes[d.bit_length() - 1] for d in high_distances]
    third_terms = far_terms[:, offset + sum(second_rows) :]
    back = xor_permute(third_terms, 1, shard_count).astype(jnp.float32)
    stacked_sums = {}
    pieces = []
    segments = []
    back_offset = 0
    for distance, size in zip(high_distances, second_rows):
        bit = distance.bit_length() - 1
        own = far_terms[:, offset : offset + size].astype(jnp.float32) + back[:, back_offset : back_offset + size]
        offset += size
        back_offset += size
        returned = xor_permute(own.astype(jnp.bfloat16), distance, shard_count)
        pieces.append(returned[:, : sizes[bit]])
        segments.append(bit)
        returned = returned.astype(jnp.float32)
        stacked_sums[bit] = returned if bit not in stacked_sums else stacked_sums[bit] + returned
    for low in range(1, low_count):
        bit = low.bit_length() - 1
        parts = [direct_terms[low - 1]]
        segments.append(bit)
        if low % 2 == 0:
            entry = low // 2
            parts += [
                stacked_sums[b][:, entry * sizes[b] : (entry + 1) * sizes[b]].astype(jnp.bfloat16)
                for b in high_bits
            ]
            segments.extend(high_bits)
        pieces.append(xor_permute(jnp.concatenate(parts, axis=1), low, shard_count))
    expand = np.zeros((rows_dev, sum(sizes[b] for b in segments)), np.float32)
    column = 0
    for bit in segments:
        group = 2 ** (bit + 1)
        for j in range(sizes[bit]):
            expand[j * group : (j + 1) * group, column + j] = 1.0 / group
        column += sizes[bit]
    expand = jnp.asarray(expand, dtype=jnp.bfloat16)
    spread = jnp.stack(
        [
            jnp.dot(expand, jnp.concatenate([piece[c] for piece in pieces], axis=0), preferred_element_type=jnp.float32)
            for c in range(2)
        ]
    )
    edges = jnp.concatenate([from_prev, from_next], axis=1)
    row_grad = terms[:, BLOCK : BLOCK + rows_dev] + edges + own_valid * spread

    def restore(hilbert_rows):
        restored = lax.dot_general(
            one_hot, hilbert_rows, (((0,), (0,)), ((), ())), preferred_element_type=jnp.float32
        )
        return restored.astype(jnp.bfloat16)

    return (attended, query_grad, restore(row_grad[0].astype(jnp.bfloat16)), restore(row_grad[1].astype(jnp.bfloat16)))


def solution(mesh):
    in_specs = (
        P(("parts", "rows", "sub"), "head"),
        P(("parts", "rows", "sub"), "head"),
        P(("parts", "rows", "sub"), "head"),
        P(("parts", "rows", "sub"), "head"),
        P(("parts", "rows", "sub"), None),
        P("parts"),
    )
    out_specs = (
        P(("parts", "rows", "sub"), "head"),
        P(("parts", "rows", "sub"), "head"),
        P(("parts", "rows", "sub"), "head"),
        P(("parts", "rows", "sub"), "head"),
    )
    return jax.shard_map(
        per_device, mesh=mesh, in_specs=in_specs, out_specs=out_specs, check_vma=False
    )
```

```python
import math

import numpy as np

import jax
import jax.numpy as jnp
from jax import lax
from jax.experimental import pallas as pl
from jax.experimental.pallas import tpu as pltpu
from jax.sharding import PartitionSpec as P

D = 512
HEADS = 8
BLOCK = 128
AXES = ("rows", "sub")
LANES = 128


def attention_kernel(
    order_col_ref, order_row_ref, q_ref, g_ref, kv_ref, cv_ref, att_ref, qg_ref, near_ref, edge_ref, far_ref, bias_ref,
    *, head_dim, near_rows
):
    rows = q_ref.shape[0]
    cols = kv_ref.shape[1]
    scale = 1.0 / math.sqrt(head_dim)
    gather = (
        order_col_ref[...] == lax.broadcasted_iota(jnp.int32, (rows, rows), 1)
    ).astype(jnp.bfloat16)
    scatter = (
        order_row_ref[...] == lax.broadcasted_iota(jnp.int32, (rows, rows), 0)
    ).astype(jnp.bfloat16)
    q_all = jnp.dot(gather, q_ref[...], preferred_element_type=jnp.float32).astype(jnp.bfloat16)
    g_all = jnp.dot(gather, g_ref[...], preferred_element_type=jnp.float32).astype(jnp.bfloat16)

    @pl.when(pl.program_id(0) == 0)
    def _():
        row = lax.broadcasted_iota(jnp.int32, (rows, cols), 0)
        col = lax.broadcasted_iota(jnp.int32, (rows, cols), 1)
        start = (row // BLOCK) * BLOCK
        in_window = (col >= start) & (col < start + 3 * BLOCK)
        ok = (col >= near_rows) | (in_window & (cv_ref[...] > 0))
        bias_ref[...] = jnp.where(ok, 0.0, -jnp.inf).astype(jnp.float32)

    nt = (((1,), (1,)), ((), ()))
    tn = (((0,), (0,)), ((), ()))
    lane = lax.broadcasted_iota(jnp.int32, (1, LANES), 1)
    k = kv_ref[0]
    v = kv_ref[1]
    att = qg = key_term = value_term = None
    for h in range(LANES // head_dim):
        sel = (lane >= h * head_dim) & (lane < (h + 1) * head_dim)
        q = jnp.where(sel, q_all, jnp.zeros_like(q_all))
        g = jnp.where(sel, g_all, jnp.zeros_like(g_all))
        s = lax.dot_general(q, k, nt, preferred_element_type=jnp.float32) * scale + bias_ref[...]
        m = jnp.max(s, axis=-1, keepdims=True)
        e = jnp.exp(s - m)
        w = e / jnp.sum(e, axis=-1, keepdims=True)
        wb = w.astype(jnp.bfloat16)
        vd = lax.dot_general(g, v, nt, preferred_element_type=jnp.float32)
        rd = jnp.sum(w * vd, axis=-1, keepdims=True)
        sg = (w * (vd - rd) * scale).astype(jnp.bfloat16)
        outs = (
            jnp.dot(wb, v, preferred_element_type=jnp.float32),
            jnp.dot(sg, k, preferred_element_type=jnp.float32),
            lax.dot_general(sg, q_all, tn, preferred_element_type=jnp.float32),
            lax.dot_general(wb, g_all, tn, preferred_element_type=jnp.float32),
        )
        if att is None:
            att, qg, key_term, value_term = outs
        else:
            att, qg, key_term, value_term = (
                jnp.where(sel, new, old) for new, old in zip(outs, (att, qg, key_term, value_term))
            )
    for c, term in enumerate((key_term, value_term)):
        near_ref[c] = term[BLOCK : BLOCK + rows]
        edge_ref[c, :BLOCK] = term[:BLOCK].astype(edge_ref.dtype)
        edge_ref[c, BLOCK:] = term[near_rows - BLOCK : near_rows].astype(edge_ref.dtype)
        far_ref[c] = term[near_rows:].astype(far_ref.dtype)
    att_ref[...] = jnp.dot(
        scatter, att.astype(jnp.bfloat16), preferred_element_type=jnp.float32
    ).astype(att_ref.dtype)
    qg_ref[...] = jnp.dot(
        scatter, qg.astype(jnp.bfloat16), preferred_element_type=jnp.float32
    ).astype(qg_ref.dtype)


def attention(order, queries, out_grad, kv_all, col_valid, head_dim, near_rows):
    rows, features = queries.shape
    cols = kv_all.shape[1]
    row_spec = pl.BlockSpec((rows, LANES), lambda i: (0, i))
    kv_spec = pl.BlockSpec((2, cols, LANES), lambda i: (0, 0, i))
    kernel = lambda *refs: attention_kernel(*refs, head_dim=head_dim, near_rows=near_rows)
    return pl.pallas_call(
        kernel,
        grid=(features // LANES,),
        in_specs=[
            pl.BlockSpec((rows, 1), lambda i: (0, 0)),
            pl.BlockSpec((1, rows), lambda i: (0, 0)),
            row_spec,
            row_spec,
            kv_spec,
            pl.BlockSpec((1, cols), lambda i: (0, 0)),
        ],
        out_specs=[
            row_spec,
            row_spec,
            pl.BlockSpec((2, rows, LANES), lambda i: (0, 0, i)),
            pl.BlockSpec((2, 2 * BLOCK, LANES), lambda i: (0, 0, i)),
            pl.BlockSpec((2, cols - near_rows, LANES), lambda i: (0, 0, i)),
        ],
        out_shape=[
            jax.ShapeDtypeStruct((rows, features), jnp.bfloat16),
            jax.ShapeDtypeStruct((rows, features), jnp.bfloat16),
            jax.ShapeDtypeStruct((2, rows, features), jnp.float32),
            jax.ShapeDtypeStruct((2, 2 * BLOCK, features), jnp.bfloat16),
            jax.ShapeDtypeStruct((2, cols - near_rows, features), jnp.bfloat16),
        ],
        scratch_shapes=[pltpu.VMEM((rows, cols), jnp.float32)],
    )(order.reshape(rows, 1), order.reshape(1, rows), queries, out_grad, kv_all, col_valid)


def xor_permute(value, distance, count):
    return lax.ppermute(value, AXES, [(i, i ^ distance) for i in range(count)])


def per_device(queries, key_table, value_table, out_grad, hilbert_order, key_valid):
    rows_dev, features = queries.shape
    head_dim = D // HEADS
    shard_count = lax.axis_size(AXES)
    shard_bits = shard_count.bit_length() - 1
    my_index = lax.axis_index(AXES)
    permute = hilbert_order[0]
    one_hot = (permute[:, None] == lax.broadcasted_iota(jnp.int32, (rows_dev, rows_dev), 1)).astype(
        jnp.bfloat16
    )

    def take(storage_rows):
        return jnp.dot(one_hot, storage_rows, preferred_element_type=jnp.float32).astype(jnp.bfloat16)

    table_rows = jnp.stack([take(key_table), take(value_table)])
    padded_valid = jnp.pad(key_valid, (BLOCK, BLOCK))
    edge_valid = lax.dynamic_slice_in_dim(padded_valid, my_index * rows_dev, rows_dev + 2 * BLOCK)
    own_valid_rows = edge_valid[BLOCK : BLOCK + rows_dev].astype(jnp.float32)
    own_valid = own_valid_rows[None, :, None]

    up = [(i, i + 1) for i in range(shard_count - 1)]
    down = [(i + 1, i) for i in range(shard_count - 1)]
    before = lax.ppermute(table_rows[:, rows_dev - BLOCK :], AXES, up)
    after = lax.ppermute(table_rows[:, :BLOCK], AXES, down)

    low_bits = shard_bits // 2
    low_count = 2**low_bits
    high_bits = list(range(low_bits, shard_bits))
    sizes = [rows_dev // 2 ** (bit + 1) for bit in range(shard_bits)]

    def pool(bits):
        matrix = np.zeros((sum(sizes[b] for b in bits), rows_dev), np.float32)
        offset = 0
        for b in bits:
            group = 2 ** (b + 1)
            for j in range(sizes[b]):
                matrix[offset + j, j * group : (j + 1) * group] = 1.0 / group
            offset += sizes[b]
        weights = (jnp.asarray(matrix) * own_valid_rows[None, :]).astype(jnp.bfloat16)
        return jnp.stack(
            [
                jnp.dot(weights, table_rows[c], preferred_element_type=jnp.float32).astype(jnp.bfloat16)
                for c in range(2)
            ]
        )

    far_chunks = []
    own_high = pool(high_bits)
    gathered = {}
    offset = 0
    for b in high_bits:
        gathered[b] = [own_high[:, offset : offset + sizes[b]]]
        offset += sizes[b]
    for low in range(1, low_count):
        bit = low.bit_length() - 1
        forwarded = high_bits if low % 2 == 0 else []
        received = xor_permute(pool([bit] + forwarded), low, shard_count)
        far_chunks.append(received[:, : sizes[bit]])
        offset = sizes[bit]
        for b in forwarded:
            gathered[b].append(received[:, offset : offset + sizes[b]])
            offset += sizes[b]
    high_distances = [high << low_bits for high in range(1, 2 ** (shard_bits - low_bits))]
    stacked = {b: jnp.concatenate(gathered[b], axis=1) for b in high_bits}
    second = []
    for distance in high_distances:
        bit = distance.bit_length() - 1
        second.append(xor_permute(stacked[bit], distance, shard_count))
    third = xor_permute(jnp.concatenate(second, axis=1), 1, shard_count)
    far_chunks = far_chunks + second + [third]

    full = jnp.concatenate([before, table_rows, after] + far_chunks, axis=1)
    near_rows = rows_dev + 2 * BLOCK
    cols = full.shape[1]
    col_valid = jnp.concatenate(
        [edge_valid, jnp.ones((cols - near_rows,), edge_valid.dtype)]
    ).reshape(1, cols)
    attended, query_grad, terms, edge_terms, far_terms = attention(
        permute, queries, out_grad, full, col_valid, head_dim, near_rows
    )

    from_next = lax.ppermute(edge_terms[:, :BLOCK], AXES, down).astype(jnp.float32)
    from_prev = lax.ppermute(edge_terms[:, BLOCK:], AXES, up).astype(jnp.float32)

    offset = 0
    direct_terms = []
    for low in range(1, low_count):
        size = sizes[low.bit_length() - 1]
        direct_terms.append(far_terms[:, offset : offset + size])
        offset += size
    half = low_count // 2
    second_rows = [half * sizes[d.bit_length() - 1] for d in high_distances]
    third_terms = far_terms[:, offset + sum(second_rows) :]
    back = xor_permute(third_terms, 1, shard_count).astype(jnp.float32)
    stacked_sums = {}
    pieces = []
    segments = []
    back_offset = 0
    for distance, size in zip(high_distances, second_rows):
        bit = distance.bit_length() - 1
        own = far_terms[:, offset : offset + size].astype(jnp.float32) + back[:, back_offset : back_offset + size]
        offset += size
        back_offset += size
        returned = xor_permute(own.astype(jnp.bfloat16), distance, shard_count)
        pieces.append(returned[:, : sizes[bit]])
        segments.append(bit)
        returned = returned.astype(jnp.float32)
        stacked_sums[bit] = returned if bit not in stacked_sums else stacked_sums[bit] + returned
    for low in range(1, low_count):
        bit = low.bit_length() - 1
        parts = [direct_terms[low - 1]]
        segments.append(bit)
        if low % 2 == 0:
            entry = low // 2
            parts += [
                stacked_sums[b][:, entry * sizes[b] : (entry + 1) * sizes[b]].astype(jnp.bfloat16)
                for b in high_bits
            ]
            segments.extend(high_bits)
        pieces.append(xor_permute(jnp.concatenate(parts, axis=1), low, shard_count))
    expand = np.zeros((rows_dev, sum(sizes[b] for b in segments)), np.float32)
    column = 0
    for bit in segments:
        group = 2 ** (bit + 1)
        for j in range(sizes[bit]):
            expand[j * group : (j + 1) * group, column + j] = 1.0 / group
        column += sizes[bit]
    expand = jnp.asarray(expand, dtype=jnp.bfloat16)
    spread = jnp.stack(
        [
            jnp.dot(expand, jnp.concatenate([piece[c] for piece in pieces], axis=0), preferred_element_type=jnp.float32)
            for c in range(2)
        ]
    )
    edges = jnp.concatenate([from_prev, from_next], axis=1)
    row_grad = terms + edges + own_valid * spread

    def restore(hilbert_rows):
        restored = lax.dot_general(
            one_hot, hilbert_rows, (((0,), (0,)), ((), ())), preferred_element_type=jnp.float32
        )
        return restored.astype(jnp.bfloat16)

    return (attended, query_grad, restore(row_grad[0].astype(jnp.bfloat16)), restore(row_grad[1].astype(jnp.bfloat16)))


def solution(mesh):
    in_specs = (
        P(("parts", "rows", "sub"), "head"),
        P(("parts", "rows", "sub"), "head"),
        P(("parts", "rows", "sub"), "head"),
        P(("parts", "rows", "sub"), "head"),
        P(("parts", "rows", "sub"), None),
        P("parts"),
    )
    out_specs = (
        P(("parts", "rows", "sub"), "head"),
        P(("parts", "rows", "sub"), "head"),
        P(("parts", "rows", "sub"), "head"),
        P(("parts", "rows", "sub"), "head"),
    )
    return jax.shard_map(
        per_device, mesh=mesh, in_specs=in_specs, out_specs=out_specs, check_vma=False
    )
```

```python
import math

import numpy as np

import jax
import jax.numpy as jnp
from jax import lax
from jax.experimental import pallas as pl
from jax.experimental.pallas import tpu as pltpu
from jax.sharding import PartitionSpec as P

D = 512
HEADS = 8
BLOCK = 128
AXES = ("rows", "sub")
LANES = 128


def attention_kernel(
    order_col_ref, order_row_ref, q_ref, g_ref, kv_ref, cv_ref, att_ref, qg_ref, near_ref, edge_ref, far_ref, bias_ref,
    *, head_dim, near_rows
):
    rows = q_ref.shape[0]
    cols = kv_ref.shape[1]
    scale = 1.0 / math.sqrt(head_dim)
    gather = (
        order_col_ref[...] == lax.broadcasted_iota(jnp.int32, (rows, rows), 1)
    ).astype(jnp.bfloat16)
    scatter = (
        order_row_ref[...] == lax.broadcasted_iota(jnp.int32, (rows, rows), 0)
    ).astype(jnp.bfloat16)
    q_all = jnp.dot(gather, q_ref[...], preferred_element_type=jnp.float32).astype(jnp.bfloat16)
    g_all = jnp.dot(gather, g_ref[...], preferred_element_type=jnp.float32).astype(jnp.bfloat16)

    @pl.when(pl.program_id(0) == 0)
    def _():
        row = lax.broadcasted_iota(jnp.int32, (rows, cols), 0)
        col = lax.broadcasted_iota(jnp.int32, (rows, cols), 1)
        start = (row // BLOCK) * BLOCK
        in_window = (col >= start) & (col < start + 3 * BLOCK)
        ok = (col >= near_rows) | (in_window & (cv_ref[...] > 0))
        bias_ref[...] = jnp.where(ok, 0.0, -jnp.inf).astype(jnp.float32)

    nt = (((1,), (1,)), ((), ()))
    tn = (((0,), (0,)), ((), ()))
    lane = lax.broadcasted_iota(jnp.int32, (1, LANES), 1)
    k = kv_ref[0]
    v = kv_ref[1]
    att = qg = key_term = value_term = None
    for h in range(LANES // head_dim):
        sel = (lane >= h * head_dim) & (lane < (h + 1) * head_dim)
        q = jnp.where(sel, q_all, jnp.zeros_like(q_all))
        g = jnp.where(sel, g_all, jnp.zeros_like(g_all))
        s = lax.dot_general(q, k, nt, preferred_element_type=jnp.float32) * scale + bias_ref[...]
        m = jnp.max(s, axis=-1, keepdims=True)
        e = jnp.exp(s - m)
        w = e / jnp.sum(e, axis=-1, keepdims=True)
        wb = w.astype(jnp.bfloat16)
        vd = lax.dot_general(g, v, nt, preferred_element_type=jnp.float32)
        rd = jnp.sum(w * vd, axis=-1, keepdims=True)
        sg = (w * (vd - rd) * scale).astype(jnp.bfloat16)
        outs = (
            jnp.dot(wb, v, preferred_element_type=jnp.float32),
            jnp.dot(sg, k, preferred_element_type=jnp.float32),
            lax.dot_general(sg, q_all, tn, preferred_element_type=jnp.float32),
            lax.dot_general(wb, g_all, tn, preferred_element_type=jnp.float32),
        )
        if att is None:
            att, qg, key_term, value_term = outs
        else:
            att, qg, key_term, value_term = (
                jnp.where(sel, new, old) for new, old in zip(outs, (att, qg, key_term, value_term))
            )
    for c, term in enumerate((key_term, value_term)):
        near_ref[c] = term[BLOCK : BLOCK + rows]
        edge_ref[c, :BLOCK] = term[:BLOCK].astype(edge_ref.dtype)
        edge_ref[c, BLOCK:] = term[near_rows - BLOCK : near_rows].astype(edge_ref.dtype)
        far_ref[c] = term[near_rows:].astype(far_ref.dtype)
    att_ref[...] = jnp.dot(
        scatter, att.astype(jnp.bfloat16), preferred_element_type=jnp.float32
    ).astype(att_ref.dtype)
    qg_ref[...] = jnp.dot(
        scatter, qg.astype(jnp.bfloat16), preferred_element_type=jnp.float32
    ).astype(qg_ref.dtype)


def attention(order, queries, out_grad, kv_all, col_valid, head_dim, near_rows):
    rows, features = queries.shape
    cols = kv_all.shape[1]
    row_spec = pl.BlockSpec((rows, LANES), lambda i: (0, i))
    kv_spec = pl.BlockSpec((2, cols, LANES), lambda i: (0, 0, i))
    kernel = lambda *refs: attention_kernel(*refs, head_dim=head_dim, near_rows=near_rows)
    return pl.pallas_call(
        kernel,
        grid=(features // LANES,),
        in_specs=[
            pl.BlockSpec((rows, 1), lambda i: (0, 0)),
            pl.BlockSpec((1, rows), lambda i: (0, 0)),
            row_spec,
            row_spec,
            kv_spec,
            pl.BlockSpec((1, cols), lambda i: (0, 0)),
        ],
        out_specs=[
            row_spec,
            row_spec,
            pl.BlockSpec((2, rows, LANES), lambda i: (0, 0, i)),
            pl.BlockSpec((2, 2 * BLOCK, LANES), lambda i: (0, 0, i)),
            pl.BlockSpec((2, cols - near_rows, LANES), lambda i: (0, 0, i)),
        ],
        out_shape=[
            jax.ShapeDtypeStruct((rows, features), jnp.bfloat16),
            jax.ShapeDtypeStruct((rows, features), jnp.bfloat16),
            jax.ShapeDtypeStruct((2, rows, features), jnp.float32),
            jax.ShapeDtypeStruct((2, 2 * BLOCK, features), jnp.bfloat16),
            jax.ShapeDtypeStruct((2, cols - near_rows, features), jnp.bfloat16),
        ],
        scratch_shapes=[pltpu.VMEM((rows, cols), jnp.float32)],
    )(order.reshape(rows, 1), order.reshape(1, rows), queries, out_grad, kv_all, col_valid)


def xor_permute(value, distance, count):
    return lax.ppermute(value, AXES, [(i, i ^ distance) for i in range(count)])


def per_device(queries, key_table, value_table, out_grad, hilbert_order, key_valid):
    rows_dev, features = queries.shape
    head_dim = D // HEADS
    shard_count = lax.axis_size(AXES)
    shard_bits = shard_count.bit_length() - 1
    my_index = lax.axis_index(AXES)
    permute = hilbert_order[0]
    one_hot = (permute[:, None] == lax.broadcasted_iota(jnp.int32, (rows_dev, rows_dev), 1)).astype(
        jnp.bfloat16
    )

    def take(storage_rows):
        return jnp.dot(one_hot, storage_rows, preferred_element_type=jnp.float32).astype(jnp.bfloat16)

    table_rows = jnp.stack([take(key_table), take(value_table)])
    padded_valid = jnp.pad(key_valid, (BLOCK, BLOCK))
    edge_valid = lax.dynamic_slice_in_dim(padded_valid, my_index * rows_dev, rows_dev + 2 * BLOCK)
    own_valid_rows = edge_valid[BLOCK : BLOCK + rows_dev].astype(jnp.float32)
    own_valid = own_valid_rows[None, :, None]

    up = [(i, i + 1) for i in range(shard_count - 1)]
    down = [(i + 1, i) for i in range(shard_count - 1)]
    before = lax.ppermute(table_rows[:, rows_dev - BLOCK :], AXES, up)
    after = lax.ppermute(table_rows[:, :BLOCK], AXES, down)

    low_bits = shard_bits // 2
    low_count = 2**low_bits
    high_bits = list(range(low_bits, shard_bits))
    sizes = [rows_dev // 2 ** (bit + 1) for bit in range(shard_bits)]

    def pool(bits):
        matrix = np.zeros((sum(sizes[b] for b in bits), rows_dev), np.float32)
        offset = 0
        for b in bits:
            group = 2 ** (b + 1)
            for j in range(sizes[b]):
                matrix[offset + j, j * group : (j + 1) * group] = 1.0 / group
            offset += sizes[b]
        weights = (jnp.asarray(matrix) * own_valid_rows[None, :]).astype(jnp.bfloat16)
        return jnp.stack(
            [
                jnp.dot(weights, table_rows[c], preferred_element_type=jnp.float32).astype(jnp.bfloat16)
                for c in range(2)
            ]
        )

    far_chunks = []
    own_high = pool(high_bits)
    gathered = {}
    offset = 0
    for b in high_bits:
        gathered[b] = [own_high[:, offset : offset + sizes[b]]]
        offset += sizes[b]
    for low in range(1, low_count):
        bit = low.bit_length() - 1
        received = xor_permute(pool([bit] + high_bits), low, shard_count)
        far_chunks.append(received[:, : sizes[bit]])
        offset = sizes[bit]
        for b in high_bits:
            gathered[b].append(received[:, offset : offset + sizes[b]])
            offset += sizes[b]
    high_distances = [high << low_bits for high in range(1, 2 ** (shard_bits - low_bits))]
    stacked = {b: jnp.concatenate(gathered[b][0::2], axis=1) for b in high_bits}
    second = []
    for distance in high_distances:
        bit = distance.bit_length() - 1
        second.append(xor_permute(stacked[bit], distance, shard_count))
    third = xor_permute(jnp.concatenate(second, axis=1), 1, shard_count)
    far_chunks = far_chunks + second + [third]

    full = jnp.concatenate([before, table_rows, after] + far_chunks, axis=1)
    near_rows = rows_dev + 2 * BLOCK
    cols = full.shape[1]
    col_valid = jnp.concatenate(
        [edge_valid, jnp.ones((cols - near_rows,), edge_valid.dtype)]
    ).reshape(1, cols)
    attended, query_grad, terms, edge_terms, far_terms = attention(
        permute, queries, out_grad, full, col_valid, head_dim, near_rows
    )

    from_next = lax.ppermute(edge_terms[:, :BLOCK], AXES, down).astype(jnp.float32)
    from_prev = lax.ppermute(edge_terms[:, BLOCK:], AXES, up).astype(jnp.float32)

    offset = 0
    direct_terms = []
    for low in range(1, low_count):
        size = sizes[low.bit_length() - 1]
        direct_terms.append(far_terms[:, offset : offset + size])
        offset += size
    half = low_count // 2
    second_rows = [half * sizes[d.bit_length() - 1] for d in high_distances]
    third_terms = far_terms[:, offset + sum(second_rows) :]
    back = xor_permute(third_terms, 1, shard_count).astype(jnp.float32)
    stacked_sums = {}
    pieces = []
    segments = []
    back_offset = 0
    for distance, size in zip(high_distances, second_rows):
        bit = distance.bit_length() - 1
        own = far_terms[:, offset : offset + size].astype(jnp.float32) + back[:, back_offset : back_offset + size]
        offset += size
        back_offset += size
        returned = xor_permute(own.astype(jnp.bfloat16), distance, shard_count)
        pieces.append(returned[:, : sizes[bit]])
        segments.append(bit)
        returned = returned.astype(jnp.float32)
        stacked_sums[bit] = returned if bit not in stacked_sums else stacked_sums[bit] + returned
    for low in range(1, low_count):
        bit = low.bit_length() - 1
        parts = [direct_terms[low - 1]]
        segments.append(bit)
        if low % 2 == 0:
            entry = low // 2
            parts += [
                stacked_sums[b][:, entry * sizes[b] : (entry + 1) * sizes[b]].astype(jnp.bfloat16)
                for b in high_bits
            ]
            segments.extend(high_bits)
        pieces.append(xor_permute(jnp.concatenate(parts, axis=1), low, shard_count))
    expand = np.zeros((rows_dev, sum(sizes[b] for b in segments)), np.float32)
    column = 0
    for bit in segments:
        group = 2 ** (bit + 1)
        for j in range(sizes[bit]):
            expand[j * group : (j + 1) * group, column + j] = 1.0 / group
        column += sizes[bit]
    expand = jnp.asarray(expand, dtype=jnp.bfloat16)
    spread = jnp.stack(
        [
            jnp.dot(expand, jnp.concatenate([piece[c] for piece in pieces], axis=0), preferred_element_type=jnp.float32)
            for c in range(2)
        ]
    )
    edges = jnp.concatenate([from_prev, from_next], axis=1)
    row_grad = terms + edges + own_valid * spread

    def restore(hilbert_rows):
        restored = lax.dot_general(
            one_hot, hilbert_rows, (((0,), (0,)), ((), ())), preferred_element_type=jnp.float32
        )
        return restored.astype(jnp.bfloat16)

    return (attended, query_grad, restore(row_grad[0].astype(jnp.bfloat16)), restore(row_grad[1].astype(jnp.bfloat16)))


def solution(mesh):
    in_specs = (
        P(("parts", "rows", "sub"), "head"),
        P(("parts", "rows", "sub"), "head"),
        P(("parts", "rows", "sub"), "head"),
        P(("parts", "rows", "sub"), "head"),
        P(("parts", "rows", "sub"), None),
        P("parts"),
    )
    out_specs = (
        P(("parts", "rows", "sub"), "head"),
        P(("parts", "rows", "sub"), "head"),
        P(("parts", "rows", "sub"), "head"),
        P(("parts", "rows", "sub"), "head"),
    )
    return jax.shard_map(
        per_device, mesh=mesh, in_specs=in_specs, out_specs=out_specs, check_vma=False
    )
```

```python
import math

import numpy as np

import jax
import jax.numpy as jnp
from jax import lax
from jax.experimental import pallas as pl
from jax.experimental.pallas import tpu as pltpu
from jax.sharding import PartitionSpec as P

D = 512
HEADS = 8
BLOCK = 128
AXES = ("rows", "sub")
LANES = 128


def attention_kernel(
    order_col_ref, order_row_ref, q_ref, g_ref, kv_ref, cv_ref, att_ref, qg_ref, near_ref, edge_ref, far_ref, bias_ref,
    *, head_dim, near_rows
):
    rows = q_ref.shape[0]
    cols = kv_ref.shape[1]
    scale = 1.0 / math.sqrt(head_dim)
    gather = (
        order_col_ref[...] == lax.broadcasted_iota(jnp.int32, (rows, rows), 1)
    ).astype(jnp.bfloat16)
    scatter = (
        order_row_ref[...] == lax.broadcasted_iota(jnp.int32, (rows, rows), 0)
    ).astype(jnp.bfloat16)
    q_all = jnp.dot(gather, q_ref[...], preferred_element_type=jnp.float32).astype(jnp.bfloat16)
    g_all = jnp.dot(gather, g_ref[...], preferred_element_type=jnp.float32).astype(jnp.bfloat16)

    @pl.when(pl.program_id(0) == 0)
    def _():
        row = lax.broadcasted_iota(jnp.int32, (rows, cols), 0)
        col = lax.broadcasted_iota(jnp.int32, (rows, cols), 1)
        start = (row // BLOCK) * BLOCK
        in_window = (col >= start) & (col < start + 3 * BLOCK)
        ok = (col >= near_rows) | (in_window & (cv_ref[...] > 0))
        bias_ref[...] = jnp.where(ok, 0.0, -jnp.inf).astype(jnp.float32)

    nt = (((1,), (1,)), ((), ()))
    tn = (((0,), (0,)), ((), ()))
    lane = lax.broadcasted_iota(jnp.int32, (1, LANES), 1)
    k = kv_ref[0]
    v = kv_ref[1]
    att = qg = key_term = value_term = None
    for h in range(LANES // head_dim):
        sel = (lane >= h * head_dim) & (lane < (h + 1) * head_dim)
        q = jnp.where(sel, q_all, jnp.zeros_like(q_all))
        g = jnp.where(sel, g_all, jnp.zeros_like(g_all))
        s = lax.dot_general(q, k, nt, preferred_element_type=jnp.float32) * scale + bias_ref[...]
        m = jnp.max(s, axis=-1, keepdims=True)
        e = jnp.exp(s - m)
        w = e / jnp.sum(e, axis=-1, keepdims=True)
        wb = w.astype(jnp.bfloat16)
        vd = lax.dot_general(g, v, nt, preferred_element_type=jnp.float32)
        rd = jnp.sum(w * vd, axis=-1, keepdims=True)
        sg = (w * (vd - rd) * scale).astype(jnp.bfloat16)
        outs = (
            jnp.dot(wb, v, preferred_element_type=jnp.float32),
            jnp.dot(sg, k, preferred_element_type=jnp.float32),
            lax.dot_general(sg, q_all, tn, preferred_element_type=jnp.float32),
            lax.dot_general(wb, g_all, tn, preferred_element_type=jnp.float32),
        )
        if att is None:
            att, qg, key_term, value_term = outs
        else:
            att, qg, key_term, value_term = (
                jnp.where(sel, new, old) for new, old in zip(outs, (att, qg, key_term, value_term))
            )
    for c, term in enumerate((key_term, value_term)):
        near_ref[c] = term[BLOCK : BLOCK + rows]
        edge_ref[c, :BLOCK] = term[:BLOCK].astype(edge_ref.dtype)
        edge_ref[c, BLOCK:] = term[near_rows - BLOCK : near_rows].astype(edge_ref.dtype)
        far_ref[c] = term[near_rows:].astype(far_ref.dtype)
    att_ref[...] = jnp.dot(
        scatter, att.astype(jnp.bfloat16), preferred_element_type=jnp.float32
    ).astype(att_ref.dtype)
    qg_ref[...] = jnp.dot(
        scatter, qg.astype(jnp.bfloat16), preferred_element_type=jnp.float32
    ).astype(qg_ref.dtype)


def attention(order, queries, out_grad, kv_all, col_valid, head_dim, near_rows):
    rows, features = queries.shape
    cols = kv_all.shape[1]
    row_spec = pl.BlockSpec((rows, LANES), lambda i: (0, i))
    kv_spec = pl.BlockSpec((2, cols, LANES), lambda i: (0, 0, i))
    kernel = lambda *refs: attention_kernel(*refs, head_dim=head_dim, near_rows=near_rows)
    return pl.pallas_call(
        kernel,
        grid=(features // LANES,),
        in_specs=[
            pl.BlockSpec((rows, 1), lambda i: (0, 0)),
            pl.BlockSpec((1, rows), lambda i: (0, 0)),
            row_spec,
            row_spec,
            kv_spec,
            pl.BlockSpec((1, cols), lambda i: (0, 0)),
        ],
        out_specs=[
            row_spec,
            row_spec,
            pl.BlockSpec((2, rows, LANES), lambda i: (0, 0, i)),
            pl.BlockSpec((2, 2 * BLOCK, LANES), lambda i: (0, 0, i)),
            pl.BlockSpec((2, cols - near_rows, LANES), lambda i: (0, 0, i)),
        ],
        out_shape=[
            jax.ShapeDtypeStruct((rows, features), jnp.bfloat16),
            jax.ShapeDtypeStruct((rows, features), jnp.bfloat16),
            jax.ShapeDtypeStruct((2, rows, features), jnp.float32),
            jax.ShapeDtypeStruct((2, 2 * BLOCK, features), jnp.bfloat16),
            jax.ShapeDtypeStruct((2, cols - near_rows, features), jnp.bfloat16),
        ],
        scratch_shapes=[pltpu.VMEM((rows, cols), jnp.float32)],
    )(order.reshape(rows, 1), order.reshape(1, rows), queries, out_grad, kv_all, col_valid)


def xor_permute(value, distance, count):
    return lax.ppermute(value, AXES, [(i, i ^ distance) for i in range(count)])


def per_device(queries, key_table, value_table, out_grad, hilbert_order, key_valid):
    rows_dev, features = queries.shape
    head_dim = D // HEADS
    shard_count = lax.axis_size(AXES)
    shard_bits = shard_count.bit_length() - 1
    my_index = lax.axis_index(AXES)
    permute = hilbert_order[0]
    one_hot = (permute[:, None] == lax.broadcasted_iota(jnp.int32, (rows_dev, rows_dev), 1)).astype(
        jnp.bfloat16
    )

    def take(storage_rows):
        return jnp.dot(one_hot, storage_rows, preferred_element_type=jnp.float32).astype(jnp.bfloat16)

    table_rows = jnp.stack([take(key_table), take(value_table)])
    padded_valid = jnp.pad(key_valid, (BLOCK, BLOCK))
    edge_valid = lax.dynamic_slice_in_dim(padded_valid, my_index * rows_dev, rows_dev + 2 * BLOCK)
    own_valid_rows = edge_valid[BLOCK : BLOCK + rows_dev].astype(jnp.float32)
    own_valid = own_valid_rows[None, :, None]

    is_even = my_index % 2 == 0
    across = [(i, i + 1) for i in range(1, shard_count - 1, 2)] + [(i, i - 1) for i in range(2, shard_count, 2)]
    first_rows = table_rows[:, :BLOCK]
    last_rows = table_rows[:, rows_dev - BLOCK :]
    crossed = lax.ppermute(jnp.where(is_even, first_rows, last_rows), AXES, across)
    beside = jnp.where(is_even, last_rows, first_rows)

    low_bits = shard_bits // 2
    low_count = 2**low_bits
    high_bits = list(range(low_bits, shard_bits))
    sizes = [rows_dev // 2 ** (bit + 1) for bit in range(shard_bits)]

    def pool(bits):
        matrix = np.zeros((sum(sizes[b] for b in bits), rows_dev), np.float32)
        offset = 0
        for b in bits:
            group = 2 ** (b + 1)
            for j in range(sizes[b]):
                matrix[offset + j, j * group : (j + 1) * group] = 1.0 / group
            offset += sizes[b]
        weights = (jnp.asarray(matrix) * own_valid_rows[None, :]).astype(jnp.bfloat16)
        return jnp.stack(
            [
                jnp.dot(weights, table_rows[c], preferred_element_type=jnp.float32).astype(jnp.bfloat16)
                for c in range(2)
            ]
        )

    far_chunks = []
    own_high = pool(high_bits)
    gathered = {}
    offset = 0
    for b in high_bits:
        gathered[b] = [own_high[:, offset : offset + sizes[b]]]
        offset += sizes[b]
    for low in range(1, low_count):
        bit = low.bit_length() - 1
        payload = pool([bit] + high_bits)
        if low == 1:
            received = xor_permute(jnp.concatenate([payload, beside], axis=1), low, shard_count)
            sibling_rows = received[:, payload.shape[1] :]
            received = received[:, : payload.shape[1]]
        else:
            received = xor_permute(payload, low, shard_count)
        far_chunks.append(received[:, : sizes[bit]])
        offset = sizes[bit]
        for b in high_bits:
            gathered[b].append(received[:, offset : offset + sizes[b]])
            offset += sizes[b]
    high_distances = [high << low_bits for high in range(1, 2 ** (shard_bits - low_bits))]
    stacked = {b: jnp.concatenate(gathered[b][0::2], axis=1) for b in high_bits}
    second = []
    for distance in high_distances:
        bit = distance.bit_length() - 1
        second.append(xor_permute(stacked[bit], distance, shard_count))
    third = xor_permute(jnp.concatenate(second, axis=1), 1, shard_count)
    far_chunks = far_chunks + second + [third]

    before = jnp.where(is_even, crossed, sibling_rows)
    after = jnp.where(is_even, sibling_rows, crossed)
    full = jnp.concatenate([before, table_rows, after] + far_chunks, axis=1)
    near_rows = rows_dev + 2 * BLOCK
    cols = full.shape[1]
    col_valid = jnp.concatenate(
        [edge_valid, jnp.ones((cols - near_rows,), edge_valid.dtype)]
    ).reshape(1, cols)
    attended, query_grad, terms, edge_terms, far_terms = attention(
        permute, queries, out_grad, full, col_valid, head_dim, near_rows
    )

    prev_edge = edge_terms[:, :BLOCK]
    next_edge = edge_terms[:, BLOCK:]
    crossed_back = lax.ppermute(jnp.where(is_even, prev_edge, next_edge), AXES, across).astype(jnp.float32)
    beside_back = jnp.where(is_even, next_edge, prev_edge)

    offset = 0
    direct_terms = []
    for low in range(1, low_count):
        size = sizes[low.bit_length() - 1]
        direct_terms.append(far_terms[:, offset : offset + size])
        offset += size
    half = low_count // 2
    second_rows = [half * sizes[d.bit_length() - 1] for d in high_distances]
    third_terms = far_terms[:, offset + sum(second_rows) :]
    back = xor_permute(third_terms, 1, shard_count).astype(jnp.float32)
    stacked_sums = {}
    pieces = []
    segments = []
    back_offset = 0
    for distance, size in zip(high_distances, second_rows):
        bit = distance.bit_length() - 1
        own = far_terms[:, offset : offset + size].astype(jnp.float32) + back[:, back_offset : back_offset + size]
        offset += size
        back_offset += size
        returned = xor_permute(own.astype(jnp.bfloat16), distance, shard_count)
        pieces.append(returned[:, : sizes[bit]])
        segments.append(bit)
        returned = returned.astype(jnp.float32)
        stacked_sums[bit] = returned if bit not in stacked_sums else stacked_sums[bit] + returned
    for low in range(1, low_count):
        bit = low.bit_length() - 1
        parts = [direct_terms[low - 1]]
        segments.append(bit)
        if low % 2 == 0:
            entry = low // 2
            parts += [
                stacked_sums[b][:, entry * sizes[b] : (entry + 1) * sizes[b]].astype(jnp.bfloat16)
                for b in high_bits
            ]
            segments.extend(high_bits)
        if low == 1:
            received = xor_permute(jnp.concatenate(parts + [beside_back], axis=1), low, shard_count)
            sibling_back = received[:, -BLOCK:].astype(jnp.float32)
            pieces.append(received[:, :-BLOCK])
        else:
            pieces.append(xor_permute(jnp.concatenate(parts, axis=1), low, shard_count))
    expand = np.zeros((rows_dev, sum(sizes[b] for b in segments)), np.float32)
    column = 0
    for bit in segments:
        group = 2 ** (bit + 1)
        for j in range(sizes[bit]):
            expand[j * group : (j + 1) * group, column + j] = 1.0 / group
        column += sizes[bit]
    expand = jnp.asarray(expand, dtype=jnp.bfloat16)
    spread = jnp.stack(
        [
            jnp.dot(expand, jnp.concatenate([piece[c] for piece in pieces], axis=0), preferred_element_type=jnp.float32)
            for c in range(2)
        ]
    )
    from_prev = jnp.where(is_even, crossed_back, sibling_back)
    from_next = jnp.where(is_even, sibling_back, crossed_back)
    edges = jnp.concatenate([from_prev, from_next], axis=1)
    row_grad = terms + edges + own_valid * spread

    def restore(hilbert_rows):
        restored = lax.dot_general(
            one_hot, hilbert_rows, (((0,), (0,)), ((), ())), preferred_element_type=jnp.float32
        )
        return restored.astype(jnp.bfloat16)

    return (attended, query_grad, restore(row_grad[0].astype(jnp.bfloat16)), restore(row_grad[1].astype(jnp.bfloat16)))


def solution(mesh):
    in_specs = (
        P(("parts", "rows", "sub"), "head"),
        P(("parts", "rows", "sub"), "head"),
        P(("parts", "rows", "sub"), "head"),
        P(("parts", "rows", "sub"), "head"),
        P(("parts", "rows", "sub"), None),
        P("parts"),
    )
    out_specs = (
        P(("parts", "rows", "sub"), "head"),
        P(("parts", "rows", "sub"), "head"),
        P(("parts", "rows", "sub"), "head"),
        P(("parts", "rows", "sub"), "head"),
    )
    return jax.shard_map(
        per_device, mesh=mesh, in_specs=in_specs, out_specs=out_specs, check_vma=False
    )
```

```python
import math

import numpy as np

import jax
import jax.numpy as jnp
from jax import lax
from jax.experimental import pallas as pl
from jax.experimental.pallas import tpu as pltpu
from jax.sharding import PartitionSpec as P

D = 512
HEADS = 8
BLOCK = 128
AXES = ("rows", "sub")
LANES = 128


def attention_kernel(
    order_col_ref, order_row_ref, q_ref, g_ref, kv_ref, cv_ref, att_ref, qg_ref, near_ref, edge_ref, far_ref, bias_ref,
    *, head_dim, near_rows
):
    rows = q_ref.shape[0]
    cols = kv_ref.shape[1]
    scale = 1.0 / math.sqrt(head_dim)
    gather = (
        order_col_ref[...] == lax.broadcasted_iota(jnp.int32, (rows, rows), 1)
    ).astype(jnp.bfloat16)
    scatter = (
        order_row_ref[...] == lax.broadcasted_iota(jnp.int32, (rows, rows), 0)
    ).astype(jnp.bfloat16)
    q_all = jnp.dot(gather, q_ref[...], preferred_element_type=jnp.float32).astype(jnp.bfloat16)
    g_all = jnp.dot(gather, g_ref[...], preferred_element_type=jnp.float32).astype(jnp.bfloat16)

    @pl.when(pl.program_id(0) == 0)
    def _():
        row = lax.broadcasted_iota(jnp.int32, (rows, cols), 0)
        col = lax.broadcasted_iota(jnp.int32, (rows, cols), 1)
        start = (row // BLOCK) * BLOCK
        in_window = (col >= start) & (col < start + 3 * BLOCK)
        ok = (col >= near_rows) | (in_window & (cv_ref[...] > 0))
        bias_ref[...] = jnp.where(ok, 0.0, -jnp.inf).astype(jnp.float32)

    nt = (((1,), (1,)), ((), ()))
    tn = (((0,), (0,)), ((), ()))
    lane = lax.broadcasted_iota(jnp.int32, (1, LANES), 1)
    k = kv_ref[0]
    v = kv_ref[1]
    att = qg = key_term = value_term = None
    for h in range(LANES // head_dim):
        sel = (lane >= h * head_dim) & (lane < (h + 1) * head_dim)
        q = jnp.where(sel, q_all, jnp.zeros_like(q_all))
        g = jnp.where(sel, g_all, jnp.zeros_like(g_all))
        s = lax.dot_general(q, k, nt, preferred_element_type=jnp.float32) * scale + bias_ref[...]
        m = jnp.max(s, axis=-1, keepdims=True)
        e = jnp.exp(s - m)
        w = e / jnp.sum(e, axis=-1, keepdims=True)
        wb = w.astype(jnp.bfloat16)
        vd = lax.dot_general(g, v, nt, preferred_element_type=jnp.float32)
        rd = jnp.sum(w * vd, axis=-1, keepdims=True)
        sg = (w * (vd - rd) * scale).astype(jnp.bfloat16)
        outs = (
            jnp.dot(wb, v, preferred_element_type=jnp.float32),
            jnp.dot(sg, k, preferred_element_type=jnp.float32),
            lax.dot_general(sg, q_all, tn, preferred_element_type=jnp.float32),
            lax.dot_general(wb, g_all, tn, preferred_element_type=jnp.float32),
        )
        if att is None:
            att, qg, key_term, value_term = outs
        else:
            att, qg, key_term, value_term = (
                jnp.where(sel, new, old) for new, old in zip(outs, (att, qg, key_term, value_term))
            )
    for c, term in enumerate((key_term, value_term)):
        near_ref[c] = term[BLOCK : BLOCK + rows]
        edge_ref[c, :BLOCK] = term[:BLOCK].astype(edge_ref.dtype)
        edge_ref[c, BLOCK:] = term[near_rows - BLOCK : near_rows].astype(edge_ref.dtype)
        far_ref[c] = term[near_rows:].astype(far_ref.dtype)
    att_ref[...] = jnp.dot(
        scatter, att.astype(jnp.bfloat16), preferred_element_type=jnp.float32
    ).astype(att_ref.dtype)
    qg_ref[...] = jnp.dot(
        scatter, qg.astype(jnp.bfloat16), preferred_element_type=jnp.float32
    ).astype(qg_ref.dtype)


def attention(order, queries, out_grad, kv_all, col_valid, head_dim, near_rows):
    rows, features = queries.shape
    cols = kv_all.shape[1]
    row_spec = pl.BlockSpec((rows, LANES), lambda i: (0, i))
    kv_spec = pl.BlockSpec((2, cols, LANES), lambda i: (0, 0, i))
    kernel = lambda *refs: attention_kernel(*refs, head_dim=head_dim, near_rows=near_rows)
    return pl.pallas_call(
        kernel,
        grid=(features // LANES,),
        in_specs=[
            pl.BlockSpec((rows, 1), lambda i: (0, 0)),
            pl.BlockSpec((1, rows), lambda i: (0, 0)),
            row_spec,
            row_spec,
            kv_spec,
            pl.BlockSpec((1, cols), lambda i: (0, 0)),
        ],
        out_specs=[
            row_spec,
            row_spec,
            pl.BlockSpec((2, rows, LANES), lambda i: (0, 0, i)),
            pl.BlockSpec((2, 2 * BLOCK, LANES), lambda i: (0, 0, i)),
            pl.BlockSpec((2, cols - near_rows, LANES), lambda i: (0, 0, i)),
        ],
        out_shape=[
            jax.ShapeDtypeStruct((rows, features), jnp.bfloat16),
            jax.ShapeDtypeStruct((rows, features), jnp.bfloat16),
            jax.ShapeDtypeStruct((2, rows, features), jnp.float32),
            jax.ShapeDtypeStruct((2, 2 * BLOCK, features), jnp.bfloat16),
            jax.ShapeDtypeStruct((2, cols - near_rows, features), jnp.bfloat16),
        ],
        scratch_shapes=[pltpu.VMEM((rows, cols), jnp.float32)],
    )(order.reshape(rows, 1), order.reshape(1, rows), queries, out_grad, kv_all, col_valid)


def xor_permute(value, distance, count):
    return lax.ppermute(value, AXES, [(i, i ^ distance) for i in range(count)])


def per_device(queries, key_table, value_table, out_grad, hilbert_order, key_valid):
    rows_dev, features = queries.shape
    head_dim = D // HEADS
    shard_count = lax.axis_size(AXES)
    shard_bits = shard_count.bit_length() - 1
    my_index = lax.axis_index(AXES)
    permute = hilbert_order[0]
    one_hot = (permute[:, None] == lax.broadcasted_iota(jnp.int32, (rows_dev, rows_dev), 1)).astype(
        jnp.bfloat16
    )

    def take(storage_rows):
        return jnp.dot(one_hot, storage_rows, preferred_element_type=jnp.float32).astype(jnp.bfloat16)

    table_rows = jnp.stack([take(key_table), take(value_table)])
    padded_valid = jnp.pad(key_valid, (BLOCK, BLOCK))
    edge_valid = lax.dynamic_slice_in_dim(padded_valid, my_index * rows_dev, rows_dev + 2 * BLOCK)
    own_valid_rows = edge_valid[BLOCK : BLOCK + rows_dev].astype(jnp.float32)
    own_valid = own_valid_rows[None, :, None]

    up = [(i, i + 1) for i in range(shard_count - 1)]
    down = [(i + 1, i) for i in range(shard_count - 1)]
    before = lax.ppermute(table_rows[:, rows_dev - BLOCK :], AXES, up)
    after = lax.ppermute(table_rows[:, :BLOCK], AXES, down)

    low_bits = 1
    low_count = 2**low_bits
    high_bits = list(range(low_bits, shard_bits))
    sizes = [rows_dev // 2 ** (bit + 1) for bit in range(shard_bits)]

    def pool(bits):
        matrix = np.zeros((sum(sizes[b] for b in bits), rows_dev), np.float32)
        offset = 0
        for b in bits:
            group = 2 ** (b + 1)
            for j in range(sizes[b]):
                matrix[offset + j, j * group : (j + 1) * group] = 1.0 / group
            offset += sizes[b]
        weights = (jnp.asarray(matrix) * own_valid_rows[None, :]).astype(jnp.bfloat16)
        return jnp.stack(
            [
                jnp.dot(weights, table_rows[c], preferred_element_type=jnp.float32).astype(jnp.bfloat16)
                for c in range(2)
            ]
        )

    far_chunks = []
    own_high = pool(high_bits)
    gathered = {}
    offset = 0
    for b in high_bits:
        gathered[b] = [own_high[:, offset : offset + sizes[b]]]
        offset += sizes[b]
    for low in range(1, low_count):
        bit = low.bit_length() - 1
        received = xor_permute(pool([bit] + high_bits), low, shard_count)
        far_chunks.append(received[:, : sizes[bit]])
        offset = sizes[bit]
        for b in high_bits:
            gathered[b].append(received[:, offset : offset + sizes[b]])
            offset += sizes[b]
    high_distances = [high << low_bits for high in range(1, 2 ** (shard_bits - low_bits))]
    stacked = {b: jnp.concatenate(gathered[b][0::2], axis=1) for b in high_bits}
    second = []
    for distance in high_distances:
        bit = distance.bit_length() - 1
        second.append(xor_permute(stacked[bit], distance, shard_count))
    third = xor_permute(jnp.concatenate(second, axis=1), 1, shard_count)
    far_chunks = far_chunks + second + [third]

    full = jnp.concatenate([before, table_rows, after] + far_chunks, axis=1)
    near_rows = rows_dev + 2 * BLOCK
    cols = full.shape[1]
    col_valid = jnp.concatenate(
        [edge_valid, jnp.ones((cols - near_rows,), edge_valid.dtype)]
    ).reshape(1, cols)
    attended, query_grad, terms, edge_terms, far_terms = attention(
        permute, queries, out_grad, full, col_valid, head_dim, near_rows
    )

    from_next = lax.ppermute(edge_terms[:, :BLOCK], AXES, down).astype(jnp.float32)
    from_prev = lax.ppermute(edge_terms[:, BLOCK:], AXES, up).astype(jnp.float32)

    offset = 0
    direct_terms = []
    for low in range(1, low_count):
        size = sizes[low.bit_length() - 1]
        direct_terms.append(far_terms[:, offset : offset + size])
        offset += size
    half = low_count // 2
    second_rows = [half * sizes[d.bit_length() - 1] for d in high_distances]
    third_terms = far_terms[:, offset + sum(second_rows) :]
    back = xor_permute(third_terms, 1, shard_count).astype(jnp.float32)
    stacked_sums = {}
    pieces = []
    segments = []
    back_offset = 0
    for distance, size in zip(high_distances, second_rows):
        bit = distance.bit_length() - 1
        own = far_terms[:, offset : offset + size].astype(jnp.float32) + back[:, back_offset : back_offset + size]
        offset += size
        back_offset += size
        returned = xor_permute(own.astype(jnp.bfloat16), distance, shard_count)
        pieces.append(returned[:, : sizes[bit]])
        segments.append(bit)
        returned = returned.astype(jnp.float32)
        stacked_sums[bit] = returned if bit not in stacked_sums else stacked_sums[bit] + returned
    for low in range(1, low_count):
        bit = low.bit_length() - 1
        parts = [direct_terms[low - 1]]
        segments.append(bit)
        if low % 2 == 0:
            entry = low // 2
            parts += [
                stacked_sums[b][:, entry * sizes[b] : (entry + 1) * sizes[b]].astype(jnp.bfloat16)
                for b in high_bits
            ]
            segments.extend(high_bits)
        pieces.append(xor_permute(jnp.concatenate(parts, axis=1), low, shard_count))
    expand = np.zeros((rows_dev, sum(sizes[b] for b in segments)), np.float32)
    column = 0
    for bit in segments:
        group = 2 ** (bit + 1)
        for j in range(sizes[bit]):
            expand[j * group : (j + 1) * group, column + j] = 1.0 / group
        column += sizes[bit]
    expand = jnp.asarray(expand, dtype=jnp.bfloat16)
    spread = jnp.stack(
        [
            jnp.dot(expand, jnp.concatenate([piece[c] for piece in pieces], axis=0), preferred_element_type=jnp.float32)
            for c in range(2)
        ]
    )
    edges = jnp.concatenate([from_prev, from_next], axis=1)
    row_grad = terms + edges + own_valid * spread

    def restore(hilbert_rows):
        restored = lax.dot_general(
            one_hot, hilbert_rows, (((0,), (0,)), ((), ())), preferred_element_type=jnp.float32
        )
        return restored.astype(jnp.bfloat16)

    return (attended, query_grad, restore(row_grad[0].astype(jnp.bfloat16)), restore(row_grad[1].astype(jnp.bfloat16)))


def solution(mesh):
    in_specs = (
        P(("parts", "rows", "sub"), "head"),
        P(("parts", "rows", "sub"), "head"),
        P(("parts", "rows", "sub"), "head"),
        P(("parts", "rows", "sub"), "head"),
        P(("parts", "rows", "sub"), None),
        P("parts"),
    )
    out_specs = (
        P(("parts", "rows", "sub"), "head"),
        P(("parts", "rows", "sub"), "head"),
        P(("parts", "rows", "sub"), "head"),
        P(("parts", "rows", "sub"), "head"),
    )
    return jax.shard_map(
        per_device, mesh=mesh, in_specs=in_specs, out_specs=out_specs, check_vma=False
    )
```

```python
import math

import numpy as np

import jax
import jax.numpy as jnp
from jax import lax
from jax.experimental import pallas as pl
from jax.experimental.pallas import tpu as pltpu
from jax.sharding import PartitionSpec as P

D = 512
HEADS = 8
BLOCK = 128
AXES = ("rows", "sub")
LANES = 128


def attention_kernel(
    order_col_ref, order_row_ref, q_ref, g_ref, kv_ref, cv_ref, att_ref, qg_ref, near_ref, edge_ref, far_ref, bias_ref,
    *, head_dim, near_rows
):
    rows = q_ref.shape[0]
    cols = kv_ref.shape[1]
    scale = 1.0 / math.sqrt(head_dim)
    gather = (
        order_col_ref[...] == lax.broadcasted_iota(jnp.int32, (rows, rows), 1)
    ).astype(jnp.bfloat16)
    scatter = (
        order_row_ref[...] == lax.broadcasted_iota(jnp.int32, (rows, rows), 0)
    ).astype(jnp.bfloat16)
    q_all = jnp.dot(gather, q_ref[...], preferred_element_type=jnp.float32).astype(jnp.bfloat16)
    g_all = jnp.dot(gather, g_ref[...], preferred_element_type=jnp.float32).astype(jnp.bfloat16)

    @pl.when(pl.program_id(0) == 0)
    def _():
        row = lax.broadcasted_iota(jnp.int32, (rows, cols), 0)
        col = lax.broadcasted_iota(jnp.int32, (rows, cols), 1)
        start = (row // BLOCK) * BLOCK
        in_window = (col >= start) & (col < start + 3 * BLOCK)
        ok = (col >= near_rows) | (in_window & (cv_ref[...] > 0))
        bias_ref[...] = jnp.where(ok, 0.0, -jnp.inf).astype(jnp.float32)

    nt = (((1,), (1,)), ((), ()))
    tn = (((0,), (0,)), ((), ()))
    lane = lax.broadcasted_iota(jnp.int32, (1, LANES), 1)
    att_parts = []
    qg_parts = []
    for pair in range(q_ref.shape[1] // LANES):
        ls = slice(pair * LANES, (pair + 1) * LANES)
        q_pair = q_all[:, ls]
        g_pair = g_all[:, ls]
        k = kv_ref[0, :, ls]
        v = kv_ref[1, :, ls]
        att = qg = key_term = value_term = None
        for h in range(LANES // head_dim):
            sel = (lane >= h * head_dim) & (lane < (h + 1) * head_dim)
            q = jnp.where(sel, q_pair, jnp.zeros_like(q_pair))
            g = jnp.where(sel, g_pair, jnp.zeros_like(g_pair))
            s = lax.dot_general(q, k, nt, preferred_element_type=jnp.float32) * scale + bias_ref[...]
            m = jnp.max(s, axis=-1, keepdims=True)
            e = jnp.exp(s - m)
            w = e / jnp.sum(e, axis=-1, keepdims=True)
            wb = w.astype(jnp.bfloat16)
            vd = lax.dot_general(g, v, nt, preferred_element_type=jnp.float32)
            rd = jnp.sum(w * vd, axis=-1, keepdims=True)
            sg = (w * (vd - rd) * scale).astype(jnp.bfloat16)
            outs = (
                jnp.dot(wb, v, preferred_element_type=jnp.float32),
                jnp.dot(sg, k, preferred_element_type=jnp.float32),
                lax.dot_general(sg, q_pair, tn, preferred_element_type=jnp.float32),
                lax.dot_general(wb, g_pair, tn, preferred_element_type=jnp.float32),
            )
            if att is None:
                att, qg, key_term, value_term = outs
            else:
                att, qg, key_term, value_term = (
                    jnp.where(sel, new, old) for new, old in zip(outs, (att, qg, key_term, value_term))
                )
        for c, term in enumerate((key_term, value_term)):
            near_ref[c, :, ls] = term[BLOCK : BLOCK + rows]
            edge_ref[c, :BLOCK, ls] = term[:BLOCK].astype(edge_ref.dtype)
            edge_ref[c, BLOCK:, ls] = term[near_rows - BLOCK : near_rows].astype(edge_ref.dtype)
            far_ref[c, :, ls] = term[near_rows:].astype(far_ref.dtype)
        att_parts.append(att.astype(jnp.bfloat16))
        qg_parts.append(qg.astype(jnp.bfloat16))
    att_ref[...] = jnp.dot(
        scatter, jnp.concatenate(att_parts, axis=1), preferred_element_type=jnp.float32
    ).astype(att_ref.dtype)
    qg_ref[...] = jnp.dot(
        scatter, jnp.concatenate(qg_parts, axis=1), preferred_element_type=jnp.float32
    ).astype(qg_ref.dtype)


def attention(order, queries, out_grad, kv_all, col_valid, head_dim, near_rows):
    rows, features = queries.shape
    cols = kv_all.shape[1]
    width = 2 * LANES if features % (2 * LANES) == 0 else LANES
    row_spec = pl.BlockSpec((rows, width), lambda i: (0, i))
    kv_spec = pl.BlockSpec((2, cols, width), lambda i: (0, 0, i))
    kernel = lambda *refs: attention_kernel(*refs, head_dim=head_dim, near_rows=near_rows)
    return pl.pallas_call(
        kernel,
        grid=(features // width,),
        in_specs=[
            pl.BlockSpec((rows, 1), lambda i: (0, 0)),
            pl.BlockSpec((1, rows), lambda i: (0, 0)),
            row_spec,
            row_spec,
            kv_spec,
            pl.BlockSpec((1, cols), lambda i: (0, 0)),
        ],
        out_specs=[
            row_spec,
            row_spec,
            pl.BlockSpec((2, rows, width), lambda i: (0, 0, i)),
            pl.BlockSpec((2, 2 * BLOCK, width), lambda i: (0, 0, i)),
            pl.BlockSpec((2, cols - near_rows, width), lambda i: (0, 0, i)),
        ],
        out_shape=[
            jax.ShapeDtypeStruct((rows, features), jnp.bfloat16),
            jax.ShapeDtypeStruct((rows, features), jnp.bfloat16),
            jax.ShapeDtypeStruct((2, rows, features), jnp.float32),
            jax.ShapeDtypeStruct((2, 2 * BLOCK, features), jnp.bfloat16),
            jax.ShapeDtypeStruct((2, cols - near_rows, features), jnp.bfloat16),
        ],
        scratch_shapes=[pltpu.VMEM((rows, cols), jnp.float32)],
    )(order.reshape(rows, 1), order.reshape(1, rows), queries, out_grad, kv_all, col_valid)


def xor_permute(value, distance, count):
    return lax.ppermute(value, AXES, [(i, i ^ distance) for i in range(count)])


def per_device(queries, key_table, value_table, out_grad, hilbert_order, key_valid):
    rows_dev, features = queries.shape
    head_dim = D // HEADS
    shard_count = lax.axis_size(AXES)
    shard_bits = shard_count.bit_length() - 1
    my_index = lax.axis_index(AXES)
    permute = hilbert_order[0]
    one_hot = (permute[:, None] == lax.broadcasted_iota(jnp.int32, (rows_dev, rows_dev), 1)).astype(
        jnp.bfloat16
    )

    def take(storage_rows):
        return jnp.dot(one_hot, storage_rows, preferred_element_type=jnp.float32).astype(jnp.bfloat16)

    table_rows = jnp.stack([take(key_table), take(value_table)])
    padded_valid = jnp.pad(key_valid, (BLOCK, BLOCK))
    edge_valid = lax.dynamic_slice_in_dim(padded_valid, my_index * rows_dev, rows_dev + 2 * BLOCK)
    own_valid_rows = edge_valid[BLOCK : BLOCK + rows_dev].astype(jnp.float32)
    own_valid = own_valid_rows[None, :, None]

    up = [(i, i + 1) for i in range(shard_count - 1)]
    down = [(i + 1, i) for i in range(shard_count - 1)]
    before = lax.ppermute(table_rows[:, rows_dev - BLOCK :], AXES, up)
    after = lax.ppermute(table_rows[:, :BLOCK], AXES, down)

    low_bits = shard_bits // 2
    low_count = 2**low_bits
    high_bits = list(range(low_bits, shard_bits))
    sizes = [rows_dev // 2 ** (bit + 1) for bit in range(shard_bits)]

    def pool(bits):
        matrix = np.zeros((sum(sizes[b] for b in bits), rows_dev), np.float32)
        offset = 0
        for b in bits:
            group = 2 ** (b + 1)
            for j in range(sizes[b]):
                matrix[offset + j, j * group : (j + 1) * group] = 1.0 / group
            offset += sizes[b]
        weights = (jnp.asarray(matrix) * own_valid_rows[None, :]).astype(jnp.bfloat16)
        return jnp.stack(
            [
                jnp.dot(weights, table_rows[c], preferred_element_type=jnp.float32).astype(jnp.bfloat16)
                for c in range(2)
            ]
        )

    far_chunks = []
    own_high = pool(high_bits)
    gathered = {}
    offset = 0
    for b in high_bits:
        gathered[b] = [own_high[:, offset : offset + sizes[b]]]
        offset += sizes[b]
    for low in range(1, low_count):
        bit = low.bit_length() - 1
        received = xor_permute(pool([bit] + high_bits), low, shard_count)
        far_chunks.append(received[:, : sizes[bit]])
        offset = sizes[bit]
        for b in high_bits:
            gathered[b].append(received[:, offset : offset + sizes[b]])
            offset += sizes[b]
    high_distances = [high << low_bits for high in range(1, 2 ** (shard_bits - low_bits))]
    stacked = {b: jnp.concatenate(gathered[b][0::2], axis=1) for b in high_bits}
    second = []
    for distance in high_distances:
        bit = distance.bit_length() - 1
        second.append(xor_permute(stacked[bit], distance, shard_count))
    third = xor_permute(jnp.concatenate(second, axis=1), 1, shard_count)
    far_chunks = far_chunks + second + [third]

    full = jnp.concatenate([before, table_rows, after] + far_chunks, axis=1)
    near_rows = rows_dev + 2 * BLOCK
    cols = full.shape[1]
    col_valid = jnp.concatenate(
        [edge_valid, jnp.ones((cols - near_rows,), edge_valid.dtype)]
    ).reshape(1, cols)
    attended, query_grad, terms, edge_terms, far_terms = attention(
        permute, queries, out_grad, full, col_valid, head_dim, near_rows
    )

    from_next = lax.ppermute(edge_terms[:, :BLOCK], AXES, down).astype(jnp.float32)
    from_prev = lax.ppermute(edge_terms[:, BLOCK:], AXES, up).astype(jnp.float32)

    offset = 0
    direct_terms = []
    for low in range(1, low_count):
        size = sizes[low.bit_length() - 1]
        direct_terms.append(far_terms[:, offset : offset + size])
        offset += size
    half = low_count // 2
    second_rows = [half * sizes[d.bit_length() - 1] for d in high_distances]
    third_terms = far_terms[:, offset + sum(second_rows) :]
    back = xor_permute(third_terms, 1, shard_count).astype(jnp.float32)
    stacked_sums = {}
    pieces = []
    segments = []
    back_offset = 0
    for distance, size in zip(high_distances, second_rows):
        bit = distance.bit_length() - 1
        own = far_terms[:, offset : offset + size].astype(jnp.float32) + back[:, back_offset : back_offset + size]
        offset += size
        back_offset += size
        returned = xor_permute(own.astype(jnp.bfloat16), distance, shard_count)
        pieces.append(returned[:, : sizes[bit]])
        segments.append(bit)
        returned = returned.astype(jnp.float32)
        stacked_sums[bit] = returned if bit not in stacked_sums else stacked_sums[bit] + returned
    for low in range(1, low_count):
        bit = low.bit_length() - 1
        parts = [direct_terms[low - 1]]
        segments.append(bit)
        if low % 2 == 0:
            entry = low // 2
            parts += [
                stacked_sums[b][:, entry * sizes[b] : (entry + 1) * sizes[b]].astype(jnp.bfloat16)
                for b in high_bits
            ]
            segments.extend(high_bits)
        pieces.append(xor_permute(jnp.concatenate(parts, axis=1), low, shard_count))
    expand = np.zeros((rows_dev, sum(sizes[b] for b in segments)), np.float32)
    column = 0
    for bit in segments:
        group = 2 ** (bit + 1)
        for j in range(sizes[bit]):
            expand[j * group : (j + 1) * group, column + j] = 1.0 / group
        column += sizes[bit]
    expand = jnp.asarray(expand, dtype=jnp.bfloat16)
    spread = jnp.stack(
        [
            jnp.dot(expand, jnp.concatenate([piece[c] for piece in pieces], axis=0), preferred_element_type=jnp.float32)
            for c in range(2)
        ]
    )
    edges = jnp.concatenate([from_prev, from_next], axis=1)
    row_grad = terms + edges + own_valid * spread

    def restore(hilbert_rows):
        restored = lax.dot_general(
            one_hot, hilbert_rows, (((0,), (0,)), ((), ())), preferred_element_type=jnp.float32
        )
        return restored.astype(jnp.bfloat16)

    return (attended, query_grad, restore(row_grad[0].astype(jnp.bfloat16)), restore(row_grad[1].astype(jnp.bfloat16)))


def solution(mesh):
    in_specs = (
        P(("parts", "rows", "sub"), "head"),
        P(("parts", "rows", "sub"), "head"),
        P(("parts", "rows", "sub"), "head"),
        P(("parts", "rows", "sub"), "head"),
        P(("parts", "rows", "sub"), None),
        P("parts"),
    )
    out_specs = (
        P(("parts", "rows", "sub"), "head"),
        P(("parts", "rows", "sub"), "head"),
        P(("parts", "rows", "sub"), "head"),
        P(("parts", "rows", "sub"), "head"),
    )
    return jax.shard_map(
        per_device, mesh=mesh, in_specs=in_specs, out_specs=out_specs, check_vma=False
    )
```

```python
import math

import numpy as np

import jax
import jax.numpy as jnp
from jax import lax
from jax.experimental import pallas as pl
from jax.experimental.pallas import tpu as pltpu
from jax.sharding import PartitionSpec as P

D = 512
HEADS = 8
BLOCK = 128
AXES = ("rows", "sub")
LANES = 128


def attention_kernel(
    order_col_ref, order_row_ref, q_ref, g_ref, kv_ref, cv_ref, att_ref, qg_ref, near_ref, edge_ref, far_ref, bias_ref,
    *, head_dim, near_rows
):
    rows = q_ref.shape[0]
    cols = kv_ref.shape[1]
    scale = 1.0 / math.sqrt(head_dim)
    gather = (
        order_col_ref[...] == lax.broadcasted_iota(jnp.int32, (rows, rows), 1)
    ).astype(jnp.bfloat16)
    scatter = (
        order_row_ref[...] == lax.broadcasted_iota(jnp.int32, (rows, rows), 0)
    ).astype(jnp.bfloat16)
    q_all = jnp.dot(gather, q_ref[...], preferred_element_type=jnp.float32).astype(jnp.bfloat16)
    g_all = jnp.dot(gather, g_ref[...], preferred_element_type=jnp.float32).astype(jnp.bfloat16)

    @pl.when(pl.program_id(0) == 0)
    def _():
        row = lax.broadcasted_iota(jnp.int32, (rows, cols), 0)
        col = lax.broadcasted_iota(jnp.int32, (rows, cols), 1)
        start = (row // BLOCK) * BLOCK
        in_window = (col >= start) & (col < start + 3 * BLOCK)
        ok = (col >= near_rows) | (in_window & (cv_ref[...] > 0))
        bias_ref[...] = jnp.where(ok, 0.0, -jnp.inf).astype(jnp.float32)

    nt = (((1,), (1,)), ((), ()))
    tn = (((0,), (0,)), ((), ()))
    lane = lax.broadcasted_iota(jnp.int32, (1, LANES), 1)
    att_parts = []
    qg_parts = []
    for pair in range(q_ref.shape[1] // LANES):
        ls = slice(pair * LANES, (pair + 1) * LANES)
        q_pair = q_all[:, ls]
        g_pair = g_all[:, ls]
        k = kv_ref[0, :, ls]
        v = kv_ref[1, :, ls]
        att = qg = key_term = value_term = None
        for h in range(LANES // head_dim):
            sel = (lane >= h * head_dim) & (lane < (h + 1) * head_dim)
            q = jnp.where(sel, q_pair, jnp.zeros_like(q_pair))
            g = jnp.where(sel, g_pair, jnp.zeros_like(g_pair))
            s = lax.dot_general(q, k, nt, preferred_element_type=jnp.float32) * scale + bias_ref[...]
            m = jnp.max(s, axis=-1, keepdims=True)
            e = jnp.exp(s - m)
            w = e / jnp.sum(e, axis=-1, keepdims=True)
            wb = w.astype(jnp.bfloat16)
            vd = lax.dot_general(g, v, nt, preferred_element_type=jnp.float32)
            rd = jnp.sum(w * vd, axis=-1, keepdims=True)
            sg = (w * (vd - rd) * scale).astype(jnp.bfloat16)
            outs = (
                jnp.dot(wb, v, preferred_element_type=jnp.float32),
                jnp.dot(sg, k, preferred_element_type=jnp.float32),
                lax.dot_general(sg, q_pair, tn, preferred_element_type=jnp.float32),
                lax.dot_general(wb, g_pair, tn, preferred_element_type=jnp.float32),
            )
            if att is None:
                att, qg, key_term, value_term = outs
            else:
                att, qg, key_term, value_term = (
                    jnp.where(sel, new, old) for new, old in zip(outs, (att, qg, key_term, value_term))
                )
        for c, term in enumerate((key_term, value_term)):
            near_ref[c, :, ls] = term[BLOCK : BLOCK + rows]
            edge_ref[c, :BLOCK, ls] = term[:BLOCK].astype(edge_ref.dtype)
            edge_ref[c, BLOCK:, ls] = term[near_rows - BLOCK : near_rows].astype(edge_ref.dtype)
            far_ref[c, :, ls] = term[near_rows:].astype(far_ref.dtype)
        att_parts.append(att.astype(jnp.bfloat16))
        qg_parts.append(qg.astype(jnp.bfloat16))
    att_ref[...] = jnp.dot(
        scatter, jnp.concatenate(att_parts, axis=1), preferred_element_type=jnp.float32
    ).astype(att_ref.dtype)
    qg_ref[...] = jnp.dot(
        scatter, jnp.concatenate(qg_parts, axis=1), preferred_element_type=jnp.float32
    ).astype(qg_ref.dtype)


def attention(order, queries, out_grad, kv_all, col_valid, head_dim, near_rows):
    rows, features = queries.shape
    cols = kv_all.shape[1]
    width = 4 * LANES if features % (4 * LANES) == 0 else (2 * LANES if features % (2 * LANES) == 0 else LANES)
    row_spec = pl.BlockSpec((rows, width), lambda i: (0, i))
    kv_spec = pl.BlockSpec((2, cols, width), lambda i: (0, 0, i))
    kernel = lambda *refs: attention_kernel(*refs, head_dim=head_dim, near_rows=near_rows)
    return pl.pallas_call(
        kernel,
        grid=(features // width,),
        in_specs=[
            pl.BlockSpec((rows, 1), lambda i: (0, 0)),
            pl.BlockSpec((1, rows), lambda i: (0, 0)),
            row_spec,
            row_spec,
            kv_spec,
            pl.BlockSpec((1, cols), lambda i: (0, 0)),
        ],
        out_specs=[
            row_spec,
            row_spec,
            pl.BlockSpec((2, rows, width), lambda i: (0, 0, i)),
            pl.BlockSpec((2, 2 * BLOCK, width), lambda i: (0, 0, i)),
            pl.BlockSpec((2, cols - near_rows, width), lambda i: (0, 0, i)),
        ],
        out_shape=[
            jax.ShapeDtypeStruct((rows, features), jnp.bfloat16),
            jax.ShapeDtypeStruct((rows, features), jnp.bfloat16),
            jax.ShapeDtypeStruct((2, rows, features), jnp.float32),
            jax.ShapeDtypeStruct((2, 2 * BLOCK, features), jnp.bfloat16),
            jax.ShapeDtypeStruct((2, cols - near_rows, features), jnp.bfloat16),
        ],
        scratch_shapes=[pltpu.VMEM((rows, cols), jnp.float32)],
    )(order.reshape(rows, 1), order.reshape(1, rows), queries, out_grad, kv_all, col_valid)


def xor_permute(value, distance, count):
    return lax.ppermute(value, AXES, [(i, i ^ distance) for i in range(count)])


def per_device(queries, key_table, value_table, out_grad, hilbert_order, key_valid):
    rows_dev, features = queries.shape
    head_dim = D // HEADS
    shard_count = lax.axis_size(AXES)
    shard_bits = shard_count.bit_length() - 1
    my_index = lax.axis_index(AXES)
    permute = hilbert_order[0]
    one_hot = (permute[:, None] == lax.broadcasted_iota(jnp.int32, (rows_dev, rows_dev), 1)).astype(
        jnp.bfloat16
    )

    def take(storage_rows):
        return jnp.dot(one_hot, storage_rows, preferred_element_type=jnp.float32).astype(jnp.bfloat16)

    table_rows = jnp.stack([take(key_table), take(value_table)])
    padded_valid = jnp.pad(key_valid, (BLOCK, BLOCK))
    edge_valid = lax.dynamic_slice_in_dim(padded_valid, my_index * rows_dev, rows_dev + 2 * BLOCK)
    own_valid_rows = edge_valid[BLOCK : BLOCK + rows_dev].astype(jnp.float32)
    own_valid = own_valid_rows[None, :, None]

    up = [(i, i + 1) for i in range(shard_count - 1)]
    down = [(i + 1, i) for i in range(shard_count - 1)]
    before = lax.ppermute(table_rows[:, rows_dev - BLOCK :], AXES, up)
    after = lax.ppermute(table_rows[:, :BLOCK], AXES, down)

    low_bits = shard_bits // 2
    low_count = 2**low_bits
    high_bits = list(range(low_bits, shard_bits))
    sizes = [rows_dev // 2 ** (bit + 1) for bit in range(shard_bits)]

    def pool(bits):
        matrix = np.zeros((sum(sizes[b] for b in bits), rows_dev), np.float32)
        offset = 0
        for b in bits:
            group = 2 ** (b + 1)
            for j in range(sizes[b]):
                matrix[offset + j, j * group : (j + 1) * group] = 1.0 / group
            offset += sizes[b]
        weights = (jnp.asarray(matrix) * own_valid_rows[None, :]).astype(jnp.bfloat16)
        return jnp.stack(
            [
                jnp.dot(weights, table_rows[c], preferred_element_type=jnp.float32).astype(jnp.bfloat16)
                for c in range(2)
            ]
        )

    far_chunks = []
    own_high = pool(high_bits)
    gathered = {}
    offset = 0
    for b in high_bits:
        gathered[b] = [own_high[:, offset : offset + sizes[b]]]
        offset += sizes[b]
    for low in range(1, low_count):
        bit = low.bit_length() - 1
        received = xor_permute(pool([bit] + high_bits), low, shard_count)
        far_chunks.append(received[:, : sizes[bit]])
        offset = sizes[bit]
        for b in high_bits:
            gathered[b].append(received[:, offset : offset + sizes[b]])
            offset += sizes[b]
    high_distances = [high << low_bits for high in range(1, 2 ** (shard_bits - low_bits))]
    stacked = {b: jnp.concatenate(gathered[b][0::2], axis=1) for b in high_bits}
    second = []
    for distance in high_distances:
        bit = distance.bit_length() - 1
        second.append(xor_permute(stacked[bit], distance, shard_count))
    third = xor_permute(jnp.concatenate(second, axis=1), 1, shard_count)
    far_chunks = far_chunks + second + [third]

    full = jnp.concatenate([before, table_rows, after] + far_chunks, axis=1)
    near_rows = rows_dev + 2 * BLOCK
    cols = full.shape[1]
    col_valid = jnp.concatenate(
        [edge_valid, jnp.ones((cols - near_rows,), edge_valid.dtype)]
    ).reshape(1, cols)
    attended, query_grad, terms, edge_terms, far_terms = attention(
        permute, queries, out_grad, full, col_valid, head_dim, near_rows
    )

    from_next = lax.ppermute(edge_terms[:, :BLOCK], AXES, down).astype(jnp.float32)
    from_prev = lax.ppermute(edge_terms[:, BLOCK:], AXES, up).astype(jnp.float32)

    offset = 0
    direct_terms = []
    for low in range(1, low_count):
        size = sizes[low.bit_length() - 1]
        direct_terms.append(far_terms[:, offset : offset + size])
        offset += size
    half = low_count // 2
    second_rows = [half * sizes[d.bit_length() - 1] for d in high_distances]
    third_terms = far_terms[:, offset + sum(second_rows) :]
    back = xor_permute(third_terms, 1, shard_count).astype(jnp.float32)
    stacked_sums = {}
    pieces = []
    segments = []
    back_offset = 0
    for distance, size in zip(high_distances, second_rows):
        bit = distance.bit_length() - 1
        own = far_terms[:, offset : offset + size].astype(jnp.float32) + back[:, back_offset : back_offset + size]
        offset += size
        back_offset += size
        returned = xor_permute(own.astype(jnp.bfloat16), distance, shard_count)
        pieces.append(returned[:, : sizes[bit]])
        segments.append(bit)
        returned = returned.astype(jnp.float32)
        stacked_sums[bit] = returned if bit not in stacked_sums else stacked_sums[bit] + returned
    for low in range(1, low_count):
        bit = low.bit_length() - 1
        parts = [direct_terms[low - 1]]
        segments.append(bit)
        if low % 2 == 0:
            entry = low // 2
            parts += [
                stacked_sums[b][:, entry * sizes[b] : (entry + 1) * sizes[b]].astype(jnp.bfloat16)
                for b in high_bits
            ]
            segments.extend(high_bits)
        pieces.append(xor_permute(jnp.concatenate(parts, axis=1), low, shard_count))
    expand = np.zeros((rows_dev, sum(sizes[b] for b in segments)), np.float32)
    column = 0
    for bit in segments:
        group = 2 ** (bit + 1)
        for j in range(sizes[bit]):
            expand[j * group : (j + 1) * group, column + j] = 1.0 / group
        column += sizes[bit]
    expand = jnp.asarray(expand, dtype=jnp.bfloat16)
    spread = jnp.stack(
        [
            jnp.dot(expand, jnp.concatenate([piece[c] for piece in pieces], axis=0), preferred_element_type=jnp.float32)
            for c in range(2)
        ]
    )
    edges = jnp.concatenate([from_prev, from_next], axis=1)
    row_grad = terms + edges + own_valid * spread

    def restore(hilbert_rows):
        restored = lax.dot_general(
            one_hot, hilbert_rows, (((0,), (0,)), ((), ())), preferred_element_type=jnp.float32
        )
        return restored.astype(jnp.bfloat16)

    return (attended, query_grad, restore(row_grad[0].astype(jnp.bfloat16)), restore(row_grad[1].astype(jnp.bfloat16)))


def solution(mesh):
    in_specs = (
        P(("parts", "rows", "sub"), "head"),
        P(("parts", "rows", "sub"), "head"),
        P(("parts", "rows", "sub"), "head"),
        P(("parts", "rows", "sub"), "head"),
        P(("parts", "rows", "sub"), None),
        P("parts"),
    )
    out_specs = (
        P(("parts", "rows", "sub"), "head"),
        P(("parts", "rows", "sub"), "head"),
        P(("parts", "rows", "sub"), "head"),
        P(("parts", "rows", "sub"), "head"),
    )
    return jax.shard_map(
        per_device, mesh=mesh, in_specs=in_specs, out_specs=out_specs, check_vma=False
    )
```

```python
import math

import numpy as np

import jax
import jax.numpy as jnp
from jax import lax
from jax.experimental import pallas as pl
from jax.experimental.pallas import tpu as pltpu
from jax.sharding import PartitionSpec as P

D = 512
HEADS = 8
BLOCK = 128
AXES = ("rows", "sub")
LANES = 128


def attention_kernel(
    order_col_ref, order_row_ref, q_ref, g_ref, cv_ref, *refs, head_dim, near_rows, piece_count
):
    kv_refs = refs[:piece_count]
    att_ref, qg_ref, near_ref, edge_ref, far_ref, bias_ref = refs[piece_count:]
    rows = q_ref.shape[0]
    cols = cv_ref.shape[1]
    scale = 1.0 / math.sqrt(head_dim)
    gather = (
        order_col_ref[...] == lax.broadcasted_iota(jnp.int32, (rows, rows), 1)
    ).astype(jnp.bfloat16)
    scatter = (
        order_row_ref[...] == lax.broadcasted_iota(jnp.int32, (rows, rows), 0)
    ).astype(jnp.bfloat16)
    q_all = jnp.dot(gather, q_ref[...], preferred_element_type=jnp.float32).astype(jnp.bfloat16)
    g_all = jnp.dot(gather, g_ref[...], preferred_element_type=jnp.float32).astype(jnp.bfloat16)

    @pl.when(pl.program_id(0) == 0)
    def _():
        row = lax.broadcasted_iota(jnp.int32, (rows, cols), 0)
        col = lax.broadcasted_iota(jnp.int32, (rows, cols), 1)
        start = (row // BLOCK) * BLOCK
        in_window = (col >= start) & (col < start + 3 * BLOCK)
        ok = (col >= near_rows) | (in_window & (cv_ref[...] > 0))
        bias_ref[...] = jnp.where(ok, 0.0, -jnp.inf).astype(jnp.float32)

    nt = (((1,), (1,)), ((), ()))
    tn = (((0,), (0,)), ((), ()))
    lane = lax.broadcasted_iota(jnp.int32, (1, LANES), 1)
    att_parts = []
    qg_parts = []
    for pair in range(q_ref.shape[1] // LANES):
        ls = slice(pair * LANES, (pair + 1) * LANES)
        q_pair = q_all[:, ls]
        g_pair = g_all[:, ls]
        k = jnp.concatenate([r[0, :, ls] for r in kv_refs], axis=0)
        v = jnp.concatenate([r[1, :, ls] for r in kv_refs], axis=0)
        att = qg = key_term = value_term = None
        for h in range(LANES // head_dim):
            sel = (lane >= h * head_dim) & (lane < (h + 1) * head_dim)
            q = jnp.where(sel, q_pair, jnp.zeros_like(q_pair))
            g = jnp.where(sel, g_pair, jnp.zeros_like(g_pair))
            s = lax.dot_general(q, k, nt, preferred_element_type=jnp.float32) * scale + bias_ref[...]
            m = jnp.max(s, axis=-1, keepdims=True)
            e = jnp.exp(s - m)
            w = e / jnp.sum(e, axis=-1, keepdims=True)
            wb = w.astype(jnp.bfloat16)
            vd = lax.dot_general(g, v, nt, preferred_element_type=jnp.float32)
            rd = jnp.sum(w * vd, axis=-1, keepdims=True)
            sg = (w * (vd - rd) * scale).astype(jnp.bfloat16)
            outs = (
                jnp.dot(wb, v, preferred_element_type=jnp.float32),
                jnp.dot(sg, k, preferred_element_type=jnp.float32),
                lax.dot_general(sg, q_pair, tn, preferred_element_type=jnp.float32),
                lax.dot_general(wb, g_pair, tn, preferred_element_type=jnp.float32),
            )
            if att is None:
                att, qg, key_term, value_term = outs
            else:
                att, qg, key_term, value_term = (
                    jnp.where(sel, new, old) for new, old in zip(outs, (att, qg, key_term, value_term))
                )
        for c, term in enumerate((key_term, value_term)):
            near_ref[c, :, ls] = term[BLOCK : BLOCK + rows]
            edge_ref[c, :BLOCK, ls] = term[:BLOCK].astype(edge_ref.dtype)
            edge_ref[c, BLOCK:, ls] = term[near_rows - BLOCK : near_rows].astype(edge_ref.dtype)
            far_ref[c, :, ls] = term[near_rows:].astype(far_ref.dtype)
        att_parts.append(att.astype(jnp.bfloat16))
        qg_parts.append(qg.astype(jnp.bfloat16))
    att_ref[...] = jnp.dot(
        scatter, jnp.concatenate(att_parts, axis=1), preferred_element_type=jnp.float32
    ).astype(att_ref.dtype)
    qg_ref[...] = jnp.dot(
        scatter, jnp.concatenate(qg_parts, axis=1), preferred_element_type=jnp.float32
    ).astype(qg_ref.dtype)


def attention(order, queries, out_grad, kv_pieces, col_valid, head_dim, near_rows):
    rows, features = queries.shape
    cols = col_valid.shape[1]
    width = 2 * LANES if features % (2 * LANES) == 0 else LANES
    row_spec = pl.BlockSpec((rows, width), lambda i: (0, i))
    kv_specs = [pl.BlockSpec((2, piece.shape[1], width), lambda i: (0, 0, i)) for piece in kv_pieces]
    kernel = lambda *refs: attention_kernel(
        *refs, head_dim=head_dim, near_rows=near_rows, piece_count=len(kv_pieces)
    )
    return pl.pallas_call(
        kernel,
        grid=(features // width,),
        in_specs=[
            pl.BlockSpec((rows, 1), lambda i: (0, 0)),
            pl.BlockSpec((1, rows), lambda i: (0, 0)),
            row_spec,
            row_spec,
            pl.BlockSpec((1, cols), lambda i: (0, 0)),
        ]
        + kv_specs,
        out_specs=[
            row_spec,
            row_spec,
            pl.BlockSpec((2, rows, width), lambda i: (0, 0, i)),
            pl.BlockSpec((2, 2 * BLOCK, width), lambda i: (0, 0, i)),
            pl.BlockSpec((2, cols - near_rows, width), lambda i: (0, 0, i)),
        ],
        out_shape=[
            jax.ShapeDtypeStruct((rows, features), jnp.bfloat16),
            jax.ShapeDtypeStruct((rows, features), jnp.bfloat16),
            jax.ShapeDtypeStruct((2, rows, features), jnp.float32),
            jax.ShapeDtypeStruct((2, 2 * BLOCK, features), jnp.bfloat16),
            jax.ShapeDtypeStruct((2, cols - near_rows, features), jnp.bfloat16),
        ],
        scratch_shapes=[pltpu.VMEM((rows, cols), jnp.float32)],
    )(order.reshape(rows, 1), order.reshape(1, rows), queries, out_grad, col_valid, *kv_pieces)


def xor_permute(value, distance, count):
    return lax.ppermute(value, AXES, [(i, i ^ distance) for i in range(count)])


def per_device(queries, key_table, value_table, out_grad, hilbert_order, key_valid):
    rows_dev, features = queries.shape
    head_dim = D // HEADS
    shard_count = lax.axis_size(AXES)
    shard_bits = shard_count.bit_length() - 1
    my_index = lax.axis_index(AXES)
    permute = hilbert_order[0]
    one_hot = (permute[:, None] == lax.broadcasted_iota(jnp.int32, (rows_dev, rows_dev), 1)).astype(
        jnp.bfloat16
    )

    def take(storage_rows):
        return jnp.dot(one_hot, storage_rows, preferred_element_type=jnp.float32).astype(jnp.bfloat16)

    table_rows = jnp.stack([take(key_table), take(value_table)])
    padded_valid = jnp.pad(key_valid, (BLOCK, BLOCK))
    edge_valid = lax.dynamic_slice_in_dim(padded_valid, my_index * rows_dev, rows_dev + 2 * BLOCK)
    own_valid_rows = edge_valid[BLOCK : BLOCK + rows_dev].astype(jnp.float32)
    own_valid = own_valid_rows[None, :, None]

    up = [(i, i + 1) for i in range(shard_count - 1)]
    down = [(i + 1, i) for i in range(shard_count - 1)]
    before = lax.ppermute(table_rows[:, rows_dev - BLOCK :], AXES, up)
    after = lax.ppermute(table_rows[:, :BLOCK], AXES, down)

    low_bits = shard_bits // 2
    low_count = 2**low_bits
    high_bits = list(range(low_bits, shard_bits))
    sizes = [rows_dev // 2 ** (bit + 1) for bit in range(shard_bits)]

    def pool(bits):
        matrix = np.zeros((sum(sizes[b] for b in bits), rows_dev), np.float32)
        offset = 0
        for b in bits:
            group = 2 ** (b + 1)
            for j in range(sizes[b]):
                matrix[offset + j, j * group : (j + 1) * group] = 1.0 / group
            offset += sizes[b]
        weights = (jnp.asarray(matrix) * own_valid_rows[None, :]).astype(jnp.bfloat16)
        return jnp.stack(
            [
                jnp.dot(weights, table_rows[c], preferred_element_type=jnp.float32).astype(jnp.bfloat16)
                for c in range(2)
            ]
        )

    far_chunks = []
    own_high = pool(high_bits)
    gathered = {}
    offset = 0
    for b in high_bits:
        gathered[b] = [own_high[:, offset : offset + sizes[b]]]
        offset += sizes[b]
    for low in range(1, low_count):
        bit = low.bit_length() - 1
        received = xor_permute(pool([bit] + high_bits), low, shard_count)
        far_chunks.append(received[:, : sizes[bit]])
        offset = sizes[bit]
        for b in high_bits:
            gathered[b].append(received[:, offset : offset + sizes[b]])
            offset += sizes[b]
    high_distances = [high << low_bits for high in range(1, 2 ** (shard_bits - low_bits))]
    stacked = {b: jnp.concatenate(gathered[b][0::2], axis=1) for b in high_bits}
    second = []
    for distance in high_distances:
        bit = distance.bit_length() - 1
        second.append(xor_permute(stacked[bit], distance, shard_count))
    third = xor_permute(jnp.concatenate(second, axis=1), 1, shard_count)
    far_chunks = far_chunks + second + [third]

    direct_count = low_count - 1
    kv_pieces = [before, table_rows, after, jnp.concatenate(far_chunks[:direct_count], axis=1)]
    kv_pieces += far_chunks[direct_count:]
    if any(piece.shape[1] % 16 for piece in kv_pieces):
        kv_pieces = [jnp.concatenate(kv_pieces, axis=1)]
    near_rows = rows_dev + 2 * BLOCK
    cols = sum(piece.shape[1] for piece in kv_pieces)
    col_valid = jnp.concatenate(
        [edge_valid, jnp.ones((cols - near_rows,), edge_valid.dtype)]
    ).reshape(1, cols)
    attended, query_grad, terms, edge_terms, far_terms = attention(
        permute, queries, out_grad, kv_pieces, col_valid, head_dim, near_rows
    )

    from_next = lax.ppermute(edge_terms[:, :BLOCK], AXES, down).astype(jnp.float32)
    from_prev = lax.ppermute(edge_terms[:, BLOCK:], AXES, up).astype(jnp.float32)

    offset = 0
    direct_terms = []
    for low in range(1, low_count):
        size = sizes[low.bit_length() - 1]
        direct_terms.append(far_terms[:, offset : offset + size])
        offset += size
    half = low_count // 2
    second_rows = [half * sizes[d.bit_length() - 1] for d in high_distances]
    third_terms = far_terms[:, offset + sum(second_rows) :]
    back = xor_permute(third_terms, 1, shard_count).astype(jnp.float32)
    stacked_sums = {}
    pieces = []
    segments = []
    back_offset = 0
    for distance, size in zip(high_distances, second_rows):
        bit = distance.bit_length() - 1
        own = far_terms[:, offset : offset + size].astype(jnp.float32) + back[:, back_offset : back_offset + size]
        offset += size
        back_offset += size
        returned = xor_permute(own.astype(jnp.bfloat16), distance, shard_count)
        pieces.append(returned[:, : sizes[bit]])
        segments.append(bit)
        returned = returned.astype(jnp.float32)
        stacked_sums[bit] = returned if bit not in stacked_sums else stacked_sums[bit] + returned
    for low in range(1, low_count):
        bit = low.bit_length() - 1
        parts = [direct_terms[low - 1]]
        segments.append(bit)
        if low % 2 == 0:
            entry = low // 2
            parts += [
                stacked_sums[b][:, entry * sizes[b] : (entry + 1) * sizes[b]].astype(jnp.bfloat16)
                for b in high_bits
            ]
            segments.extend(high_bits)
        pieces.append(xor_permute(jnp.concatenate(parts, axis=1), low, shard_count))
    expand = np.zeros((rows_dev, sum(sizes[b] for b in segments)), np.float32)
    column = 0
    for bit in segments:
        group = 2 ** (bit + 1)
        for j in range(sizes[bit]):
            expand[j * group : (j + 1) * group, column + j] = 1.0 / group
        column += sizes[bit]
    expand = jnp.asarray(expand, dtype=jnp.bfloat16)
    spread = jnp.stack(
        [
            jnp.dot(expand, jnp.concatenate([piece[c] for piece in pieces], axis=0), preferred_element_type=jnp.float32)
            for c in range(2)
        ]
    )
    edges = jnp.concatenate([from_prev, from_next], axis=1)
    row_grad = terms + edges + own_valid * spread

    def restore(hilbert_rows):
        restored = lax.dot_general(
            one_hot, hilbert_rows, (((0,), (0,)), ((), ())), preferred_element_type=jnp.float32
        )
        return restored.astype(jnp.bfloat16)

    return (attended, query_grad, restore(row_grad[0].astype(jnp.bfloat16)), restore(row_grad[1].astype(jnp.bfloat16)))


def solution(mesh):
    in_specs = (
        P(("parts", "rows", "sub"), "head"),
        P(("parts", "rows", "sub"), "head"),
        P(("parts", "rows", "sub"), "head"),
        P(("parts", "rows", "sub"), "head"),
        P(("parts", "rows", "sub"), None),
        P("parts"),
    )
    out_specs = (
        P(("parts", "rows", "sub"), "head"),
        P(("parts", "rows", "sub"), "head"),
        P(("parts", "rows", "sub"), "head"),
        P(("parts", "rows", "sub"), "head"),
    )
    return jax.shard_map(
        per_device, mesh=mesh, in_specs=in_specs, out_specs=out_specs, check_vma=False
    )
```

```python
import math

import numpy as np

import jax
import jax.numpy as jnp
from jax import lax
from jax.experimental import pallas as pl
from jax.experimental.pallas import tpu as pltpu
from jax.sharding import PartitionSpec as P

D = 512
HEADS = 8
BLOCK = 128
AXES = ("rows", "sub")
LANES = 128


def attention_kernel(
    order_col_ref, order_row_ref, q_ref, g_ref, cv_ref, *refs, head_dim, near_rows, piece_count
):
    kv_refs = refs[:piece_count]
    att_ref, qg_ref, near_ref, edge_ref, far_ref, bias_ref = refs[piece_count:]
    rows = q_ref.shape[0]
    cols = cv_ref.shape[1]
    scale = 1.0 / math.sqrt(head_dim)
    gather = (
        order_col_ref[...] == lax.broadcasted_iota(jnp.int32, (rows, rows), 1)
    ).astype(jnp.bfloat16)
    scatter = (
        order_row_ref[...] == lax.broadcasted_iota(jnp.int32, (rows, rows), 0)
    ).astype(jnp.bfloat16)
    q_all = jnp.dot(gather, q_ref[...], preferred_element_type=jnp.float32).astype(jnp.bfloat16)
    g_all = jnp.dot(gather, g_ref[...], preferred_element_type=jnp.float32).astype(jnp.bfloat16)

    @pl.when(pl.program_id(0) == 0)
    def _():
        row = lax.broadcasted_iota(jnp.int32, (rows, cols), 0)
        col = lax.broadcasted_iota(jnp.int32, (rows, cols), 1)
        start = (row // BLOCK) * BLOCK
        in_window = (col >= start) & (col < start + 3 * BLOCK)
        ok = (col >= near_rows) | (in_window & (cv_ref[...] > 0))
        bias_ref[...] = jnp.where(ok, 0.0, -jnp.inf).astype(jnp.float32)

    nt = (((1,), (1,)), ((), ()))
    tn = (((0,), (0,)), ((), ()))
    lane = lax.broadcasted_iota(jnp.int32, (1, LANES), 1)
    att_parts = []
    qg_parts = []
    for pair in range(q_ref.shape[1] // LANES):
        ls = slice(pair * LANES, (pair + 1) * LANES)
        q_pair = q_all[:, ls]
        g_pair = g_all[:, ls]
        k = jnp.concatenate([r[0, :, ls] for r in kv_refs], axis=0)
        v = jnp.concatenate([r[1, :, ls] for r in kv_refs], axis=0)
        att = qg = key_term = value_term = None
        for h in range(LANES // head_dim):
            sel = (lane >= h * head_dim) & (lane < (h + 1) * head_dim)
            q = jnp.where(sel, q_pair, jnp.zeros_like(q_pair))
            g = jnp.where(sel, g_pair, jnp.zeros_like(g_pair))
            s = lax.dot_general(q, k, nt, preferred_element_type=jnp.float32) * scale + bias_ref[...]
            m = jnp.max(s, axis=-1, keepdims=True)
            e = jnp.exp(s - m)
            w = e / jnp.sum(e, axis=-1, keepdims=True)
            wb = w.astype(jnp.bfloat16)
            vd = lax.dot_general(g, v, nt, preferred_element_type=jnp.float32)
            rd = jnp.sum(w * vd, axis=-1, keepdims=True)
            sg = (w * (vd - rd) * scale).astype(jnp.bfloat16)
            outs = (
                jnp.dot(wb, v, preferred_element_type=jnp.float32),
                jnp.dot(sg, k, preferred_element_type=jnp.float32),
                lax.dot_general(sg, q_pair, tn, preferred_element_type=jnp.float32),
                lax.dot_general(wb, g_pair, tn, preferred_element_type=jnp.float32),
            )
            if att is None:
                att, qg, key_term, value_term = outs
            else:
                att, qg, key_term, value_term = (
                    jnp.where(sel, new, old) for new, old in zip(outs, (att, qg, key_term, value_term))
                )
        for c, term in enumerate((key_term, value_term)):
            near_ref[c, :, ls] = term[BLOCK : BLOCK + rows]
            edge_ref[c, :BLOCK, ls] = term[:BLOCK].astype(edge_ref.dtype)
            edge_ref[c, BLOCK:, ls] = term[near_rows - BLOCK : near_rows].astype(edge_ref.dtype)
            far_ref[c, :, ls] = term[near_rows:].astype(far_ref.dtype)
        att_parts.append(att.astype(jnp.bfloat16))
        qg_parts.append(qg.astype(jnp.bfloat16))
    att_ref[...] = jnp.dot(
        scatter, jnp.concatenate(att_parts, axis=1), preferred_element_type=jnp.float32
    ).astype(att_ref.dtype)
    qg_ref[...] = jnp.dot(
        scatter, jnp.concatenate(qg_parts, axis=1), preferred_element_type=jnp.float32
    ).astype(qg_ref.dtype)


def attention(order, queries, out_grad, kv_pieces, col_valid, head_dim, near_rows):
    rows, features = queries.shape
    cols = col_valid.shape[1]
    width = 2 * LANES if features % (2 * LANES) == 0 else LANES
    row_spec = pl.BlockSpec((rows, width), lambda i: (0, i))
    kv_specs = [pl.BlockSpec((2, piece.shape[1], width), lambda i: (0, 0, i)) for piece in kv_pieces]
    kernel = lambda *refs: attention_kernel(
        *refs, head_dim=head_dim, near_rows=near_rows, piece_count=len(kv_pieces)
    )
    return pl.pallas_call(
        kernel,
        grid=(features // width,),
        in_specs=[
            pl.BlockSpec((rows, 1), lambda i: (0, 0)),
            pl.BlockSpec((1, rows), lambda i: (0, 0)),
            row_spec,
            row_spec,
            pl.BlockSpec((1, cols), lambda i: (0, 0)),
        ]
        + kv_specs,
        out_specs=[
            row_spec,
            row_spec,
            pl.BlockSpec((2, rows, width), lambda i: (0, 0, i)),
            pl.BlockSpec((2, 2 * BLOCK, width), lambda i: (0, 0, i)),
            pl.BlockSpec((2, cols - near_rows, width), lambda i: (0, 0, i)),
        ],
        out_shape=[
            jax.ShapeDtypeStruct((rows, features), jnp.bfloat16),
            jax.ShapeDtypeStruct((rows, features), jnp.bfloat16),
            jax.ShapeDtypeStruct((2, rows, features), jnp.float32),
            jax.ShapeDtypeStruct((2, 2 * BLOCK, features), jnp.bfloat16),
            jax.ShapeDtypeStruct((2, cols - near_rows, features), jnp.bfloat16),
        ],
        scratch_shapes=[pltpu.VMEM((rows, cols), jnp.float32)],
    )(order.reshape(rows, 1), order.reshape(1, rows), queries, out_grad, col_valid, *kv_pieces)


def xor_permute(value, distance, count):
    return lax.ppermute(value, AXES, [(i, i ^ distance) for i in range(count)])


def per_device(queries, key_table, value_table, out_grad, hilbert_order, key_valid):
    rows_dev, features = queries.shape
    head_dim = D // HEADS
    shard_count = lax.axis_size(AXES)
    shard_bits = shard_count.bit_length() - 1
    my_index = lax.axis_index(AXES)
    permute = hilbert_order[0]
    one_hot = (permute[:, None] == lax.broadcasted_iota(jnp.int32, (rows_dev, rows_dev), 1)).astype(
        jnp.bfloat16
    )

    def take(storage_rows):
        return jnp.dot(one_hot, storage_rows, preferred_element_type=jnp.float32).astype(jnp.bfloat16)

    table_rows = jnp.stack([take(key_table), take(value_table)])
    padded_valid = jnp.pad(key_valid, (BLOCK, BLOCK))
    edge_valid = lax.dynamic_slice_in_dim(padded_valid, my_index * rows_dev, rows_dev + 2 * BLOCK)
    own_valid_rows = edge_valid[BLOCK : BLOCK + rows_dev].astype(jnp.float32)
    own_valid = own_valid_rows[None, :, None]

    up = [(i, i + 1) for i in range(shard_count - 1)]
    down = [(i + 1, i) for i in range(shard_count - 1)]
    before = lax.ppermute(table_rows[:, rows_dev - BLOCK :], AXES, up)
    after = lax.ppermute(table_rows[:, :BLOCK], AXES, down)

    low_bits = shard_bits // 2
    low_count = 2**low_bits
    high_bits = list(range(low_bits, shard_bits))
    sizes = [rows_dev // 2 ** (bit + 1) for bit in range(shard_bits)]

    def pool(bits):
        matrix = np.zeros((sum(sizes[b] for b in bits), rows_dev), np.float32)
        offset = 0
        for b in bits:
            group = 2 ** (b + 1)
            for j in range(sizes[b]):
                matrix[offset + j, j * group : (j + 1) * group] = 1.0 / group
            offset += sizes[b]
        weights = (jnp.asarray(matrix) * own_valid_rows[None, :]).astype(jnp.bfloat16)
        return jnp.stack(
            [
                jnp.dot(weights, table_rows[c], preferred_element_type=jnp.float32).astype(jnp.bfloat16)
                for c in range(2)
            ]
        )

    far_chunks = []
    own_high = pool(high_bits)
    gathered = {}
    offset = 0
    for b in high_bits:
        gathered[b] = [own_high[:, offset : offset + sizes[b]]]
        offset += sizes[b]
    for low in range(1, low_count):
        bit = low.bit_length() - 1
        forwarded = high_bits if low % 2 == 0 else []
        received = xor_permute(pool([bit] + forwarded), low, shard_count)
        far_chunks.append(received[:, : sizes[bit]])
        offset = sizes[bit]
        for b in forwarded:
            gathered[b].append(received[:, offset : offset + sizes[b]])
            offset += sizes[b]
    high_distances = [high << low_bits for high in range(1, 2 ** (shard_bits - low_bits))]
    stacked = {b: jnp.concatenate(gathered[b], axis=1) for b in high_bits}
    second = []
    for distance in high_distances:
        bit = distance.bit_length() - 1
        second.append(xor_permute(stacked[bit], distance, shard_count))
    third = xor_permute(jnp.concatenate(second, axis=1), 1, shard_count)
    far_chunks = far_chunks + second + [third]

    direct_count = low_count - 1
    kv_pieces = [before, table_rows, after, jnp.concatenate(far_chunks[:direct_count], axis=1)]
    kv_pieces += far_chunks[direct_count:]
    if any(piece.shape[1] % 16 for piece in kv_pieces):
        kv_pieces = [jnp.concatenate(kv_pieces, axis=1)]
    near_rows = rows_dev + 2 * BLOCK
    cols = sum(piece.shape[1] for piece in kv_pieces)
    col_valid = jnp.concatenate(
        [edge_valid, jnp.ones((cols - near_rows,), edge_valid.dtype)]
    ).reshape(1, cols)
    attended, query_grad, terms, edge_terms, far_terms = attention(
        permute, queries, out_grad, kv_pieces, col_valid, head_dim, near_rows
    )

    from_next = lax.ppermute(edge_terms[:, :BLOCK], AXES, down).astype(jnp.float32)
    from_prev = lax.ppermute(edge_terms[:, BLOCK:], AXES, up).astype(jnp.float32)

    offset = 0
    direct_terms = []
    for low in range(1, low_count):
        size = sizes[low.bit_length() - 1]
        direct_terms.append(far_terms[:, offset : offset + size])
        offset += size
    half = low_count // 2
    second_rows = [half * sizes[d.bit_length() - 1] for d in high_distances]
    third_terms = far_terms[:, offset + sum(second_rows) :]
    back = xor_permute(third_terms, 1, shard_count).astype(jnp.float32)
    stacked_sums = {}
    pieces = []
    segments = []
    back_offset = 0
    for distance, size in zip(high_distances, second_rows):
        bit = distance.bit_length() - 1
        own = far_terms[:, offset : offset + size].astype(jnp.float32) + back[:, back_offset : back_offset + size]
        offset += size
        back_offset += size
        returned = xor_permute(own.astype(jnp.bfloat16), distance, shard_count)
        pieces.append(returned[:, : sizes[bit]])
        segments.append(bit)
        returned = returned.astype(jnp.float32)
        stacked_sums[bit] = returned if bit not in stacked_sums else stacked_sums[bit] + returned
    for low in range(1, low_count):
        bit = low.bit_length() - 1
        parts = [direct_terms[low - 1]]
        segments.append(bit)
        if low % 2 == 0:
            entry = low // 2
            parts += [
                stacked_sums[b][:, entry * sizes[b] : (entry + 1) * sizes[b]].astype(jnp.bfloat16)
                for b in high_bits
            ]
            segments.extend(high_bits)
        pieces.append(xor_permute(jnp.concatenate(parts, axis=1), low, shard_count))
    expand = np.zeros((rows_dev, sum(sizes[b] for b in segments)), np.float32)
    column = 0
    for bit in segments:
        group = 2 ** (bit + 1)
        for j in range(sizes[bit]):
            expand[j * group : (j + 1) * group, column + j] = 1.0 / group
        column += sizes[bit]
    expand = jnp.asarray(expand, dtype=jnp.bfloat16)
    spread = jnp.stack(
        [
            jnp.dot(expand, jnp.concatenate([piece[c] for piece in pieces], axis=0), preferred_element_type=jnp.float32)
            for c in range(2)
        ]
    )
    edges = jnp.concatenate([from_prev, from_next], axis=1)
    row_grad = terms + edges + own_valid * spread

    def restore(hilbert_rows):
        restored = lax.dot_general(
            one_hot, hilbert_rows, (((0,), (0,)), ((), ())), preferred_element_type=jnp.float32
        )
        return restored.astype(jnp.bfloat16)

    return (attended, query_grad, restore(row_grad[0].astype(jnp.bfloat16)), restore(row_grad[1].astype(jnp.bfloat16)))


def solution(mesh):
    in_specs = (
        P(("parts", "rows", "sub"), "head"),
        P(("parts", "rows", "sub"), "head"),
        P(("parts", "rows", "sub"), "head"),
        P(("parts", "rows", "sub"), "head"),
        P(("parts", "rows", "sub"), None),
        P("parts"),
    )
    out_specs = (
        P(("parts", "rows", "sub"), "head"),
        P(("parts", "rows", "sub"), "head"),
        P(("parts", "rows", "sub"), "head"),
        P(("parts", "rows", "sub"), "head"),
    )
    return jax.shard_map(
        per_device, mesh=mesh, in_specs=in_specs, out_specs=out_specs, check_vma=False
    )
```
